32 devices in a mesh: ctx: 4 (over z), pipe: 8 (over y, x, core).
Axes of the slice: x: 2, y: 2, z: 4, core: 2. Of those that a mesh axis runs over, the one named last changes fastest.
Arguments:
- qkv_in: bfloat16 [8, 512, 3, 256], P('pipe', 'ctx'), may hold values from -6 to 6
- qkv_saved: bfloat16 [8, 512, 3, 256], P('pipe', 'ctx'), may hold values from -6 to 6
- conv_saved: float32 [8, 512, 256], P('pipe', 'ctx'), may hold values from -6 to 6
- out_grad: bfloat16 [8, 512, 256], P('pipe', 'ctx'), may hold values from -6 to 6
- filters: float32 [8, 16, 512], P('pipe', None, 'ctx'), may hold values from -32768 to 32768
Outputs:
- next_input: bfloat16 [8, 512, 256], P('pipe', 'ctx')
- prev_grad: bfloat16 [8, 512, 3, 256], P('pipe', 'ctx')
- filter_grad: float32 [8, 16, 512], P('pipe', None, 'ctx')
The draws below stay inside these ranges and needn't reach their ends.
All inputs are finite; a program needn't handle non-finite values.
Results may differ from the reference program's by a relative error of at most 0.001.
Values may be sent and summed in bfloat16 or wider, within the bound.
No kernel may reach another device: no remote copies, remote signals or barrier semaphores. Data moves between devices by JAX's collectives and lax.ppermute only.
A program may use at most 64 MiB of HBM per device.

```python
import math
import jax
import jax.numpy as jnp
from jax import lax

C = 256
CPF = 16
TOK_DEV = 128
G = 16
SEQ = 512
NFFT = 1024
SECTIONS = 8


def draw_filters(key, part):
    keyset = jax.random.split(key, 6)
    grid_shape = (SECTIONS, G)
    slow_tenths = 5
    is_slow = jax.random.randint(keyset[0], grid_shape, 0, 10) < slow_tenths
    slow_tau = jnp.exp(jax.random.uniform(keyset[1], grid_shape, jnp.float32, math.log(SEQ / 2.0), math.log(4.0 * SEQ)))
    fast_tau = jnp.exp(jax.random.uniform(keyset[2], grid_shape, jnp.float32, math.log(TOK_DEV / 8.0), math.log(TOK_DEV / 5.0)))
    decay_len = jnp.where(is_slow, slow_tau, fast_tau)
    places = jnp.arange(SEQ, dtype=jnp.float32)
    decay_profile = jnp.exp(-places[None, None, :] / decay_len[:, :, None])
    dropout_position = jax.random.randint(keyset[3], (SECTIONS, G, 4), 0, SEQ)
    dropout_keep_mask = jax.random.uniform(keyset[4], (SECTIONS, G, 4), jnp.float32, 0.5, 0.8)
    position_index = jnp.arange(SEQ, dtype=jnp.int32)
    for pulse_number in range(4):
        handed_forward = position_index[None, None, :] > dropout_position[:, :, pulse_number:pulse_number + 1]
        decay_profile = decay_profile * jnp.where(handed_forward, dropout_keep_mask[:, :, pulse_number:pulse_number + 1], 1.0)
    amplitude = jnp.sqrt(2.0 / decay_len + 1.0 / SEQ) * math.sqrt(CPF * SEQ)
    noise_draw = jax.random.truncated_normal(keyset[5], -4.0, 4.0, (SECTIONS, G, SEQ), jnp.float32)
    return noise_draw * decay_profile * amplitude[:, :, None]


def levels(rng, shape, shards, low, largest):
    def one(axis_at, shards_of):
        heights = jax.random.uniform(jax.random.fold_in(jax.random.fold_in(rng, 6), axis_at), (shards_of,), jnp.float32, low / len(shards), largest / len(shards))
        return jnp.repeat(jnp.exp(heights), shape[axis_at] // shards_of).reshape((-1,) + (1,) * (len(shape) - axis_at - 1))

    gain = one(*shards[0])
    for cut in shards[1:]:
        gain = gain * one(*cut)
    return gain


def noise(rng, shape, scale, bound, cuts=(), kind=jnp.bfloat16):
    gain = levels(rng, shape, cuts, -0.22, 0.18) if cuts else 1.0
    array = jax.random.normal(rng, shape, jnp.float32) * scale * gain
    return jnp.minimum(jnp.maximum(array, -bound), bound).astype(kind)


def setup_inputs(seed: int = 0) -> dict:
    seeds = jax.random.split(jax.random.key(seed), 6)
    return {
        "qkv_in": noise(seeds[0], (SECTIONS, SEQ, 3, C), 1.0, 6.0, ((0, 8), (1, 4))),
        "qkv_saved": noise(seeds[1], (SECTIONS, SEQ, 3, C), 1.0, 6.0, ((0, 8), (1, 4))),
        "conv_saved": noise(seeds[2], (SECTIONS, SEQ, C), 1.0, 6.0, ((0, 8), (1, 4)), jnp.float32),
        "out_grad": noise(seeds[3], (SECTIONS, SEQ, C), 1.0, 6.0, ((0, 8), (1, 4))),
        "filters": draw_filters(jax.random.fold_in(seeds[5], 71), 0),
    }


def section_step(operands):
    inputs, saved_in, kept_conv, upstream_in, filter_rows = operands
    filter_scale = (CPF * SEQ) ** -0.5
    taps = filter_rows * filter_scale
    taps_chan = jnp.repeat(taps, CPF, axis=0)
    filter_spec = jnp.fft.rfft(taps_chan, n=NFFT, axis=1)
    query = inputs[:, 0].astype(jnp.float32)
    keyed = inputs[:, 1].astype(jnp.float32)
    valued = inputs[:, 2].astype(jnp.float32)
    mixed = keyed * valued
    mixed_spec = jnp.fft.rfft(mixed.T, n=NFFT, axis=1)
    conv = jnp.fft.irfft(filter_spec * mixed_spec, n=NFFT, axis=1)[:, :SEQ].T
    result = (query * conv).astype(jnp.bfloat16)
    query_back = saved_in[:, 0].astype(jnp.float32)
    key_back = saved_in[:, 1].astype(jnp.float32)
    value_back = saved_in[:, 2].astype(jnp.float32)
    mixed_back = key_back * value_back
    upstream = upstream_in.astype(jnp.float32)
    weighted = upstream * query_back
    grad_query = upstream * kept_conv
    weighted_spec = jnp.fft.rfft(weighted.T, n=NFFT, axis=1)
    grad_mixed = jnp.fft.irfft(jnp.conj(filter_spec) * weighted_spec, n=NFFT, axis=1)[:, :SEQ].T
    grad_key = grad_mixed * value_back
    grad_value = grad_mixed * key_back
    grad_stack = jnp.stack([grad_query, grad_key, grad_value], axis=1).astype(jnp.bfloat16)
    back_spec = jnp.fft.rfft(mixed_back.T, n=NFFT, axis=1)
    lagged = jnp.fft.irfft(jnp.conj(back_spec) * weighted_spec, n=NFFT, axis=1)[:, :SEQ]
    filter_grad = lagged.reshape(G, CPF, SEQ).sum(axis=1) * filter_scale
    return result, grad_stack, filter_grad


def reference(qkv_in, qkv_saved, conv_saved, out_grad, filters):
    result, grad_stack, filter_grad = lax.map(section_step, (qkv_in, qkv_saved, conv_saved, out_grad, filters))
    next_input = jnp.concatenate([jnp.zeros_like(result[:1]), result[:-1]], axis=0)
    prev_grad = jnp.concatenate([grad_stack[1:], jnp.zeros_like(grad_stack[:1])], axis=0)
    return next_input, prev_grad, filter_grad
```

```python
import math

import numpy as np

import jax
import jax.numpy as jnp
from jax import lax
from jax.sharding import PartitionSpec as P

CPF = 16
CHUNK_BYTES = 36 * 2**20

highest = lax.Precision.HIGHEST


def from_behind(x, axis, by):
    devices = lax.axis_size(axis)
    pairs = [(i, i + by) for i in range(devices) if 0 <= i + by < devices]
    return lax.ppermute(x, axis, pairs)


def inner_tables(block):
    ids = np.arange(block)
    theta = 2.0 * np.pi * ((ids[:, None] * ids[None, :]) % block) / block
    cos, sin = np.cos(theta), np.sin(theta)
    fwd = np.block([[cos, -sin], [sin, cos]])
    inv = np.block([[cos, sin], [-sin, cos]])
    return jnp.asarray(fwd.T, jnp.float32), jnp.asarray(inv.T, jnp.float32)


def outer_tables(blocks, block, outer):
    size = outer * block
    pos = np.arange(blocks)[:, None, None] * block + np.arange(block)[None, :, None]
    prod = (pos * np.arange(outer)[None, None, :]) % size
    theta = 2.0 * np.pi * prod / size
    return jnp.asarray(np.cos(theta), jnp.float32), jnp.asarray(-np.sin(theta), jnp.float32)


def to_spectrum(x, cw, sw, fwd):
    blocks = x.shape[0]
    tail = (1,) * (x.ndim - 2)
    re = sum(cw[p].reshape(cw.shape[1:] + tail) * x[p][:, None] for p in range(blocks))
    im = sum(sw[p].reshape(sw.shape[1:] + tail) * x[p][:, None] for p in range(blocks))
    stacked = jnp.concatenate([re, im], axis=0)
    shape = stacked.shape
    out = jnp.dot(fwd, stacked.reshape(shape[0], -1), precision=highest)
    return out.reshape(shape)


def to_signal(spec, inv, wc, ws):
    shape = spec.shape
    block = shape[0] // 2
    z = jnp.dot(inv, spec.reshape(shape[0], -1), precision=highest).reshape(shape)
    tail = (1,) * (spec.ndim - 2)
    wc = wc.reshape(wc.shape + tail)
    ws = ws.reshape(ws.shape + tail)
    return jnp.sum(wc * z[:block] + ws * z[block:], axis=1)


def chunk_work(x3, hx, tables):
    cw, sw, fwd, inv, wc, ws = tables
    block = x3.shape[1]
    spec = to_spectrum(x3, cw, sw, fwd)
    hspec = to_spectrum(hx, cw, sw, fwd)
    hspec = jnp.repeat(hspec, CPF, axis=-1)
    hr, hi = hspec[:block], hspec[block:]
    mr, mi = spec[:block, :, 0], spec[block:, :, 0]
    wr, wi = spec[:block, :, 1], spec[block:, :, 1]
    br, bi = spec[:block, :, 2], spec[block:, :, 2]
    conv_r = hr * mr - hi * mi
    conv_i = hr * mi + hi * mr
    gm_r = hr * wr + hi * wi
    gm_i = hr * wi - hi * wr
    fg_r = br * wr + bi * wi
    fg_i = br * wi - bi * wr
    lead = fg_r.shape[:-1]
    fg_r = fg_r.reshape(lead + (-1, CPF)).sum(axis=-1)
    fg_i = fg_i.reshape(lead + (-1, CPF)).sum(axis=-1)
    pair = jnp.concatenate(
        [jnp.stack([conv_r, gm_r], axis=2), jnp.stack([conv_i, gm_i], axis=2)], axis=0
    )
    both = to_signal(pair, inv, wc, ws)
    fg = to_signal(jnp.concatenate([fg_r, fg_i], axis=0), inv, wc, ws)
    return both[:, 0], both[:, 1], fg


def on_device(qkv_in, qkv_saved, conv_saved, out_grad, filters):
    blocks = lax.axis_size("ctx")
    place = lax.axis_index("ctx")
    block = qkv_in.shape[1]
    channels = qkv_in.shape[3]
    groups = filters.shape[1]
    length = blocks * block
    outer = 2 * blocks
    size = outer * block
    filter_scale = (CPF * length) ** (-0.5)

    query_in = qkv_in[0, :, 0].astype(jnp.float32)
    mixed_in = qkv_in[0, :, 1].astype(jnp.float32) * qkv_in[0, :, 2].astype(jnp.float32)
    query_back = qkv_saved[0, :, 0].astype(jnp.float32)
    key_back = qkv_saved[0, :, 1].astype(jnp.float32)
    value_back = qkv_saved[0, :, 2].astype(jnp.float32)
    mixed_back = key_back * value_back
    upstream = out_grad[0].astype(jnp.float32)
    weighted = upstream * query_back
    grad_query = upstream * conv_saved[0]

    payload = jnp.concatenate([mixed_in, weighted, mixed_back, filters[0].T], axis=1)
    full = lax.all_gather(payload, "ctx")
    x3 = full[:, :, : 3 * channels].reshape(blocks, block, 3, channels)
    hx = full[:, :, 3 * channels :]

    cw, sw = outer_tables(blocks, block, outer)
    fwd, inv = inner_tables(block)
    pos = place * block + jnp.arange(block, dtype=jnp.int32)
    prod = (pos[:, None] * jnp.arange(outer, dtype=jnp.int32)[None, :]) % size
    theta = prod.astype(jnp.float32) * (2.0 * math.pi / size)
    wc = jnp.cos(theta) / size
    ws = -jnp.sin(theta) / size
    tables = (cw, sw, fwd, inv, wc, ws)

    per_group = 2 * block * outer * 4 * 4 * CPF * blocks
    gchunk = groups
    while gchunk > 1 and gchunk * per_group > CHUNK_BYTES and groups % (gchunk // 2) == 0:
        gchunk //= 2
    nchunk = groups // gchunk
    if nchunk == 1:
        conv, grad_mixed, fg = chunk_work(x3, hx, tables)
    else:
        cc = gchunk * CPF
        xs = x3.reshape(blocks, block, 3, nchunk, cc).transpose(3, 0, 1, 2, 4)
        hs = hx.reshape(blocks, block, nchunk, gchunk).transpose(2, 0, 1, 3)
        conv, grad_mixed, fg = lax.map(lambda a: chunk_work(a[0], a[1], tables), (xs, hs))
        conv = conv.transpose(1, 0, 2).reshape(block, channels)
        grad_mixed = grad_mixed.transpose(1, 0, 2).reshape(block, channels)
        fg = fg.transpose(1, 0, 2).reshape(block, groups)

    conv = conv * filter_scale
    grad_mixed = grad_mixed * filter_scale
    result = (query_in * conv).astype(jnp.bfloat16)
    next_input = from_behind(result[None], "pipe", 1)
    grad_key = grad_mixed * value_back
    grad_value = grad_mixed * key_back
    grad_stack = jnp.stack([grad_query, grad_key, grad_value], axis=1).astype(jnp.bfloat16)
    prev_grad = from_behind(grad_stack[None], "pipe", -1)
    filter_grad = (fg * filter_scale).T[None]
    return (next_input, prev_grad, filter_grad)


def solution(mesh):
    return jax.shard_map(
        on_device,
        mesh=mesh,
        in_specs=(
            P("pipe", "ctx", None, None),
            P("pipe", "ctx", None, None),
            P("pipe", "ctx", None),
            P("pipe", "ctx", None),
            P("pipe", None, "ctx"),
        ),
        out_specs=(P("pipe", "ctx", None), P("pipe", "ctx", None, None), P("pipe", None, "ctx")),
        check_vma=False,
    )
```

```python
import math

import numpy as np

import jax
import jax.numpy as jnp
from jax import lax
from jax.sharding import PartitionSpec as P

CPF = 16
CHUNK_BYTES = 36 * 2**20

highest = lax.Precision.HIGHEST
precise = lax.Precision.HIGHEST


def from_behind(x, axis, by):
    devices = lax.axis_size(axis)
    pairs = [(i, i + by) for i in range(devices) if 0 <= i + by < devices]
    return lax.ppermute(x, axis, pairs)


def inner_tables(block):
    ids = np.arange(block)
    theta = 2.0 * np.pi * ((ids[:, None] * ids[None, :]) % block) / block
    cos, sin = np.cos(theta), np.sin(theta)
    fwd = np.block([[cos, -sin], [sin, cos]])
    inv = np.block([[cos, sin], [-sin, cos]])
    return jnp.asarray(fwd.T, jnp.float32), jnp.asarray(inv.T, jnp.float32)


def outer_tables(blocks, block, outer):
    size = outer * block
    pos = np.arange(blocks)[:, None, None] * block + np.arange(block)[None, :, None]
    prod = (pos * np.arange(outer)[None, None, :]) % size
    theta = 2.0 * np.pi * prod / size
    return jnp.asarray(np.cos(theta), jnp.float32), jnp.asarray(-np.sin(theta), jnp.float32)


def to_spectrum(x, cw, sw, fwd):
    blocks = x.shape[0]
    tail = (1,) * (x.ndim - 2)
    re = sum(cw[p].reshape(cw.shape[1:] + tail) * x[p][:, None] for p in range(blocks))
    im = sum(sw[p].reshape(sw.shape[1:] + tail) * x[p][:, None] for p in range(blocks))
    stacked = jnp.concatenate([re, im], axis=0)
    shape = stacked.shape
    out = jnp.dot(fwd, stacked.reshape(shape[0], -1), precision=highest)
    return out.reshape(shape)


def local_signal(spec, inverse):
    shape = spec.shape
    flat = spec.reshape(shape[0] * shape[1], -1)
    out = jnp.dot(inverse, flat, precision=precise)
    return out.reshape((inverse.shape[0],) + shape[2:])


def all_signal(spec, inv, cw, sw):
    shape = spec.shape
    block = shape[0] // 2
    size = shape[1] * block
    z = jnp.dot(inv, spec.reshape(shape[0], -1), precision=precise).reshape(shape)
    tail = (1,) * (spec.ndim - 2)
    zr, zi = z[:block], z[block:]
    rows = []
    for p in range(cw.shape[0]):
        c = cw[p].reshape(cw.shape[1:] + tail)
        s = sw[p].reshape(sw.shape[1:] + tail)
        rows.append(jnp.sum(c * zr + s * zi, axis=1))
    return jnp.stack(rows) / size


def chunk_work(x3, hx, tables):
    cw, sw, fwd, inv, inverse = tables
    block = x3.shape[1]
    spec = to_spectrum(x3, cw, sw, fwd)
    hspec = to_spectrum(hx, cw, sw, fwd)
    hspec = jnp.repeat(hspec, CPF, axis=-1)
    hr, hi = hspec[:block], hspec[block:]
    mr, mi = spec[:block, :, 0], spec[block:, :, 0]
    wr, wi = spec[:block, :, 1], spec[block:, :, 1]
    br, bi = spec[:block, :, 2], spec[block:, :, 2]
    conv_r = hr * mr - hi * mi
    conv_i = hr * mi + hi * mr
    gm_r = hr * wr + hi * wi
    gm_i = hr * wi - hi * wr
    fg_r = br * wr + bi * wi
    fg_i = br * wi - bi * wr
    lead = fg_r.shape[:-1]
    fg_r = fg_r.reshape(lead + (-1, CPF)).sum(axis=-1)
    fg_i = fg_i.reshape(lead + (-1, CPF)).sum(axis=-1)
    pair = jnp.concatenate(
        [jnp.stack([conv_r, gm_r], axis=2), jnp.stack([conv_i, gm_i], axis=2)], axis=0
    )
    both = local_signal(pair, inverse)
    fg = all_signal(jnp.concatenate([fg_r, fg_i], axis=0), inv, cw, sw)
    return both[:, 0], both[:, 1], fg


def on_device(qkv_in, qkv_saved, conv_saved, out_grad, filters):
    blocks = lax.axis_size("ctx")
    place = lax.axis_index("ctx")
    block = qkv_in.shape[1]
    channels = qkv_in.shape[3]
    groups = filters.shape[1]
    length = blocks * block
    outer = 2 * blocks
    size = outer * block
    filter_scale = (CPF * length) ** (-0.5)

    query_in = qkv_in[0, :, 0].astype(jnp.float32)
    mixed_in = qkv_in[0, :, 1].astype(jnp.float32) * qkv_in[0, :, 2].astype(jnp.float32)
    query_back = qkv_saved[0, :, 0].astype(jnp.float32)
    key_back = qkv_saved[0, :, 1].astype(jnp.float32)
    value_back = qkv_saved[0, :, 2].astype(jnp.float32)
    mixed_back = key_back * value_back
    upstream = out_grad[0].astype(jnp.float32)
    weighted = upstream * query_back
    grad_query = upstream * conv_saved[0]
    taps = filters[0].T

    ahead = jnp.concatenate([mixed_in, taps], axis=1)
    behind = jnp.concatenate([weighted, taps], axis=1)
    got_ahead = [from_behind(ahead, "ctx", s) for s in range(1, blocks)]
    got_behind = [from_behind(behind, "ctx", -s) for s in range(1, blocks)]
    pool = jnp.stack([jnp.zeros_like(ahead)] + got_ahead + got_behind)
    ids = jnp.arange(blocks, dtype=jnp.int32)
    pick = jnp.where(ids < place, place - ids, jnp.where(ids > place, blocks - 1 + ids - place, 0))
    gathered = pool[pick]
    mine = (ids == place)[:, None, None]
    mixed_all = jnp.where(mine, mixed_in[None], gathered[:, :, :channels])
    weighted_all = jnp.where(mine, weighted[None], gathered[:, :, :channels])
    back_all = jnp.where(mine, mixed_back[None], 0.0)
    hx = jnp.where(mine, taps[None], gathered[:, :, channels:])
    x3 = jnp.stack([mixed_all, weighted_all, back_all], axis=2)

    cw, sw = outer_tables(blocks, block, outer)
    fwd, inv = inner_tables(block)
    pos = place * block + jnp.arange(block, dtype=jnp.int32)
    freq = (
        jnp.arange(outer, dtype=jnp.int32)[None, :]
        + outer * jnp.arange(block, dtype=jnp.int32)[:, None]
    )
    prod = (pos[:, None, None] * freq[None]) % size
    theta = prod.astype(jnp.float32) * (2.0 * math.pi / size)
    inverse = jnp.concatenate([jnp.cos(theta), -jnp.sin(theta)], axis=1) / size
    inverse = inverse.reshape(block, 2 * block * outer)
    tables = (cw, sw, fwd, inv, inverse)

    per_group = 2 * block * outer * 4 * 4 * CPF * blocks
    gchunk = groups
    while gchunk > 1 and gchunk * per_group > CHUNK_BYTES and groups % (gchunk // 2) == 0:
        gchunk //= 2
    nchunk = groups // gchunk
    if nchunk == 1:
        conv, grad_mixed, fg = chunk_work(x3, hx, tables)
    else:
        cc = gchunk * CPF
        xs = x3.reshape(blocks, block, 3, nchunk, cc).transpose(3, 0, 1, 2, 4)
        hs = hx.reshape(blocks, block, nchunk, gchunk).transpose(2, 0, 1, 3)
        conv, grad_mixed, fg = lax.map(lambda a: chunk_work(a[0], a[1], tables), (xs, hs))
        conv = conv.transpose(1, 0, 2).reshape(block, channels)
        grad_mixed = grad_mixed.transpose(1, 0, 2).reshape(block, channels)
        fg = fg.transpose(1, 2, 0, 3).reshape(blocks, block, groups)

    lag_sum = fg[place]
    for s in range(1, blocks):
        dest = (place + s) % blocks
        pairs = [(i, (i + s) % blocks) for i in range(blocks)]
        lag_sum = lag_sum + lax.ppermute(fg[dest], "ctx", pairs)

    conv = conv * filter_scale
    grad_mixed = grad_mixed * filter_scale
    result = (query_in * conv).astype(jnp.bfloat16)
    next_input = from_behind(result[None], "pipe", 1)
    grad_key = grad_mixed * value_back
    grad_value = grad_mixed * key_back
    grad_stack = jnp.stack([grad_query, grad_key, grad_value], axis=1).astype(jnp.bfloat16)
    prev_grad = from_behind(grad_stack[None], "pipe", -1)
    filter_grad = (lag_sum * filter_scale).T[None]
    return (next_input, prev_grad, filter_grad)


def solution(mesh):
    return jax.shard_map(
        on_device,
        mesh=mesh,
        in_specs=(
            P("pipe", "ctx", None, None),
            P("pipe", "ctx", None, None),
            P("pipe", "ctx", None),
            P("pipe", "ctx", None),
            P("pipe", None, "ctx"),
        ),
        out_specs=(P("pipe", "ctx", None), P("pipe", "ctx", None, None), P("pipe", None, "ctx")),
        check_vma=False,
    )
```

```python
import math

import numpy as np

import jax
import jax.numpy as jnp
from jax import lax
from jax.sharding import PartitionSpec as P

CPF = 16
CHUNK_BYTES = 36 * 2**20
STEPWISE = 4

highest = lax.Precision.HIGHEST
precise = lax.Precision.HIGH


def from_behind(x, axis, by):
    devices = lax.axis_size(axis)
    pairs = [(i, i + by) for i in range(devices) if 0 <= i + by < devices]
    return lax.ppermute(x, axis, pairs)


def inner_tables(block):
    ids = np.arange(block)
    theta = 2.0 * np.pi * ((ids[:, None] * ids[None, :]) % block) / block
    cos, sin = np.cos(theta), np.sin(theta)
    fwd = np.block([[cos, -sin], [sin, cos]])
    inv = np.block([[cos, sin], [-sin, cos]])
    return jnp.asarray(fwd, jnp.float32), jnp.asarray(inv, jnp.float32)


def outer_tables(blocks, block, outer):
    size = outer * block
    pos = np.arange(blocks)[:, None, None] * block + np.arange(block)[None, None, :]
    prod = (pos * np.arange(outer)[None, :, None]) % size
    theta = 2.0 * np.pi * prod / size
    return jnp.asarray(np.cos(theta), jnp.float32), jnp.asarray(-np.sin(theta), jnp.float32)


def outer_step(parts, cw, sw, index):
    c = lax.dynamic_index_in_dim(cw, index, keepdims=False)
    s = lax.dynamic_index_in_dim(sw, index, keepdims=False)
    tail = (1,) * (parts.ndim - 1)
    c = c.reshape(c.shape[:1] + tail + c.shape[1:])
    s = s.reshape(s.shape[:1] + tail + s.shape[1:])
    return jnp.concatenate([c * parts[None], s * parts[None]], axis=-1)


def inner_step(y, mat):
    shape = y.shape
    return jnp.dot(y.reshape(-1, shape[-1]), mat, precision=precise).reshape(shape)


def chunk_work(local3, common, hsum, tables):
    cw, sw, fwd, inv, inverse, place = tables
    block = local3.shape[-1]
    outer = cw.shape[1]
    own = outer_step(local3, cw, sw, place)
    y = jnp.stack([own[:, 0] + common, own[:, 1] + common, own[:, 2]], axis=1)
    spec = inner_step(y, fwd)
    hspec = jnp.repeat(inner_step(hsum, fwd), CPF, axis=1)
    hr, hi = hspec[..., :block], hspec[..., block:]
    mr, mi = spec[:, 0, :, :block], spec[:, 0, :, block:]
    wr, wi = spec[:, 1, :, :block], spec[:, 1, :, block:]
    br, bi = spec[:, 2, :, :block], spec[:, 2, :, block:]
    conv = jnp.concatenate([hr * mr - hi * mi, hr * mi + hi * mr], axis=-1)
    gm = jnp.concatenate([hr * wr + hi * wi, hr * wi - hi * wr], axis=-1)
    fgs = jnp.concatenate([br * wr + bi * wi, br * wi - bi * wr], axis=-1)
    fgs = fgs.reshape(outer, -1, CPF, 2 * block).sum(axis=2)
    pair = jnp.stack([conv, gm]).transpose(0, 2, 1, 3)
    rows = pair.shape[0] * pair.shape[1]
    both = jnp.dot(pair.reshape(rows, -1), inverse, precision=precise)
    both = both.reshape(2, -1, block)
    z = inner_step(fgs, inv)
    zr, zi = z[..., :block], z[..., block:]
    fg = jnp.stack(
        [jnp.sum(cw[p][:, None] * zr + sw[p][:, None] * zi, axis=0) for p in range(cw.shape[0])]
    )
    return both[0], both[1], fg / (outer * block)


def on_device(qkv_in, qkv_saved, conv_saved, out_grad, filters):
    blocks = lax.axis_size("ctx")
    place = lax.axis_index("ctx")
    block = qkv_in.shape[1]
    channels = qkv_in.shape[3]
    groups = filters.shape[1]
    length = blocks * block
    outer = 2 * blocks
    size = outer * block
    filter_scale = (CPF * length) ** (-0.5)

    query_in = qkv_in[0, :, 0].astype(jnp.float32)
    mixed_in = qkv_in[0, :, 1].astype(jnp.float32) * qkv_in[0, :, 2].astype(jnp.float32)
    query_back = qkv_saved[0, :, 0].astype(jnp.float32)
    key_back = qkv_saved[0, :, 1].astype(jnp.float32)
    value_back = qkv_saved[0, :, 2].astype(jnp.float32)
    mixed_back = key_back * value_back
    upstream = out_grad[0].astype(jnp.float32)
    weighted = upstream * query_back
    grad_query = upstream * conv_saved[0]
    taps = filters[0]

    cw, sw = outer_tables(blocks, block, outer)
    fwd, inv = inner_tables(block)

    mixed_rows = mixed_in.T
    weighted_rows = weighted.T
    received = []
    for s in range(1, blocks):
        dest = place + s
        first = jnp.where(dest < blocks, mixed_rows, weighted_rows)
        payload = jnp.concatenate([first, taps], axis=0)
        pairs = [(i, (i + s) % blocks) for i in range(blocks)]
        received.append(lax.ppermute(payload, "ctx", pairs))
    hsum = outer_step(taps, cw, sw, place)
    if blocks <= STEPWISE:
        common = 0.0
        for s, got in enumerate(received, start=1):
            part = outer_step(got, cw, sw, (place - s) % blocks)
            common = common + part[:, :channels]
            hsum = hsum + part[:, channels:]
    else:
        got = jnp.stack(received)
        sources = (place - jnp.arange(1, blocks, dtype=jnp.int32)) % blocks
        weights = jnp.concatenate([cw[sources], sw[sources]], axis=-1)
        both = jnp.concatenate([got, got], axis=-1)
        part = jnp.einsum("sfp,scp->fcp", weights, both, precision=highest)
        common = part[:, :channels]
        hsum = hsum + part[:, channels:]
    local3 = jnp.stack([mixed_rows, weighted_rows, mixed_back.T])

    pos = place * block + jnp.arange(block, dtype=jnp.int32)
    freq = (
        jnp.arange(outer, dtype=jnp.int32)[:, None, None]
        + outer * jnp.arange(block, dtype=jnp.int32)[None, None, :]
    )
    prod = (freq * pos[None, :, None]) % size
    theta = prod.astype(jnp.float32) * (2.0 * math.pi / size)
    inverse = jnp.concatenate([jnp.cos(theta), -jnp.sin(theta)], axis=-1) / size
    inverse = inverse.transpose(0, 2, 1).reshape(outer * 2 * block, block)
    tables = (cw, sw, fwd, inv, inverse, place)

    per_group = 2 * block * outer * 4 * 4 * CPF * blocks
    gchunk = groups
    while gchunk > 1 and gchunk * per_group > CHUNK_BYTES and groups % (gchunk // 2) == 0:
        gchunk //= 2
    nchunk = groups // gchunk
    if nchunk == 1:
        conv, grad_mixed, fg = chunk_work(local3, common, hsum, tables)
    else:
        cc = gchunk * CPF
        ls = local3.reshape(3, nchunk, cc, block).transpose(1, 0, 2, 3)
        cs = common.reshape(outer, nchunk, cc, 2 * block).transpose(1, 0, 2, 3)
        hs = hsum.reshape(outer, nchunk, gchunk, 2 * block).transpose(1, 0, 2, 3)
        conv, grad_mixed, fg = lax.map(lambda a: chunk_work(a[0], a[1], a[2], tables), (ls, cs, hs))
        conv = conv.reshape(channels, block)
        grad_mixed = grad_mixed.reshape(channels, block)
        fg = fg.transpose(1, 0, 2, 3).reshape(blocks, groups, block)

    lag_sum = fg[place]
    for s in range(1, blocks):
        dest = (place + s) % blocks
        pairs = [(i, (i + s) % blocks) for i in range(blocks)]
        lag_sum = lag_sum + lax.ppermute(fg[dest], "ctx", pairs)

    conv = conv.T * filter_scale
    grad_mixed = grad_mixed.T * filter_scale
    result = (query_in * conv).astype(jnp.bfloat16)
    next_input = from_behind(result[None], "pipe", 1)
    grad_key = grad_mixed * value_back
    grad_value = grad_mixed * key_back
    grad_stack = jnp.stack([grad_query, grad_key, grad_value], axis=1).astype(jnp.bfloat16)
    prev_grad = from_behind(grad_stack[None], "pipe", -1)
    filter_grad = (lag_sum * filter_scale)[None]
    return (next_input, prev_grad, filter_grad)


def solution(mesh):
    return jax.shard_map(
        on_device,
        mesh=mesh,
        in_specs=(
            P("pipe", "ctx", None, None),
            P("pipe", "ctx", None, None),
            P("pipe", "ctx", None),
            P("pipe", "ctx", None),
            P("pipe", None, "ctx"),
        ),
        out_specs=(P("pipe", "ctx", None), P("pipe", "ctx", None, None), P("pipe", None, "ctx")),
        check_vma=False,
    )
```

```python
import math

import numpy as np

import jax
import jax.numpy as jnp
from jax import lax
from jax.sharding import PartitionSpec as P

CPF = 16
CHUNK_BYTES = 36 * 2**20
STEPWISE = 4
DENSE = 4

highest = lax.Precision.HIGHEST
precise = lax.Precision.HIGH


def from_behind(x, axis, by):
    devices = lax.axis_size(axis)
    pairs = [(i, i + by) for i in range(devices) if 0 <= i + by < devices]
    return lax.ppermute(x, axis, pairs)


def inner_tables(block):
    ids = np.arange(block)
    theta = 2.0 * np.pi * ((ids[:, None] * ids[None, :]) % block) / block
    cos, sin = np.cos(theta), np.sin(theta)
    fwd = np.block([[cos, -sin], [sin, cos]])
    inv = np.block([[cos, sin], [-sin, cos]])
    return jnp.asarray(fwd, jnp.float32), jnp.asarray(inv, jnp.float32)


def outer_tables(blocks, block, outer):
    size = outer * block
    pos = np.arange(blocks)[:, None, None] * block + np.arange(block)[None, None, :]
    prod = (pos * np.arange(outer)[None, :, None]) % size
    theta = 2.0 * np.pi * prod / size
    return jnp.asarray(np.cos(theta), jnp.float32), jnp.asarray(-np.sin(theta), jnp.float32)


def outer_step(parts, cw, sw, index):
    c = lax.dynamic_index_in_dim(cw, index, keepdims=False)
    s = lax.dynamic_index_in_dim(sw, index, keepdims=False)
    tail = (1,) * (parts.ndim - 1)
    c = c.reshape(c.shape[:1] + tail + c.shape[1:])
    s = s.reshape(s.shape[:1] + tail + s.shape[1:])
    return jnp.concatenate([c * parts[None], s * parts[None]], axis=-1)


def inner_step(y, mat):
    shape = y.shape
    return jnp.dot(y.reshape(-1, shape[-1]), mat, precision=precise).reshape(shape)


def packed_tables(blocks, block):
    size = 2 * blocks * block
    half = size // 2
    ids = np.arange(block)
    freqs = np.arange(half)
    theta = 2.0 * np.pi * ((ids[:, None] * freqs[None, :]) % size) / size
    phase = 2.0 * np.pi * ((np.arange(blocks)[:, None] * block * freqs[None, :]) % size) / size
    as32 = lambda a: jnp.asarray(a, jnp.float32)
    return as32(np.cos(theta)), as32(np.sin(theta)), as32(np.cos(phase)), as32(np.sin(phase))


def block_table(packed, index):
    base_c, base_s, turn_c, turn_s = packed
    c = lax.dynamic_index_in_dim(turn_c, index, keepdims=True)
    s = lax.dynamic_index_in_dim(turn_s, index, keepdims=True)
    cos = base_c * c - base_s * s
    sin = base_s * c + base_c * s
    block, half = cos.shape
    first = lax.broadcasted_iota(jnp.int32, (block, half), 1) == 0
    sign = 1.0 - 2.0 * (lax.broadcasted_iota(jnp.int32, (block, half), 0) % 2).astype(jnp.float32)
    return jnp.concatenate([cos, jnp.where(first, sign, -sin)], axis=1)


def packed_products(h, a, conj):
    half = h.shape[1] // 2
    hr, hi = h[:, :half], h[:, half:]
    ar, ai = a[:, :half], a[:, half:]
    first = lax.broadcasted_iota(jnp.int32, hr.shape, 1) == 0
    sign = -1.0 if conj else 1.0
    re = hr * ar - sign * jnp.where(first, 0.0, hi * ai)
    im = jnp.where(first, hi * ai, hr * ai + sign * (hi * ar))
    return jnp.concatenate([re, im], axis=1)


def dense_path(place, blocks, mixed_rows, weighted_rows, back_rows, taps):
    channels, block = mixed_rows.shape
    size = 2 * blocks * block
    half = size // 2
    packed = packed_tables(blocks, block)
    acc = 0.0
    for s in range(1, blocks):
        first = jnp.where(place + s < blocks, mixed_rows, weighted_rows)
        payload = jnp.concatenate([first, back_rows, taps], axis=0)
        pairs = [(i, (i + s) % blocks) for i in range(blocks)]
        got = lax.ppermute(payload, "ctx", pairs)
        table = block_table(packed, (place - s) % blocks)
        acc = acc + jnp.dot(got, table, precision=precise)
    own_table = block_table(packed, place)
    own = jnp.concatenate([mixed_rows, weighted_rows, back_rows, taps], axis=0)
    loc = jnp.dot(own, own_table, precision=precise)
    c = channels
    mixed_spec = loc[:c] + acc[:c]
    weighted_spec = loc[c : 2 * c] + acc[:c]
    back_spec = loc[2 * c : 3 * c] + acc[c : 2 * c]
    taps_spec = jnp.repeat(loc[3 * c :] + acc[2 * c :], CPF, axis=0)
    conv = packed_products(taps_spec, mixed_spec, False)
    gm = packed_products(taps_spec, weighted_spec, True)
    fgs = packed_products(back_spec, weighted_spec, True)
    fgs = fgs.reshape(-1, CPF, size).sum(axis=1)
    both = jnp.concatenate([conv, gm, fgs], axis=0)
    cols = lax.broadcasted_iota(jnp.int32, (1, size), 1)
    weight = jnp.where((cols == 0) | (cols == half), 1.0 / size, 2.0 / size)
    out = jnp.einsum("tf,rf->tr", own_table * weight, both, precision=precise)
    return out[:, :c], out[:, c : 2 * c], out[:, 2 * c :].T


def chunk_work(local3, common, hsum, tables):
    cw, sw, fwd, inv, inverse, place = tables
    block = local3.shape[-1]
    outer = cw.shape[1]
    own = outer_step(local3, cw, sw, place)
    y = jnp.stack([own[:, 0] + common, own[:, 1] + common, own[:, 2]], axis=1)
    spec = inner_step(y, fwd)
    hspec = jnp.repeat(inner_step(hsum, fwd), CPF, axis=1)
    hr, hi = hspec[..., :block], hspec[..., block:]
    mr, mi = spec[:, 0, :, :block], spec[:, 0, :, block:]
    wr, wi = spec[:, 1, :, :block], spec[:, 1, :, block:]
    br, bi = spec[:, 2, :, :block], spec[:, 2, :, block:]
    conv = jnp.concatenate([hr * mr - hi * mi, hr * mi + hi * mr], axis=-1)
    gm = jnp.concatenate([hr * wr + hi * wi, hr * wi - hi * wr], axis=-1)
    fgs = jnp.concatenate([br * wr + bi * wi, br * wi - bi * wr], axis=-1)
    fgs = fgs.reshape(outer, -1, CPF, 2 * block).sum(axis=2)
    pair = jnp.stack([conv, gm]).transpose(0, 2, 1, 3)
    rows = pair.shape[0] * pair.shape[1]
    both = jnp.dot(pair.reshape(rows, -1), inverse, precision=precise)
    both = both.reshape(2, -1, block)
    z = inner_step(fgs, inv)
    zr, zi = z[..., :block], z[..., block:]
    fg = jnp.stack(
        [jnp.sum(cw[p][:, None] * zr + sw[p][:, None] * zi, axis=0) for p in range(cw.shape[0])]
    )
    return both[0], both[1], fg / (outer * block)


def finish(conv, grad_mixed, lag, filter_scale, query_in, grad_query, key_back, value_back):
    conv = conv * filter_scale
    grad_mixed = grad_mixed * filter_scale
    result = (query_in * conv).astype(jnp.bfloat16)
    next_input = from_behind(result[None], "pipe", 1)
    grad_key = grad_mixed * value_back
    grad_value = grad_mixed * key_back
    grad_stack = jnp.stack([grad_query, grad_key, grad_value], axis=1).astype(jnp.bfloat16)
    prev_grad = from_behind(grad_stack[None], "pipe", -1)
    filter_grad = (lag * filter_scale)[None]
    return (next_input, prev_grad, filter_grad)


def on_device(qkv_in, qkv_saved, conv_saved, out_grad, filters):
    blocks = lax.axis_size("ctx")
    place = lax.axis_index("ctx")
    block = qkv_in.shape[1]
    channels = qkv_in.shape[3]
    groups = filters.shape[1]
    length = blocks * block
    outer = 2 * blocks
    size = outer * block
    filter_scale = (CPF * length) ** (-0.5)

    query_in = qkv_in[0, :, 0].astype(jnp.float32)
    mixed_in = qkv_in[0, :, 1].astype(jnp.float32) * qkv_in[0, :, 2].astype(jnp.float32)
    query_back = qkv_saved[0, :, 0].astype(jnp.float32)
    key_back = qkv_saved[0, :, 1].astype(jnp.float32)
    value_back = qkv_saved[0, :, 2].astype(jnp.float32)
    mixed_back = key_back * value_back
    upstream = out_grad[0].astype(jnp.float32)
    weighted = upstream * query_back
    grad_query = upstream * conv_saved[0]
    taps = filters[0]

    if blocks <= DENSE:
        conv, grad_mixed, lag = dense_path(
            place, blocks, mixed_in.T, weighted.T, mixed_back.T, taps
        )
        return finish(
            conv, grad_mixed, lag, filter_scale, query_in, grad_query, key_back, value_back
        )

    cw, sw = outer_tables(blocks, block, outer)
    fwd, inv = inner_tables(block)

    mixed_rows = mixed_in.T
    weighted_rows = weighted.T
    received = []
    for s in range(1, blocks):
        dest = place + s
        first = jnp.where(dest < blocks, mixed_rows, weighted_rows)
        payload = jnp.concatenate([first, taps], axis=0)
        pairs = [(i, (i + s) % blocks) for i in range(blocks)]
        received.append(lax.ppermute(payload, "ctx", pairs))
    hsum = outer_step(taps, cw, sw, place)
    if blocks <= STEPWISE:
        common = 0.0
        for s, got in enumerate(received, start=1):
            part = outer_step(got, cw, sw, (place - s) % blocks)
            common = common + part[:, :channels]
            hsum = hsum + part[:, channels:]
    else:
        got = jnp.stack(received)
        sources = (place - jnp.arange(1, blocks, dtype=jnp.int32)) % blocks
        weights = jnp.concatenate([cw[sources], sw[sources]], axis=-1)
        both = jnp.concatenate([got, got], axis=-1)
        part = jnp.einsum("sfp,scp->fcp", weights, both, precision=highest)
        common = part[:, :channels]
        hsum = hsum + part[:, channels:]
    local3 = jnp.stack([mixed_rows, weighted_rows, mixed_back.T])

    pos = place * block + jnp.arange(block, dtype=jnp.int32)
    freq = (
        jnp.arange(outer, dtype=jnp.int32)[:, None, None]
        + outer * jnp.arange(block, dtype=jnp.int32)[None, None, :]
    )
    prod = (freq * pos[None, :, None]) % size
    theta = prod.astype(jnp.float32) * (2.0 * math.pi / size)
    inverse = jnp.concatenate([jnp.cos(theta), -jnp.sin(theta)], axis=-1) / size
    inverse = inverse.transpose(0, 2, 1).reshape(outer * 2 * block, block)
    tables = (cw, sw, fwd, inv, inverse, place)

    per_group = 2 * block * outer * 4 * 4 * CPF * blocks
    gchunk = groups
    while gchunk > 1 and gchunk * per_group > CHUNK_BYTES and groups % (gchunk // 2) == 0:
        gchunk //= 2
    nchunk = groups // gchunk
    if nchunk == 1:
        conv, grad_mixed, fg = chunk_work(local3, common, hsum, tables)
    else:
        cc = gchunk * CPF
        ls = local3.reshape(3, nchunk, cc, block).transpose(1, 0, 2, 3)
        cs = common.reshape(outer, nchunk, cc, 2 * block).transpose(1, 0, 2, 3)
        hs = hsum.reshape(outer, nchunk, gchunk, 2 * block).transpose(1, 0, 2, 3)
        conv, grad_mixed, fg = lax.map(lambda a: chunk_work(a[0], a[1], a[2], tables), (ls, cs, hs))
        conv = conv.reshape(channels, block)
        grad_mixed = grad_mixed.reshape(channels, block)
        fg = fg.transpose(1, 0, 2, 3).reshape(blocks, groups, block)

    lag_sum = fg[place]
    for s in range(1, blocks):
        dest = (place + s) % blocks
        pairs = [(i, (i + s) % blocks) for i in range(blocks)]
        lag_sum = lag_sum + lax.ppermute(fg[dest], "ctx", pairs)

    return finish(
        conv.T, grad_mixed.T, lag_sum, filter_scale, query_in, grad_query, key_back, value_back
    )


def solution(mesh):
    return jax.shard_map(
        on_device,
        mesh=mesh,
        in_specs=(
            P("pipe", "ctx", None, None),
            P("pipe", "ctx", None, None),
            P("pipe", "ctx", None),
            P("pipe", "ctx", None),
            P("pipe", None, "ctx"),
        ),
        out_specs=(P("pipe", "ctx", None), P("pipe", "ctx", None, None), P("pipe", None, "ctx")),
        check_vma=False,
    )
```

```python
import math

import numpy as np

import jax
import jax.numpy as jnp
from jax import lax
from jax.sharding import PartitionSpec as P

CPF = 16
CHUNK_BYTES = 36 * 2**20
STEPWISE = 4
DENSE = 4

highest = lax.Precision.HIGHEST
precise = lax.Precision.HIGH


def from_behind(x, axis, by):
    devices = lax.axis_size(axis)
    pairs = [(i, i + by) for i in range(devices) if 0 <= i + by < devices]
    return lax.ppermute(x, axis, pairs)


def inner_tables(block):
    ids = np.arange(block)
    theta = 2.0 * np.pi * ((ids[:, None] * ids[None, :]) % block) / block
    cos, sin = np.cos(theta), np.sin(theta)
    fwd = np.block([[cos, -sin], [sin, cos]])
    inv = np.block([[cos, sin], [-sin, cos]])
    return jnp.asarray(fwd, jnp.float32), jnp.asarray(inv, jnp.float32)


def outer_tables(blocks, block, outer):
    size = outer * block
    pos = np.arange(blocks)[:, None, None] * block + np.arange(block)[None, None, :]
    prod = (pos * np.arange(outer)[None, :, None]) % size
    theta = 2.0 * np.pi * prod / size
    return jnp.asarray(np.cos(theta), jnp.float32), jnp.asarray(-np.sin(theta), jnp.float32)


def outer_step(parts, cw, sw, index):
    c = lax.dynamic_index_in_dim(cw, index, keepdims=False)
    s = lax.dynamic_index_in_dim(sw, index, keepdims=False)
    tail = (1,) * (parts.ndim - 1)
    c = c.reshape(c.shape[:1] + tail + c.shape[1:])
    s = s.reshape(s.shape[:1] + tail + s.shape[1:])
    return jnp.concatenate([c * parts[None], s * parts[None]], axis=-1)


def inner_step(y, mat):
    shape = y.shape
    return jnp.dot(y.reshape(-1, shape[-1]), mat, precision=precise).reshape(shape)


def packed_tables(blocks, block):
    size = 2 * blocks * block
    half = size // 2
    ids = np.arange(block)
    freqs = np.arange(half)
    theta = 2.0 * np.pi * ((ids[:, None] * freqs[None, :]) % size) / size
    phase = 2.0 * np.pi * ((np.arange(blocks)[:, None] * block * freqs[None, :]) % size) / size
    as32 = lambda a: jnp.asarray(a, jnp.float32)
    return as32(np.cos(theta)), as32(np.sin(theta)), as32(np.cos(phase)), as32(np.sin(phase))


def block_table(packed, index):
    base_c, base_s, turn_c, turn_s = packed
    c = lax.dynamic_index_in_dim(turn_c, index, keepdims=True)
    s = lax.dynamic_index_in_dim(turn_s, index, keepdims=True)
    cos = base_c * c - base_s * s
    sin = base_s * c + base_c * s
    block, half = cos.shape
    first = lax.broadcasted_iota(jnp.int32, (block, half), 1) == 0
    sign = 1.0 - 2.0 * (lax.broadcasted_iota(jnp.int32, (block, half), 0) % 2).astype(jnp.float32)
    return jnp.concatenate([cos, jnp.where(first, sign, -sin)], axis=1)


def packed_products(h, a, conj):
    half = h.shape[1] // 2
    hr, hi = h[:, :half], h[:, half:]
    ar, ai = a[:, :half], a[:, half:]
    first = lax.broadcasted_iota(jnp.int32, hr.shape, 1) == 0
    sign = -1.0 if conj else 1.0
    re = hr * ar - sign * jnp.where(first, 0.0, hi * ai)
    im = jnp.where(first, hi * ai, hr * ai + sign * (hi * ar))
    return jnp.concatenate([re, im], axis=1)


def dense_path(place, blocks, mixed_rows, weighted_rows, back_rows, taps):
    channels, block = mixed_rows.shape
    size = 2 * blocks * block
    half = size // 2
    packed = packed_tables(blocks, block)
    acc = 0.0
    for s in range(1, blocks):
        first = jnp.where(place + s < blocks, mixed_rows, weighted_rows)
        payload = jnp.concatenate([first, taps], axis=0)
        pairs = [(i, (i + s) % blocks) for i in range(blocks)]
        got = lax.ppermute(payload, "ctx", pairs)
        table = block_table(packed, (place - s) % blocks)
        acc = acc + jnp.dot(got, table, precision=precise)
    own_table = block_table(packed, place)
    own = jnp.concatenate([mixed_rows, weighted_rows, back_rows, taps], axis=0)
    loc = jnp.dot(own, own_table, precision=precise)
    c = channels
    mixed_spec = loc[:c] + acc[:c]
    weighted_spec = loc[c : 2 * c] + acc[:c]
    back_spec = loc[2 * c : 3 * c]
    taps_spec = jnp.repeat(loc[3 * c :] + acc[c:], CPF, axis=0)
    conv = packed_products(taps_spec, mixed_spec, False)
    gm = packed_products(taps_spec, weighted_spec, True)
    fgs = packed_products(back_spec, weighted_spec, True)
    fgs = fgs.reshape(-1, CPF, size).sum(axis=1)
    cols = lax.broadcasted_iota(jnp.int32, (1, size), 1)
    weight = jnp.where((cols == 0) | (cols == half), 1.0 / size, 2.0 / size)
    both = jnp.concatenate([conv, gm], axis=0)
    out = jnp.einsum("tf,rf->tr", own_table * weight, both, precision=precise)
    lag = jnp.einsum("rf,tf->rt", fgs, own_table * weight, precision=precise)
    for s in range(1, blocks):
        table = block_table(packed, (place + s) % blocks) * weight
        share = jnp.einsum("rf,tf->rt", fgs, table, precision=precise)
        pairs = [(i, (i + s) % blocks) for i in range(blocks)]
        lag = lag + lax.ppermute(share, "ctx", pairs)
    return out[:, :c], out[:, c:], lag


def chunk_work(local3, common, hsum, tables):
    cw, sw, fwd, inv, inverse, place = tables
    block = local3.shape[-1]
    outer = cw.shape[1]
    own = outer_step(local3, cw, sw, place)
    y = jnp.stack([own[:, 0] + common, own[:, 1] + common, own[:, 2]], axis=1)
    spec = inner_step(y, fwd)
    hspec = jnp.repeat(inner_step(hsum, fwd), CPF, axis=1)
    hr, hi = hspec[..., :block], hspec[..., block:]
    mr, mi = spec[:, 0, :, :block], spec[:, 0, :, block:]
    wr, wi = spec[:, 1, :, :block], spec[:, 1, :, block:]
    br, bi = spec[:, 2, :, :block], spec[:, 2, :, block:]
    conv = jnp.concatenate([hr * mr - hi * mi, hr * mi + hi * mr], axis=-1)
    gm = jnp.concatenate([hr * wr + hi * wi, hr * wi - hi * wr], axis=-1)
    fgs = jnp.concatenate([br * wr + bi * wi, br * wi - bi * wr], axis=-1)
    fgs = fgs.reshape(outer, -1, CPF, 2 * block).sum(axis=2)
    pair = jnp.stack([conv, gm]).transpose(0, 2, 1, 3)
    rows = pair.shape[0] * pair.shape[1]
    both = jnp.dot(pair.reshape(rows, -1), inverse, precision=precise)
    both = both.reshape(2, -1, block)
    z = inner_step(fgs, inv)
    zr, zi = z[..., :block], z[..., block:]
    fg = jnp.stack(
        [jnp.sum(cw[p][:, None] * zr + sw[p][:, None] * zi, axis=0) for p in range(cw.shape[0])]
    )
    return both[0], both[1], fg / (outer * block)


def finish(conv, grad_mixed, lag, filter_scale, query_in, grad_query, key_back, value_back):
    conv = conv * filter_scale
    grad_mixed = grad_mixed * filter_scale
    result = (query_in * conv).astype(jnp.bfloat16)
    next_input = from_behind(result[None], "pipe", 1)
    grad_key = grad_mixed * value_back
    grad_value = grad_mixed * key_back
    grad_stack = jnp.stack([grad_query, grad_key, grad_value], axis=1).astype(jnp.bfloat16)
    prev_grad = from_behind(grad_stack[None], "pipe", -1)
    filter_grad = (lag * filter_scale)[None]
    return (next_input, prev_grad, filter_grad)


def on_device(qkv_in, qkv_saved, conv_saved, out_grad, filters):
    blocks = lax.axis_size("ctx")
    place = lax.axis_index("ctx")
    block = qkv_in.shape[1]
    channels = qkv_in.shape[3]
    groups = filters.shape[1]
    length = blocks * block
    outer = 2 * blocks
    size = outer * block
    filter_scale = (CPF * length) ** (-0.5)

    query_in = qkv_in[0, :, 0].astype(jnp.float32)
    mixed_in = qkv_in[0, :, 1].astype(jnp.float32) * qkv_in[0, :, 2].astype(jnp.float32)
    query_back = qkv_saved[0, :, 0].astype(jnp.float32)
    key_back = qkv_saved[0, :, 1].astype(jnp.float32)
    value_back = qkv_saved[0, :, 2].astype(jnp.float32)
    mixed_back = key_back * value_back
    upstream = out_grad[0].astype(jnp.float32)
    weighted = upstream * query_back
    grad_query = upstream * conv_saved[0]
    taps = filters[0]

    if blocks <= DENSE:
        conv, grad_mixed, lag = dense_path(
            place, blocks, mixed_in.T, weighted.T, mixed_back.T, taps
        )
        return finish(
            conv, grad_mixed, lag, filter_scale, query_in, grad_query, key_back, value_back
        )

    cw, sw = outer_tables(blocks, block, outer)
    fwd, inv = inner_tables(block)

    mixed_rows = mixed_in.T
    weighted_rows = weighted.T
    received = []
    for s in range(1, blocks):
        dest = place + s
        first = jnp.where(dest < blocks, mixed_rows, weighted_rows)
        payload = jnp.concatenate([first, taps], axis=0)
        pairs = [(i, (i + s) % blocks) for i in range(blocks)]
        received.append(lax.ppermute(payload, "ctx", pairs))
    hsum = outer_step(taps, cw, sw, place)
    if blocks <= STEPWISE:
        common = 0.0
        for s, got in enumerate(received, start=1):
            part = outer_step(got, cw, sw, (place - s) % blocks)
            common = common + part[:, :channels]
            hsum = hsum + part[:, channels:]
    else:
        got = jnp.stack(received)
        sources = (place - jnp.arange(1, blocks, dtype=jnp.int32)) % blocks
        weights = jnp.concatenate([cw[sources], sw[sources]], axis=-1)
        both = jnp.concatenate([got, got], axis=-1)
        part = jnp.einsum("sfp,scp->fcp", weights, both, precision=highest)
        common = part[:, :channels]
        hsum = hsum + part[:, channels:]
    local3 = jnp.stack([mixed_rows, weighted_rows, mixed_back.T])

    pos = place * block + jnp.arange(block, dtype=jnp.int32)
    freq = (
        jnp.arange(outer, dtype=jnp.int32)[:, None, None]
        + outer * jnp.arange(block, dtype=jnp.int32)[None, None, :]
    )
    prod = (freq * pos[None, :, None]) % size
    theta = prod.astype(jnp.float32) * (2.0 * math.pi / size)
    inverse = jnp.concatenate([jnp.cos(theta), -jnp.sin(theta)], axis=-1) / size
    inverse = inverse.transpose(0, 2, 1).reshape(outer * 2 * block, block)
    tables = (cw, sw, fwd, inv, inverse, place)

    per_group = 2 * block * outer * 4 * 4 * CPF * blocks
    gchunk = groups
    while gchunk > 1 and gchunk * per_group > CHUNK_BYTES and groups % (gchunk // 2) == 0:
        gchunk //= 2
    nchunk = groups // gchunk
    if nchunk == 1:
        conv, grad_mixed, fg = chunk_work(local3, common, hsum, tables)
    else:
        cc = gchunk * CPF
        ls = local3.reshape(3, nchunk, cc, block).transpose(1, 0, 2, 3)
        cs = common.reshape(outer, nchunk, cc, 2 * block).transpose(1, 0, 2, 3)
        hs = hsum.reshape(outer, nchunk, gchunk, 2 * block).transpose(1, 0, 2, 3)
        conv, grad_mixed, fg = lax.map(lambda a: chunk_work(a[0], a[1], a[2], tables), (ls, cs, hs))
        conv = conv.reshape(channels, block)
        grad_mixed = grad_mixed.reshape(channels, block)
        fg = fg.transpose(1, 0, 2, 3).reshape(blocks, groups, block)

    lag_sum = fg[place]
    for s in range(1, blocks):
        dest = (place + s) % blocks
        pairs = [(i, (i + s) % blocks) for i in range(blocks)]
        lag_sum = lag_sum + lax.ppermute(fg[dest], "ctx", pairs)

    return finish(
        conv.T, grad_mixed.T, lag_sum, filter_scale, query_in, grad_query, key_back, value_back
    )


def solution(mesh):
    return jax.shard_map(
        on_device,
        mesh=mesh,
        in_specs=(
            P("pipe", "ctx", None, None),
            P("pipe", "ctx", None, None),
            P("pipe", "ctx", None),
            P("pipe", "ctx", None),
            P("pipe", None, "ctx"),
        ),
        out_specs=(P("pipe", "ctx", None), P("pipe", "ctx", None, None), P("pipe", None, "ctx")),
        check_vma=False,
    )
```

```python
import math

import numpy as np

import jax
import jax.numpy as jnp
from jax import lax
from jax.sharding import PartitionSpec as P

CPF = 16
CHUNK_BYTES = 36 * 2**20
STEPWISE = 4
DENSE = 4

highest = lax.Precision.HIGHEST
precise = lax.Precision.HIGH


def from_behind(x, axis, by):
    devices = lax.axis_size(axis)
    pairs = [(i, i + by) for i in range(devices) if 0 <= i + by < devices]
    return lax.ppermute(x, axis, pairs)


def inner_tables(block):
    ids = np.arange(block)
    theta = 2.0 * np.pi * ((ids[:, None] * ids[None, :]) % block) / block
    cos, sin = np.cos(theta), np.sin(theta)
    fwd = np.block([[cos, -sin], [sin, cos]])
    inv = np.block([[cos, sin], [-sin, cos]])
    return jnp.asarray(fwd, jnp.float32), jnp.asarray(inv, jnp.float32)


def outer_tables(blocks, block, outer):
    size = outer * block
    pos = np.arange(blocks)[:, None, None] * block + np.arange(block)[None, None, :]
    prod = (pos * np.arange(outer)[None, :, None]) % size
    theta = 2.0 * np.pi * prod / size
    return jnp.asarray(np.cos(theta), jnp.float32), jnp.asarray(-np.sin(theta), jnp.float32)


def outer_step(parts, cw, sw, index):
    c = lax.dynamic_index_in_dim(cw, index, keepdims=False)
    s = lax.dynamic_index_in_dim(sw, index, keepdims=False)
    tail = (1,) * (parts.ndim - 1)
    c = c.reshape(c.shape[:1] + tail + c.shape[1:])
    s = s.reshape(s.shape[:1] + tail + s.shape[1:])
    return jnp.concatenate([c * parts[None], s * parts[None]], axis=-1)


def inner_step(y, mat):
    shape = y.shape
    return jnp.dot(y.reshape(-1, shape[-1]), mat, precision=precise).reshape(shape)


def packed_tables(blocks, block):
    size = 2 * blocks * block
    half = size // 2
    ids = np.arange(block)
    freqs = np.arange(half)
    theta = 2.0 * np.pi * ((ids[:, None] * freqs[None, :]) % size) / size
    phase = 2.0 * np.pi * ((np.arange(blocks)[:, None] * block * freqs[None, :]) % size) / size
    as32 = lambda a: jnp.asarray(a, jnp.float32)
    return as32(np.cos(theta)), as32(np.sin(theta)), as32(np.cos(phase)), as32(np.sin(phase))


def block_table(packed, index):
    base_c, base_s, turn_c, turn_s = packed
    c = lax.dynamic_index_in_dim(turn_c, index, keepdims=True)
    s = lax.dynamic_index_in_dim(turn_s, index, keepdims=True)
    cos = base_c * c - base_s * s
    sin = base_s * c + base_c * s
    block, half = cos.shape
    first = lax.broadcasted_iota(jnp.int32, (block, half), 1) == 0
    sign = 1.0 - 2.0 * (lax.broadcasted_iota(jnp.int32, (block, half), 0) % 2).astype(jnp.float32)
    return jnp.concatenate([cos, jnp.where(first, sign, -sin)], axis=1)


def packed_products(h, a, conj):
    half = h.shape[1] // 2
    hr, hi = h[:, :half], h[:, half:]
    ar, ai = a[:, :half], a[:, half:]
    first = lax.broadcasted_iota(jnp.int32, hr.shape, 1) == 0
    sign = -1.0 if conj else 1.0
    re = hr * ar - sign * jnp.where(first, 0.0, hi * ai)
    im = jnp.where(first, hi * ai, hr * ai + sign * (hi * ar))
    return jnp.concatenate([re, im], axis=1)


def dense_path(place, blocks, mixed_rows, weighted_rows, back_rows, taps):
    channels, block = mixed_rows.shape
    size = 2 * blocks * block
    half = size // 2
    packed = packed_tables(blocks, block)
    acc = 0.0
    for s in range(1, blocks):
        first = jnp.where(place + s < blocks, mixed_rows, weighted_rows)
        payload = jnp.concatenate([first, taps], axis=0)
        pairs = [(i, (i + s) % blocks) for i in range(blocks)]
        got = lax.ppermute(payload, "ctx", pairs)
        table = block_table(packed, (place - s) % blocks)
        acc = acc + jnp.dot(got, table, precision=precise)
    own_table = block_table(packed, place)
    own = jnp.concatenate([mixed_rows, weighted_rows, back_rows, taps], axis=0)
    loc = jnp.dot(own, own_table, precision=precise)
    c = channels
    mixed_spec = loc[:c] + acc[:c]
    weighted_spec = loc[c : 2 * c] + acc[:c]
    back_spec = loc[2 * c : 3 * c]
    taps_spec = jnp.repeat(loc[3 * c :] + acc[c:], CPF, axis=0)
    conv = packed_products(taps_spec, mixed_spec, False)
    gm = packed_products(taps_spec, weighted_spec, True)
    fgs = packed_products(back_spec, weighted_spec, True)
    fgs = fgs.reshape(-1, CPF, size).sum(axis=1)
    cols = lax.broadcasted_iota(jnp.int32, (1, size), 1)
    weight = jnp.where((cols == 0) | (cols == half), 1.0 / size, 2.0 / size)
    both = jnp.concatenate([conv, gm], axis=0)
    out = jnp.einsum("tf,rf->tr", own_table * weight, both, precision=precise)
    tables = jnp.stack([block_table(packed, b) for b in range(blocks)]) * weight
    shares = jnp.einsum("rf,btf->brt", fgs, tables, precision=precise)
    lag = lax.psum_scatter(shares, "ctx", scatter_dimension=0, tiled=True)[0]
    return out[:, :c], out[:, c:], lag


def chunk_work(local3, common, hsum, tables):
    cw, sw, fwd, inv, inverse, place = tables
    block = local3.shape[-1]
    outer = cw.shape[1]
    own = outer_step(local3, cw, sw, place)
    y = jnp.stack([own[:, 0] + common, own[:, 1] + common, own[:, 2]], axis=1)
    spec = inner_step(y, fwd)
    hspec = jnp.repeat(inner_step(hsum, fwd), CPF, axis=1)
    hr, hi = hspec[..., :block], hspec[..., block:]
    mr, mi = spec[:, 0, :, :block], spec[:, 0, :, block:]
    wr, wi = spec[:, 1, :, :block], spec[:, 1, :, block:]
    br, bi = spec[:, 2, :, :block], spec[:, 2, :, block:]
    conv = jnp.concatenate([hr * mr - hi * mi, hr * mi + hi * mr], axis=-1)
    gm = jnp.concatenate([hr * wr + hi * wi, hr * wi - hi * wr], axis=-1)
    fgs = jnp.concatenate([br * wr + bi * wi, br * wi - bi * wr], axis=-1)
    fgs = fgs.reshape(outer, -1, CPF, 2 * block).sum(axis=2)
    pair = jnp.stack([conv, gm]).transpose(0, 2, 1, 3)
    rows = pair.shape[0] * pair.shape[1]
    both = jnp.dot(pair.reshape(rows, -1), inverse, precision=precise)
    both = both.reshape(2, -1, block)
    z = inner_step(fgs, inv)
    zr, zi = z[..., :block], z[..., block:]
    fg = jnp.stack(
        [jnp.sum(cw[p][:, None] * zr + sw[p][:, None] * zi, axis=0) for p in range(cw.shape[0])]
    )
    return both[0], both[1], fg / (outer * block)


def finish(conv, grad_mixed, lag, filter_scale, query_in, grad_query, key_back, value_back):
    conv = conv * filter_scale
    grad_mixed = grad_mixed * filter_scale
    result = (query_in * conv).astype(jnp.bfloat16)
    next_input = from_behind(result[None], "pipe", 1)
    grad_key = grad_mixed * value_back
    grad_value = grad_mixed * key_back
    grad_stack = jnp.stack([grad_query, grad_key, grad_value], axis=1).astype(jnp.bfloat16)
    prev_grad = from_behind(grad_stack[None], "pipe", -1)
    filter_grad = (lag * filter_scale)[None]
    return (next_input, prev_grad, filter_grad)


def on_device(qkv_in, qkv_saved, conv_saved, out_grad, filters):
    blocks = lax.axis_size("ctx")
    place = lax.axis_index("ctx")
    block = qkv_in.shape[1]
    channels = qkv_in.shape[3]
    groups = filters.shape[1]
    length = blocks * block
    outer = 2 * blocks
    size = outer * block
    filter_scale = (CPF * length) ** (-0.5)

    query_in = qkv_in[0, :, 0].astype(jnp.float32)
    mixed_in = qkv_in[0, :, 1].astype(jnp.float32) * qkv_in[0, :, 2].astype(jnp.float32)
    query_back = qkv_saved[0, :, 0].astype(jnp.float32)
    key_back = qkv_saved[0, :, 1].astype(jnp.float32)
    value_back = qkv_saved[0, :, 2].astype(jnp.float32)
    mixed_back = key_back * value_back
    upstream = out_grad[0].astype(jnp.float32)
    weighted = upstream * query_back
    grad_query = upstream * conv_saved[0]
    taps = filters[0]

    if blocks <= DENSE:
        conv, grad_mixed, lag = dense_path(
            place, blocks, mixed_in.T, weighted.T, mixed_back.T, taps
        )
        return finish(
            conv, grad_mixed, lag, filter_scale, query_in, grad_query, key_back, value_back
        )

    cw, sw = outer_tables(blocks, block, outer)
    fwd, inv = inner_tables(block)

    mixed_rows = mixed_in.T
    weighted_rows = weighted.T
    received = []
    for s in range(1, blocks):
        dest = place + s
        first = jnp.where(dest < blocks, mixed_rows, weighted_rows)
        payload = jnp.concatenate([first, taps], axis=0)
        pairs = [(i, (i + s) % blocks) for i in range(blocks)]
        received.append(lax.ppermute(payload, "ctx", pairs))
    hsum = outer_step(taps, cw, sw, place)
    if blocks <= STEPWISE:
        common = 0.0
        for s, got in enumerate(received, start=1):
            part = outer_step(got, cw, sw, (place - s) % blocks)
            common = common + part[:, :channels]
            hsum = hsum + part[:, channels:]
    else:
        got = jnp.stack(received)
        sources = (place - jnp.arange(1, blocks, dtype=jnp.int32)) % blocks
        weights = jnp.concatenate([cw[sources], sw[sources]], axis=-1)
        both = jnp.concatenate([got, got], axis=-1)
        part = jnp.einsum("sfp,scp->fcp", weights, both, precision=highest)
        common = part[:, :channels]
        hsum = hsum + part[:, channels:]
    local3 = jnp.stack([mixed_rows, weighted_rows, mixed_back.T])

    pos = place * block + jnp.arange(block, dtype=jnp.int32)
    freq = (
        jnp.arange(outer, dtype=jnp.int32)[:, None, None]
        + outer * jnp.arange(block, dtype=jnp.int32)[None, None, :]
    )
    prod = (freq * pos[None, :, None]) % size
    theta = prod.astype(jnp.float32) * (2.0 * math.pi / size)
    inverse = jnp.concatenate([jnp.cos(theta), -jnp.sin(theta)], axis=-1) / size
    inverse = inverse.transpose(0, 2, 1).reshape(outer * 2 * block, block)
    tables = (cw, sw, fwd, inv, inverse, place)

    per_group = 2 * block * outer * 4 * 4 * CPF * blocks
    gchunk = groups
    while gchunk > 1 and gchunk * per_group > CHUNK_BYTES and groups % (gchunk // 2) == 0:
        gchunk //= 2
    nchunk = groups // gchunk
    if nchunk == 1:
        conv, grad_mixed, fg = chunk_work(local3, common, hsum, tables)
    else:
        cc = gchunk * CPF
        ls = local3.reshape(3, nchunk, cc, block).transpose(1, 0, 2, 3)
        cs = common.reshape(outer, nchunk, cc, 2 * block).transpose(1, 0, 2, 3)
        hs = hsum.reshape(outer, nchunk, gchunk, 2 * block).transpose(1, 0, 2, 3)
        conv, grad_mixed, fg = lax.map(lambda a: chunk_work(a[0], a[1], a[2], tables), (ls, cs, hs))
        conv = conv.reshape(channels, block)
        grad_mixed = grad_mixed.reshape(channels, block)
        fg = fg.transpose(1, 0, 2, 3).reshape(blocks, groups, block)

    lag_sum = fg[place]
    for s in range(1, blocks):
        dest = (place + s) % blocks
        pairs = [(i, (i + s) % blocks) for i in range(blocks)]
        lag_sum = lag_sum + lax.ppermute(fg[dest], "ctx", pairs)

    return finish(
        conv.T, grad_mixed.T, lag_sum, filter_scale, query_in, grad_query, key_back, value_back
    )


def solution(mesh):
    return jax.shard_map(
        on_device,
        mesh=mesh,
        in_specs=(
            P("pipe", "ctx", None, None),
            P("pipe", "ctx", None, None),
            P("pipe", "ctx", None),
            P("pipe", "ctx", None),
            P("pipe", None, "ctx"),
        ),
        out_specs=(P("pipe", "ctx", None), P("pipe", "ctx", None, None), P("pipe", None, "ctx")),
        check_vma=False,
    )
```

```python
import math

import numpy as np

import jax
import jax.numpy as jnp
from jax import lax
from jax.sharding import PartitionSpec as P

CPF = 16
CHUNK_BYTES = 36 * 2**20
STEPWISE = 4
DENSE = 4

highest = lax.Precision.HIGHEST
precise = lax.Precision.HIGH


def from_behind(x, axis, by):
    devices = lax.axis_size(axis)
    pairs = [(i, i + by) for i in range(devices) if 0 <= i + by < devices]
    return lax.ppermute(x, axis, pairs)


def inner_tables(block):
    ids = np.arange(block)
    theta = 2.0 * np.pi * ((ids[:, None] * ids[None, :]) % block) / block
    cos, sin = np.cos(theta), np.sin(theta)
    fwd = np.block([[cos, -sin], [sin, cos]])
    inv = np.block([[cos, sin], [-sin, cos]])
    return jnp.asarray(fwd, jnp.float32), jnp.asarray(inv, jnp.float32)


def outer_tables(blocks, block, outer):
    size = outer * block
    pos = np.arange(blocks)[:, None, None] * block + np.arange(block)[None, None, :]
    prod = (pos * np.arange(outer)[None, :, None]) % size
    theta = 2.0 * np.pi * prod / size
    return jnp.asarray(np.cos(theta), jnp.float32), jnp.asarray(-np.sin(theta), jnp.float32)


def outer_step(parts, cw, sw, index):
    c = lax.dynamic_index_in_dim(cw, index, keepdims=False)
    s = lax.dynamic_index_in_dim(sw, index, keepdims=False)
    tail = (1,) * (parts.ndim - 1)
    c = c.reshape(c.shape[:1] + tail + c.shape[1:])
    s = s.reshape(s.shape[:1] + tail + s.shape[1:])
    return jnp.concatenate([c * parts[None], s * parts[None]], axis=-1)


def inner_step(y, mat):
    shape = y.shape
    return jnp.dot(y.reshape(-1, shape[-1]), mat, precision=precise).reshape(shape)


def packed_tables(blocks, block):
    size = 2 * blocks * block
    half = size // 2
    ids = np.arange(block)
    freqs = np.arange(half)
    theta = 2.0 * np.pi * ((ids[:, None] * freqs[None, :]) % size) / size
    phase = 2.0 * np.pi * ((np.arange(blocks)[:, None] * block * freqs[None, :]) % size) / size
    as32 = lambda a: jnp.asarray(a, jnp.float32)
    return as32(np.cos(theta)), as32(np.sin(theta)), as32(np.cos(phase)), as32(np.sin(phase))


def block_table(packed, index):
    base_c, base_s, turn_c, turn_s = packed
    c = lax.dynamic_index_in_dim(turn_c, index, keepdims=True)
    s = lax.dynamic_index_in_dim(turn_s, index, keepdims=True)
    cos = base_c * c - base_s * s
    sin = base_s * c + base_c * s
    block, half = cos.shape
    first = lax.broadcasted_iota(jnp.int32, (block, half), 1) == 0
    sign = 1.0 - 2.0 * (lax.broadcasted_iota(jnp.int32, (block, half), 0) % 2).astype(jnp.float32)
    return jnp.concatenate([cos, jnp.where(first, sign, -sin)], axis=1)


def packed_products(h, a, conj):
    half = h.shape[1] // 2
    hr, hi = h[:, :half], h[:, half:]
    ar, ai = a[:, :half], a[:, half:]
    first = lax.broadcasted_iota(jnp.int32, hr.shape, 1) == 0
    sign = -1.0 if conj else 1.0
    re = hr * ar - sign * jnp.where(first, 0.0, hi * ai)
    im = jnp.where(first, hi * ai, hr * ai + sign * (hi * ar))
    return jnp.concatenate([re, im], axis=1)


def dense_path(place, blocks, mixed_rows, weighted_rows, back_rows, taps):
    channels, block = mixed_rows.shape
    size = 2 * blocks * block
    half = size // 2
    packed = packed_tables(blocks, block)
    target = lax.broadcasted_iota(jnp.int32, (blocks, 1, 1), 0)
    first = jnp.where(target > place, mixed_rows[None], weighted_rows[None])
    payload = jnp.concatenate([first, jnp.broadcast_to(taps, (blocks,) + taps.shape)], axis=1)
    payload = jnp.where(target == place, 0.0, payload)
    got = lax.all_to_all(payload, "ctx", 0, 0, tiled=True)
    tables = jnp.stack([block_table(packed, b) for b in range(blocks)])
    acc = jnp.einsum("brp,bpf->rf", got, tables, precision=precise)
    own_table = block_table(packed, place)
    own = jnp.concatenate([mixed_rows, weighted_rows, back_rows, taps], axis=0)
    loc = jnp.dot(own, own_table, precision=precise)
    c = channels
    mixed_spec = loc[:c] + acc[:c]
    weighted_spec = loc[c : 2 * c] + acc[:c]
    back_spec = loc[2 * c : 3 * c]
    taps_spec = jnp.repeat(loc[3 * c :] + acc[c:], CPF, axis=0)
    conv = packed_products(taps_spec, mixed_spec, False)
    gm = packed_products(taps_spec, weighted_spec, True)
    fgs = packed_products(back_spec, weighted_spec, True)
    fgs = fgs.reshape(-1, CPF, size).sum(axis=1)
    cols = lax.broadcasted_iota(jnp.int32, (1, size), 1)
    weight = jnp.where((cols == 0) | (cols == half), 1.0 / size, 2.0 / size)
    both = jnp.concatenate([conv, gm], axis=0)
    out = jnp.einsum("tf,rf->tr", own_table * weight, both, precision=precise)
    lag = jnp.einsum("rf,tf->rt", fgs, own_table * weight, precision=precise)
    for s in range(1, blocks):
        table = block_table(packed, (place + s) % blocks) * weight
        share = jnp.einsum("rf,tf->rt", fgs, table, precision=precise)
        pairs = [(i, (i + s) % blocks) for i in range(blocks)]
        lag = lag + lax.ppermute(share, "ctx", pairs)
    return out[:, :c], out[:, c:], lag


def chunk_work(local3, common, hsum, tables):
    cw, sw, fwd, inv, inverse, place = tables
    block = local3.shape[-1]
    outer = cw.shape[1]
    own = outer_step(local3, cw, sw, place)
    y = jnp.stack([own[:, 0] + common, own[:, 1] + common, own[:, 2]], axis=1)
    spec = inner_step(y, fwd)
    hspec = jnp.repeat(inner_step(hsum, fwd), CPF, axis=1)
    hr, hi = hspec[..., :block], hspec[..., block:]
    mr, mi = spec[:, 0, :, :block], spec[:, 0, :, block:]
    wr, wi = spec[:, 1, :, :block], spec[:, 1, :, block:]
    br, bi = spec[:, 2, :, :block], spec[:, 2, :, block:]
    conv = jnp.concatenate([hr * mr - hi * mi, hr * mi + hi * mr], axis=-1)
    gm = jnp.concatenate([hr * wr + hi * wi, hr * wi - hi * wr], axis=-1)
    fgs = jnp.concatenate([br * wr + bi * wi, br * wi - bi * wr], axis=-1)
    fgs = fgs.reshape(outer, -1, CPF, 2 * block).sum(axis=2)
    pair = jnp.stack([conv, gm]).transpose(0, 2, 1, 3)
    rows = pair.shape[0] * pair.shape[1]
    both = jnp.dot(pair.reshape(rows, -1), inverse, precision=precise)
    both = both.reshape(2, -1, block)
    z = inner_step(fgs, inv)
    zr, zi = z[..., :block], z[..., block:]
    fg = jnp.stack(
        [jnp.sum(cw[p][:, None] * zr + sw[p][:, None] * zi, axis=0) for p in range(cw.shape[0])]
    )
    return both[0], both[1], fg / (outer * block)


def finish(conv, grad_mixed, lag, filter_scale, query_in, grad_query, key_back, value_back):
    conv = conv * filter_scale
    grad_mixed = grad_mixed * filter_scale
    result = (query_in * conv).astype(jnp.bfloat16)
    next_input = from_behind(result[None], "pipe", 1)
    grad_key = grad_mixed * value_back
    grad_value = grad_mixed * key_back
    grad_stack = jnp.stack([grad_query, grad_key, grad_value], axis=1).astype(jnp.bfloat16)
    prev_grad = from_behind(grad_stack[None], "pipe", -1)
    filter_grad = (lag * filter_scale)[None]
    return (next_input, prev_grad, filter_grad)


def on_device(qkv_in, qkv_saved, conv_saved, out_grad, filters):
    blocks = lax.axis_size("ctx")
    place = lax.axis_index("ctx")
    block = qkv_in.shape[1]
    channels = qkv_in.shape[3]
    groups = filters.shape[1]
    length = blocks * block
    outer = 2 * blocks
    size = outer * block
    filter_scale = (CPF * length) ** (-0.5)

    query_in = qkv_in[0, :, 0].astype(jnp.float32)
    mixed_in = qkv_in[0, :, 1].astype(jnp.float32) * qkv_in[0, :, 2].astype(jnp.float32)
    query_back = qkv_saved[0, :, 0].astype(jnp.float32)
    key_back = qkv_saved[0, :, 1].astype(jnp.float32)
    value_back = qkv_saved[0, :, 2].astype(jnp.float32)
    mixed_back = key_back * value_back
    upstream = out_grad[0].astype(jnp.float32)
    weighted = upstream * query_back
    grad_query = upstream * conv_saved[0]
    taps = filters[0]

    if blocks <= DENSE:
        conv, grad_mixed, lag = dense_path(
            place, blocks, mixed_in.T, weighted.T, mixed_back.T, taps
        )
        return finish(
            conv, grad_mixed, lag, filter_scale, query_in, grad_query, key_back, value_back
        )

    cw, sw = outer_tables(blocks, block, outer)
    fwd, inv = inner_tables(block)

    mixed_rows = mixed_in.T
    weighted_rows = weighted.T
    received = []
    for s in range(1, blocks):
        dest = place + s
        first = jnp.where(dest < blocks, mixed_rows, weighted_rows)
        payload = jnp.concatenate([first, taps], axis=0)
        pairs = [(i, (i + s) % blocks) for i in range(blocks)]
        received.append(lax.ppermute(payload, "ctx", pairs))
    hsum = outer_step(taps, cw, sw, place)
    if blocks <= STEPWISE:
        common = 0.0
        for s, got in enumerate(received, start=1):
            part = outer_step(got, cw, sw, (place - s) % blocks)
            common = common + part[:, :channels]
            hsum = hsum + part[:, channels:]
    else:
        got = jnp.stack(received)
        sources = (place - jnp.arange(1, blocks, dtype=jnp.int32)) % blocks
        weights = jnp.concatenate([cw[sources], sw[sources]], axis=-1)
        both = jnp.concatenate([got, got], axis=-1)
        part = jnp.einsum("sfp,scp->fcp", weights, both, precision=highest)
        common = part[:, :channels]
        hsum = hsum + part[:, channels:]
    local3 = jnp.stack([mixed_rows, weighted_rows, mixed_back.T])

    pos = place * block + jnp.arange(block, dtype=jnp.int32)
    freq = (
        jnp.arange(outer, dtype=jnp.int32)[:, None, None]
        + outer * jnp.arange(block, dtype=jnp.int32)[None, None, :]
    )
    prod = (freq * pos[None, :, None]) % size
    theta = prod.astype(jnp.float32) * (2.0 * math.pi / size)
    inverse = jnp.concatenate([jnp.cos(theta), -jnp.sin(theta)], axis=-1) / size
    inverse = inverse.transpose(0, 2, 1).reshape(outer * 2 * block, block)
    tables = (cw, sw, fwd, inv, inverse, place)

    per_group = 2 * block * outer * 4 * 4 * CPF * blocks
    gchunk = groups
    while gchunk > 1 and gchunk * per_group > CHUNK_BYTES and groups % (gchunk // 2) == 0:
        gchunk //= 2
    nchunk = groups // gchunk
    if nchunk == 1:
        conv, grad_mixed, fg = chunk_work(local3, common, hsum, tables)
    else:
        cc = gchunk * CPF
        ls = local3.reshape(3, nchunk, cc, block).transpose(1, 0, 2, 3)
        cs = common.reshape(outer, nchunk, cc, 2 * block).transpose(1, 0, 2, 3)
        hs = hsum.reshape(outer, nchunk, gchunk, 2 * block).transpose(1, 0, 2, 3)
        conv, grad_mixed, fg = lax.map(lambda a: chunk_work(a[0], a[1], a[2], tables), (ls, cs, hs))
        conv = conv.reshape(channels, block)
        grad_mixed = grad_mixed.reshape(channels, block)
        fg = fg.transpose(1, 0, 2, 3).reshape(blocks, groups, block)

    lag_sum = fg[place]
    for s in range(1, blocks):
        dest = (place + s) % blocks
        pairs = [(i, (i + s) % blocks) for i in range(blocks)]
        lag_sum = lag_sum + lax.ppermute(fg[dest], "ctx", pairs)

    return finish(
        conv.T, grad_mixed.T, lag_sum, filter_scale, query_in, grad_query, key_back, value_back
    )


def solution(mesh):
    return jax.shard_map(
        on_device,
        mesh=mesh,
        in_specs=(
            P("pipe", "ctx", None, None),
            P("pipe", "ctx", None, None),
            P("pipe", "ctx", None),
            P("pipe", "ctx", None),
            P("pipe", None, "ctx"),
        ),
        out_specs=(P("pipe", "ctx", None), P("pipe", "ctx", None, None), P("pipe", None, "ctx")),
        check_vma=False,
    )
```

```python
import math

import numpy as np

import jax
import jax.numpy as jnp
from jax import lax
from jax.sharding import PartitionSpec as P

CPF = 16
CHUNK_BYTES = 36 * 2**20
STEPWISE = 4
DENSE = 4

highest = lax.Precision.HIGHEST
precise = lax.Precision.HIGH


def from_behind(x, axis, by):
    devices = lax.axis_size(axis)
    pairs = [(i, i + by) for i in range(devices) if 0 <= i + by < devices]
    return lax.ppermute(x, axis, pairs)


def inner_tables(block):
    ids = np.arange(block)
    theta = 2.0 * np.pi * ((ids[:, None] * ids[None, :]) % block) / block
    cos, sin = np.cos(theta), np.sin(theta)
    fwd = np.block([[cos, -sin], [sin, cos]])
    inv = np.block([[cos, sin], [-sin, cos]])
    return jnp.asarray(fwd, jnp.float32), jnp.asarray(inv, jnp.float32)


def outer_tables(blocks, block, outer):
    size = outer * block
    pos = np.arange(blocks)[:, None, None] * block + np.arange(block)[None, None, :]
    prod = (pos * np.arange(outer)[None, :, None]) % size
    theta = 2.0 * np.pi * prod / size
    return jnp.asarray(np.cos(theta), jnp.float32), jnp.asarray(-np.sin(theta), jnp.float32)


def outer_step(parts, cw, sw, index):
    c = lax.dynamic_index_in_dim(cw, index, keepdims=False)
    s = lax.dynamic_index_in_dim(sw, index, keepdims=False)
    tail = (1,) * (parts.ndim - 1)
    c = c.reshape(c.shape[:1] + tail + c.shape[1:])
    s = s.reshape(s.shape[:1] + tail + s.shape[1:])
    return jnp.concatenate([c * parts[None], s * parts[None]], axis=-1)


def inner_step(y, mat):
    shape = y.shape
    return jnp.dot(y.reshape(-1, shape[-1]), mat, precision=precise).reshape(shape)


def packed_tables(blocks, block):
    size = 2 * blocks * block
    half = size // 2
    ids = np.arange(block)
    freqs = np.arange(half)
    theta = 2.0 * np.pi * ((ids[:, None] * freqs[None, :]) % size) / size
    phase = 2.0 * np.pi * ((np.arange(blocks)[:, None] * block * freqs[None, :]) % size) / size
    as32 = lambda a: jnp.asarray(a, jnp.float32)
    return as32(np.cos(theta)), as32(np.sin(theta)), as32(np.cos(phase)), as32(np.sin(phase))


def block_table(packed, index):
    base_c, base_s, turn_c, turn_s = packed
    c = lax.dynamic_index_in_dim(turn_c, index, keepdims=True)
    s = lax.dynamic_index_in_dim(turn_s, index, keepdims=True)
    cos = base_c * c - base_s * s
    sin = base_s * c + base_c * s
    block, half = cos.shape
    first = lax.broadcasted_iota(jnp.int32, (block, half), 1) == 0
    sign = 1.0 - 2.0 * (lax.broadcasted_iota(jnp.int32, (block, half), 0) % 2).astype(jnp.float32)
    return jnp.concatenate([cos, jnp.where(first, sign, -sin)], axis=1)


def packed_products(h, a, conj):
    half = h.shape[1] // 2
    hr, hi = h[:, :half], h[:, half:]
    ar, ai = a[:, :half], a[:, half:]
    first = lax.broadcasted_iota(jnp.int32, hr.shape, 1) == 0
    sign = -1.0 if conj else 1.0
    re = hr * ar - sign * jnp.where(first, 0.0, hi * ai)
    im = jnp.where(first, hi * ai, hr * ai + sign * (hi * ar))
    return jnp.concatenate([re, im], axis=1)


def dense_path(place, blocks, mixed_rows, weighted_rows, back_rows, taps):
    channels, block = mixed_rows.shape
    size = 2 * blocks * block
    half = size // 2
    packed = packed_tables(blocks, block)
    acc = 0.0
    for s in range(1, blocks):
        first = jnp.where(place + s < blocks, mixed_rows, weighted_rows)
        payload = jnp.concatenate([first, taps], axis=0)
        pairs = [(i, (i + s) % blocks) for i in range(blocks)]
        got = lax.ppermute(payload, "ctx", pairs)
        table = block_table(packed, (place - s) % blocks)
        acc = acc + jnp.dot(got, table, precision=precise)
    own_table = block_table(packed, place)
    own = jnp.concatenate([mixed_rows, weighted_rows, back_rows, taps], axis=0)
    loc = jnp.dot(own, own_table, precision=precise)
    c = channels
    mixed_spec = loc[:c] + acc[:c]
    weighted_spec = loc[c : 2 * c] + acc[:c]
    back_spec = loc[2 * c : 3 * c]
    taps_spec = jnp.repeat(loc[3 * c :] + acc[c:], CPF, axis=0)
    conv = packed_products(taps_spec, mixed_spec, False)
    gm = packed_products(taps_spec, weighted_spec, True)
    fgs = packed_products(back_spec, weighted_spec, True)
    fgs = fgs.reshape(-1, CPF, size).sum(axis=1)
    cols = lax.broadcasted_iota(jnp.int32, (1, size), 1)
    weight = jnp.where((cols == 0) | (cols == half), 1.0 / size, 2.0 / size)
    both = jnp.concatenate([conv, gm], axis=0)
    out = jnp.einsum("tf,rf->tr", own_table * weight, both, precision=precise)
    if blocks & (blocks - 1):
        lag = jnp.einsum("rf,tf->rt", fgs, own_table * weight, precision=precise)
        for s in range(1, blocks):
            table = block_table(packed, (place + s) % blocks) * weight
            share = jnp.einsum("rf,tf->rt", fgs, table, precision=precise)
            pairs = [(i, (i + s) % blocks) for i in range(blocks)]
            lag = lag + lax.ppermute(share, "ctx", pairs)
        return out[:, :c], out[:, c:], lag
    tables = jnp.stack([block_table(packed, b) for b in range(blocks)]) * weight
    shares = jnp.einsum("rf,btf->brt", fgs, tables, precision=precise)
    bit = blocks // 2
    while bit:
        shares = shares.reshape((2, -1) + shares.shape[1:])
        mine = (place // bit) % 2
        keep = lax.dynamic_index_in_dim(shares, mine, keepdims=False)
        give = lax.dynamic_index_in_dim(shares, 1 - mine, keepdims=False)
        pairs = [(i, i ^ bit) for i in range(blocks)]
        shares = keep + lax.ppermute(give, "ctx", pairs)
        bit //= 2
    return out[:, :c], out[:, c:], shares[0]


def chunk_work(local3, common, hsum, tables):
    cw, sw, fwd, inv, inverse, place = tables
    block = local3.shape[-1]
    outer = cw.shape[1]
    own = outer_step(local3, cw, sw, place)
    y = jnp.stack([own[:, 0] + common, own[:, 1] + common, own[:, 2]], axis=1)
    spec = inner_step(y, fwd)
    hspec = jnp.repeat(inner_step(hsum, fwd), CPF, axis=1)
    hr, hi = hspec[..., :block], hspec[..., block:]
    mr, mi = spec[:, 0, :, :block], spec[:, 0, :, block:]
    wr, wi = spec[:, 1, :, :block], spec[:, 1, :, block:]
    br, bi = spec[:, 2, :, :block], spec[:, 2, :, block:]
    conv = jnp.concatenate([hr * mr - hi * mi, hr * mi + hi * mr], axis=-1)
    gm = jnp.concatenate([hr * wr + hi * wi, hr * wi - hi * wr], axis=-1)
    fgs = jnp.concatenate([br * wr + bi * wi, br * wi - bi * wr], axis=-1)
    fgs = fgs.reshape(outer, -1, CPF, 2 * block).sum(axis=2)
    pair = jnp.stack([conv, gm]).transpose(0, 2, 1, 3)
    rows = pair.shape[0] * pair.shape[1]
    both = jnp.dot(pair.reshape(rows, -1), inverse, precision=precise)
    both = both.reshape(2, -1, block)
    z = inner_step(fgs, inv)
    zr, zi = z[..., :block], z[..., block:]
    fg = jnp.stack(
        [jnp.sum(cw[p][:, None] * zr + sw[p][:, None] * zi, axis=0) for p in range(cw.shape[0])]
    )
    return both[0], both[1], fg / (outer * block)


def finish(conv, grad_mixed, lag, filter_scale, query_in, grad_query, key_back, value_back):
    conv = conv * filter_scale
    grad_mixed = grad_mixed * filter_scale
    result = (query_in * conv).astype(jnp.bfloat16)
    next_input = from_behind(result[None], "pipe", 1)
    grad_key = grad_mixed * value_back
    grad_value = grad_mixed * key_back
    grad_stack = jnp.stack([grad_query, grad_key, grad_value], axis=1).astype(jnp.bfloat16)
    prev_grad = from_behind(grad_stack[None], "pipe", -1)
    filter_grad = (lag * filter_scale)[None]
    return (next_input, prev_grad, filter_grad)


def on_device(qkv_in, qkv_saved, conv_saved, out_grad, filters):
    blocks = lax.axis_size("ctx")
    place = lax.axis_index("ctx")
    block = qkv_in.shape[1]
    channels = qkv_in.shape[3]
    groups = filters.shape[1]
    length = blocks * block
    outer = 2 * blocks
    size = outer * block
    filter_scale = (CPF * length) ** (-0.5)

    query_in = qkv_in[0, :, 0].astype(jnp.float32)
    mixed_in = qkv_in[0, :, 1].astype(jnp.float32) * qkv_in[0, :, 2].astype(jnp.float32)
    query_back = qkv_saved[0, :, 0].astype(jnp.float32)
    key_back = qkv_saved[0, :, 1].astype(jnp.float32)
    value_back = qkv_saved[0, :, 2].astype(jnp.float32)
    mixed_back = key_back * value_back
    upstream = out_grad[0].astype(jnp.float32)
    weighted = upstream * query_back
    grad_query = upstream * conv_saved[0]
    taps = filters[0]

    if blocks <= DENSE:
        conv, grad_mixed, lag = dense_path(
            place, blocks, mixed_in.T, weighted.T, mixed_back.T, taps
        )
        return finish(
            conv, grad_mixed, lag, filter_scale, query_in, grad_query, key_back, value_back
        )

    cw, sw = outer_tables(blocks, block, outer)
    fwd, inv = inner_tables(block)

    mixed_rows = mixed_in.T
    weighted_rows = weighted.T
    received = []
    for s in range(1, blocks):
        dest = place + s
        first = jnp.where(dest < blocks, mixed_rows, weighted_rows)
        payload = jnp.concatenate([first, taps], axis=0)
        pairs = [(i, (i + s) % blocks) for i in range(blocks)]
        received.append(lax.ppermute(payload, "ctx", pairs))
    hsum = outer_step(taps, cw, sw, place)
    if blocks <= STEPWISE:
        common = 0.0
        for s, got in enumerate(received, start=1):
            part = outer_step(got, cw, sw, (place - s) % blocks)
            common = common + part[:, :channels]
            hsum = hsum + part[:, channels:]
    else:
        got = jnp.stack(received)
        sources = (place - jnp.arange(1, blocks, dtype=jnp.int32)) % blocks
        weights = jnp.concatenate([cw[sources], sw[sources]], axis=-1)
        both = jnp.concatenate([got, got], axis=-1)
        part = jnp.einsum("sfp,scp->fcp", weights, both, precision=highest)
        common = part[:, :channels]
        hsum = hsum + part[:, channels:]
    local3 = jnp.stack([mixed_rows, weighted_rows, mixed_back.T])

    pos = place * block + jnp.arange(block, dtype=jnp.int32)
    freq = (
        jnp.arange(outer, dtype=jnp.int32)[:, None, None]
        + outer * jnp.arange(block, dtype=jnp.int32)[None, None, :]
    )
    prod = (freq * pos[None, :, None]) % size
    theta = prod.astype(jnp.float32) * (2.0 * math.pi / size)
    inverse = jnp.concatenate([jnp.cos(theta), -jnp.sin(theta)], axis=-1) / size
    inverse = inverse.transpose(0, 2, 1).reshape(outer * 2 * block, block)
    tables = (cw, sw, fwd, inv, inverse, place)

    per_group = 2 * block * outer * 4 * 4 * CPF * blocks
    gchunk = groups
    while gchunk > 1 and gchunk * per_group > CHUNK_BYTES and groups % (gchunk // 2) == 0:
        gchunk //= 2
    nchunk = groups // gchunk
    if nchunk == 1:
        conv, grad_mixed, fg = chunk_work(local3, common, hsum, tables)
    else:
        cc = gchunk * CPF
        ls = local3.reshape(3, nchunk, cc, block).transpose(1, 0, 2, 3)
        cs = common.reshape(outer, nchunk, cc, 2 * block).transpose(1, 0, 2, 3)
        hs = hsum.reshape(outer, nchunk, gchunk, 2 * block).transpose(1, 0, 2, 3)
        conv, grad_mixed, fg = lax.map(lambda a: chunk_work(a[0], a[1], a[2], tables), (ls, cs, hs))
        conv = conv.reshape(channels, block)
        grad_mixed = grad_mixed.reshape(channels, block)
        fg = fg.transpose(1, 0, 2, 3).reshape(blocks, groups, block)

    lag_sum = fg[place]
    for s in range(1, blocks):
        dest = (place + s) % blocks
        pairs = [(i, (i + s) % blocks) for i in range(blocks)]
        lag_sum = lag_sum + lax.ppermute(fg[dest], "ctx", pairs)

    return finish(
        conv.T, grad_mixed.T, lag_sum, filter_scale, query_in, grad_query, key_back, value_back
    )


def solution(mesh):
    return jax.shard_map(
        on_device,
        mesh=mesh,
        in_specs=(
            P("pipe", "ctx", None, None),
            P("pipe", "ctx", None, None),
            P("pipe", "ctx", None),
            P("pipe", "ctx", None),
            P("pipe", None, "ctx"),
        ),
        out_specs=(P("pipe", "ctx", None), P("pipe", "ctx", None, None), P("pipe", None, "ctx")),
        check_vma=False,
    )
```

```python
import math

import numpy as np

import jax
import jax.numpy as jnp
from jax import lax
from jax.sharding import PartitionSpec as P

CPF = 16
CHUNK_BYTES = 36 * 2**20
STEPWISE = 4
DENSE = 4

highest = lax.Precision.HIGHEST
precise = lax.Precision.HIGH


def from_behind(x, axis, by):
    devices = lax.axis_size(axis)
    pairs = [(i, i + by) for i in range(devices) if 0 <= i + by < devices]
    return lax.ppermute(x, axis, pairs)


def inner_tables(block):
    ids = np.arange(block)
    theta = 2.0 * np.pi * ((ids[:, None] * ids[None, :]) % block) / block
    cos, sin = np.cos(theta), np.sin(theta)
    fwd = np.block([[cos, -sin], [sin, cos]])
    inv = np.block([[cos, sin], [-sin, cos]])
    return jnp.asarray(fwd, jnp.float32), jnp.asarray(inv, jnp.float32)


def outer_tables(blocks, block, outer):
    size = outer * block
    pos = np.arange(blocks)[:, None, None] * block + np.arange(block)[None, None, :]
    prod = (pos * np.arange(outer)[None, :, None]) % size
    theta = 2.0 * np.pi * prod / size
    return jnp.asarray(np.cos(theta), jnp.float32), jnp.asarray(-np.sin(theta), jnp.float32)


def outer_step(parts, cw, sw, index):
    c = lax.dynamic_index_in_dim(cw, index, keepdims=False)
    s = lax.dynamic_index_in_dim(sw, index, keepdims=False)
    tail = (1,) * (parts.ndim - 1)
    c = c.reshape(c.shape[:1] + tail + c.shape[1:])
    s = s.reshape(s.shape[:1] + tail + s.shape[1:])
    return jnp.concatenate([c * parts[None], s * parts[None]], axis=-1)


def inner_step(y, mat):
    shape = y.shape
    return jnp.dot(y.reshape(-1, shape[-1]), mat, precision=precise).reshape(shape)


def packed_tables(blocks, block):
    size = 2 * blocks * block
    half = size // 2
    pos = np.arange(blocks * block)
    theta = 2.0 * np.pi * ((pos[:, None] * np.arange(half)[None, :]) % size) / size
    im = -np.sin(theta)
    im[:, 0] = 1.0 - 2.0 * (pos % 2)
    table = np.concatenate([np.cos(theta), im], axis=1)
    return jnp.asarray(table.reshape(blocks, block, size), jnp.float32)


def block_table(packed, index):
    return lax.dynamic_index_in_dim(packed, index, keepdims=False)


def packed_products(h, a, conj):
    half = h.shape[1] // 2
    hr, hi = h[:, :half], h[:, half:]
    ar, ai = a[:, :half], a[:, half:]
    first = lax.broadcasted_iota(jnp.int32, hr.shape, 1) == 0
    sign = -1.0 if conj else 1.0
    re = hr * ar - sign * jnp.where(first, 0.0, hi * ai)
    im = jnp.where(first, hi * ai, hr * ai + sign * (hi * ar))
    return jnp.concatenate([re, im], axis=1)


def dense_path(place, blocks, mixed_rows, weighted_rows, back_rows, taps):
    channels, block = mixed_rows.shape
    size = 2 * blocks * block
    half = size // 2
    packed = packed_tables(blocks, block)
    acc = 0.0
    for s in range(1, blocks):
        first = jnp.where(place + s < blocks, mixed_rows, weighted_rows)
        payload = jnp.concatenate([first, taps], axis=0)
        pairs = [(i, (i + s) % blocks) for i in range(blocks)]
        got = lax.ppermute(payload, "ctx", pairs)
        table = block_table(packed, (place - s) % blocks)
        acc = acc + jnp.dot(got, table, precision=precise)
    own_table = block_table(packed, place)
    own = jnp.concatenate([mixed_rows, weighted_rows, back_rows, taps], axis=0)
    loc = jnp.dot(own, own_table, precision=precise)
    c = channels
    mixed_spec = loc[:c] + acc[:c]
    weighted_spec = loc[c : 2 * c] + acc[:c]
    back_spec = loc[2 * c : 3 * c]
    taps_spec = jnp.repeat(loc[3 * c :] + acc[c:], CPF, axis=0)
    conv = packed_products(taps_spec, mixed_spec, False)
    gm = packed_products(taps_spec, weighted_spec, True)
    fgs = packed_products(back_spec, weighted_spec, True)
    fgs = fgs.reshape(-1, CPF, size).sum(axis=1)
    cols = lax.broadcasted_iota(jnp.int32, (1, size), 1)
    weight = jnp.where((cols == 0) | (cols == half), 1.0 / size, 2.0 / size)
    both = jnp.concatenate([conv, gm], axis=0)
    out = jnp.einsum("tf,rf->tr", own_table * weight, both, precision=precise)
    lag = jnp.einsum("rf,tf->rt", fgs, own_table * weight, precision=precise)
    for s in range(1, blocks):
        table = block_table(packed, (place + s) % blocks) * weight
        share = jnp.einsum("rf,tf->rt", fgs, table, precision=precise)
        pairs = [(i, (i + s) % blocks) for i in range(blocks)]
        lag = lag + lax.ppermute(share, "ctx", pairs)
    return out[:, :c], out[:, c:], lag


def chunk_work(local3, common, hsum, tables):
    cw, sw, fwd, inv, inverse, place = tables
    block = local3.shape[-1]
    outer = cw.shape[1]
    own = outer_step(local3, cw, sw, place)
    y = jnp.stack([own[:, 0] + common, own[:, 1] + common, own[:, 2]], axis=1)
    spec = inner_step(y, fwd)
    hspec = jnp.repeat(inner_step(hsum, fwd), CPF, axis=1)
    hr, hi = hspec[..., :block], hspec[..., block:]
    mr, mi = spec[:, 0, :, :block], spec[:, 0, :, block:]
    wr, wi = spec[:, 1, :, :block], spec[:, 1, :, block:]
    br, bi = spec[:, 2, :, :block], spec[:, 2, :, block:]
    conv = jnp.concatenate([hr * mr - hi * mi, hr * mi + hi * mr], axis=-1)
    gm = jnp.concatenate([hr * wr + hi * wi, hr * wi - hi * wr], axis=-1)
    fgs = jnp.concatenate([br * wr + bi * wi, br * wi - bi * wr], axis=-1)
    fgs = fgs.reshape(outer, -1, CPF, 2 * block).sum(axis=2)
    pair = jnp.stack([conv, gm]).transpose(0, 2, 1, 3)
    rows = pair.shape[0] * pair.shape[1]
    both = jnp.dot(pair.reshape(rows, -1), inverse, precision=precise)
    both = both.reshape(2, -1, block)
    z = inner_step(fgs, inv)
    zr, zi = z[..., :block], z[..., block:]
    fg = jnp.stack(
        [jnp.sum(cw[p][:, None] * zr + sw[p][:, None] * zi, axis=0) for p in range(cw.shape[0])]
    )
    return both[0], both[1], fg / (outer * block)


def finish(conv, grad_mixed, lag, filter_scale, query_in, grad_query, key_back, value_back):
    conv = conv * filter_scale
    grad_mixed = grad_mixed * filter_scale
    result = (query_in * conv).astype(jnp.bfloat16)
    next_input = from_behind(result[None], "pipe", 1)
    grad_key = grad_mixed * value_back
    grad_value = grad_mixed * key_back
    grad_stack = jnp.stack([grad_query, grad_key, grad_value], axis=1).astype(jnp.bfloat16)
    prev_grad = from_behind(grad_stack[None], "pipe", -1)
    filter_grad = (lag * filter_scale)[None]
    return (next_input, prev_grad, filter_grad)


def on_device(qkv_in, qkv_saved, conv_saved, out_grad, filters):
    blocks = lax.axis_size("ctx")
    place = lax.axis_index("ctx")
    block = qkv_in.shape[1]
    channels = qkv_in.shape[3]
    groups = filters.shape[1]
    length = blocks * block
    outer = 2 * blocks
    size = outer * block
    filter_scale = (CPF * length) ** (-0.5)

    query_in = qkv_in[0, :, 0].astype(jnp.float32)
    mixed_in = qkv_in[0, :, 1].astype(jnp.float32) * qkv_in[0, :, 2].astype(jnp.float32)
    query_back = qkv_saved[0, :, 0].astype(jnp.float32)
    key_back = qkv_saved[0, :, 1].astype(jnp.float32)
    value_back = qkv_saved[0, :, 2].astype(jnp.float32)
    mixed_back = key_back * value_back
    upstream = out_grad[0].astype(jnp.float32)
    weighted = upstream * query_back
    grad_query = upstream * conv_saved[0]
    taps = filters[0]

    if blocks <= DENSE:
        conv, grad_mixed, lag = dense_path(
            place, blocks, mixed_in.T, weighted.T, mixed_back.T, taps
        )
        return finish(
            conv, grad_mixed, lag, filter_scale, query_in, grad_query, key_back, value_back
        )

    cw, sw = outer_tables(blocks, block, outer)
    fwd, inv = inner_tables(block)

    mixed_rows = mixed_in.T
    weighted_rows = weighted.T
    received = []
    for s in range(1, blocks):
        dest = place + s
        first = jnp.where(dest < blocks, mixed_rows, weighted_rows)
        payload = jnp.concatenate([first, taps], axis=0)
        pairs = [(i, (i + s) % blocks) for i in range(blocks)]
        received.append(lax.ppermute(payload, "ctx", pairs))
    hsum = outer_step(taps, cw, sw, place)
    if blocks <= STEPWISE:
        common = 0.0
        for s, got in enumerate(received, start=1):
            part = outer_step(got, cw, sw, (place - s) % blocks)
            common = common + part[:, :channels]
            hsum = hsum + part[:, channels:]
    else:
        got = jnp.stack(received)
        sources = (place - jnp.arange(1, blocks, dtype=jnp.int32)) % blocks
        weights = jnp.concatenate([cw[sources], sw[sources]], axis=-1)
        both = jnp.concatenate([got, got], axis=-1)
        part = jnp.einsum("sfp,scp->fcp", weights, both, precision=highest)
        common = part[:, :channels]
        hsum = hsum + part[:, channels:]
    local3 = jnp.stack([mixed_rows, weighted_rows, mixed_back.T])

    pos = place * block + jnp.arange(block, dtype=jnp.int32)
    freq = (
        jnp.arange(outer, dtype=jnp.int32)[:, None, None]
        + outer * jnp.arange(block, dtype=jnp.int32)[None, None, :]
    )
    prod = (freq * pos[None, :, None]) % size
    theta = prod.astype(jnp.float32) * (2.0 * math.pi / size)
    inverse = jnp.concatenate([jnp.cos(theta), -jnp.sin(theta)], axis=-1) / size
    inverse = inverse.transpose(0, 2, 1).reshape(outer * 2 * block, block)
    tables = (cw, sw, fwd, inv, inverse, place)

    per_group = 2 * block * outer * 4 * 4 * CPF * blocks
    gchunk = groups
    while gchunk > 1 and gchunk * per_group > CHUNK_BYTES and groups % (gchunk // 2) == 0:
        gchunk //= 2
    nchunk = groups // gchunk
    if nchunk == 1:
        conv, grad_mixed, fg = chunk_work(local3, common, hsum, tables)
    else:
        cc = gchunk * CPF
        ls = local3.reshape(3, nchunk, cc, block).transpose(1, 0, 2, 3)
        cs = common.reshape(outer, nchunk, cc, 2 * block).transpose(1, 0, 2, 3)
        hs = hsum.reshape(outer, nchunk, gchunk, 2 * block).transpose(1, 0, 2, 3)
        conv, grad_mixed, fg = lax.map(lambda a: chunk_work(a[0], a[1], a[2], tables), (ls, cs, hs))
        conv = conv.reshape(channels, block)
        grad_mixed = grad_mixed.reshape(channels, block)
        fg = fg.transpose(1, 0, 2, 3).reshape(blocks, groups, block)

    lag_sum = fg[place]
    for s in range(1, blocks):
        dest = (place + s) % blocks
        pairs = [(i, (i + s) % blocks) for i in range(blocks)]
        lag_sum = lag_sum + lax.ppermute(fg[dest], "ctx", pairs)

    return finish(
        conv.T, grad_mixed.T, lag_sum, filter_scale, query_in, grad_query, key_back, value_back
    )


def solution(mesh):
    return jax.shard_map(
        on_device,
        mesh=mesh,
        in_specs=(
            P("pipe", "ctx", None, None),
            P("pipe", "ctx", None, None),
            P("pipe", "ctx", None),
            P("pipe", "ctx", None),
            P("pipe", None, "ctx"),
        ),
        out_specs=(P("pipe", "ctx", None), P("pipe", "ctx", None, None), P("pipe", None, "ctx")),
        check_vma=False,
    )
```

```python
import math

import numpy as np

import jax
import jax.numpy as jnp
from jax import lax
from jax.sharding import PartitionSpec as P

CPF = 16
CHUNK_BYTES = 36 * 2**20
STEPWISE = 4
DENSE = 4

highest = lax.Precision.HIGHEST
precise = lax.Precision.HIGH


def from_behind(x, axis, by):
    devices = lax.axis_size(axis)
    pairs = [(i, i + by) for i in range(devices) if 0 <= i + by < devices]
    return lax.ppermute(x, axis, pairs)


def inner_tables(block):
    ids = np.arange(block)
    theta = 2.0 * np.pi * ((ids[:, None] * ids[None, :]) % block) / block
    cos, sin = np.cos(theta), np.sin(theta)
    fwd = np.block([[cos, -sin], [sin, cos]])
    inv = np.block([[cos, sin], [-sin, cos]])
    return jnp.asarray(fwd, jnp.float32), jnp.asarray(inv, jnp.float32)


def outer_tables(blocks, block, outer):
    size = outer * block
    pos = np.arange(blocks)[:, None, None] * block + np.arange(block)[None, None, :]
    prod = (pos * np.arange(outer)[None, :, None]) % size
    theta = 2.0 * np.pi * prod / size
    return jnp.asarray(np.cos(theta), jnp.float32), jnp.asarray(-np.sin(theta), jnp.float32)


def outer_step(parts, cw, sw, index):
    c = lax.dynamic_index_in_dim(cw, index, keepdims=False)
    s = lax.dynamic_index_in_dim(sw, index, keepdims=False)
    tail = (1,) * (parts.ndim - 1)
    c = c.reshape(c.shape[:1] + tail + c.shape[1:])
    s = s.reshape(s.shape[:1] + tail + s.shape[1:])
    return jnp.concatenate([c * parts[None], s * parts[None]], axis=-1)


def inner_step(y, mat):
    shape = y.shape
    return jnp.dot(y.reshape(-1, shape[-1]), mat, precision=precise).reshape(shape)


def packed_tables(blocks, block):
    size = 2 * blocks * block
    half = size // 2
    ids = np.arange(block)
    freqs = np.arange(half)
    theta = 2.0 * np.pi * ((ids[:, None] * freqs[None, :]) % size) / size
    phase = 2.0 * np.pi * ((np.arange(blocks)[:, None] * block * freqs[None, :]) % size) / size
    as32 = lambda a: jnp.asarray(a, jnp.float32)
    return as32(np.cos(theta)), as32(np.sin(theta)), as32(np.cos(phase)), as32(np.sin(phase))


def block_table(packed, index):
    base_c, base_s, turn_c, turn_s = packed
    c = lax.dynamic_index_in_dim(turn_c, index, keepdims=True)
    s = lax.dynamic_index_in_dim(turn_s, index, keepdims=True)
    cos = base_c * c - base_s * s
    sin = base_s * c + base_c * s
    block, half = cos.shape
    first = lax.broadcasted_iota(jnp.int32, (block, half), 1) == 0
    sign = 1.0 - 2.0 * (lax.broadcasted_iota(jnp.int32, (block, half), 0) % 2).astype(jnp.float32)
    return jnp.concatenate([cos, jnp.where(first, sign, -sin)], axis=1)


def packed_products(h, a, conj):
    half = h.shape[1] // 2
    hr, hi = h[:, :half], h[:, half:]
    ar, ai = a[:, :half], a[:, half:]
    first = lax.broadcasted_iota(jnp.int32, hr.shape, 1) == 0
    sign = -1.0 if conj else 1.0
    re = hr * ar - sign * jnp.where(first, 0.0, hi * ai)
    im = jnp.where(first, hi * ai, hr * ai + sign * (hi * ar))
    return jnp.concatenate([re, im], axis=1)


def dense_path(place, blocks, mixed, weighted, back, taps):
    block, channels = mixed.shape
    size = 2 * blocks * block
    half = size // 2
    packed = packed_tables(blocks, block)
    acc = 0.0
    for s in range(1, blocks):
        first = jnp.where(place + s < blocks, mixed, weighted)
        payload = jnp.concatenate([first, taps], axis=1)
        pairs = [(i, (i + s) % blocks) for i in range(blocks)]
        got = lax.ppermute(payload, "ctx", pairs)
        table = block_table(packed, (place - s) % blocks)
        acc = acc + jnp.einsum("pr,pf->rf", got, table, precision=precise)
    own_table = block_table(packed, place)
    own = jnp.concatenate([mixed, weighted, back, taps], axis=1)
    loc = jnp.einsum("pr,pf->rf", own, own_table, precision=precise)
    c = channels
    mixed_spec = loc[:c] + acc[:c]
    weighted_spec = loc[c : 2 * c] + acc[:c]
    back_spec = loc[2 * c : 3 * c]
    taps_spec = jnp.repeat(loc[3 * c :] + acc[c:], CPF, axis=0)
    conv = packed_products(taps_spec, mixed_spec, False)
    gm = packed_products(taps_spec, weighted_spec, True)
    fgs = packed_products(back_spec, weighted_spec, True)
    fgs = fgs.reshape(-1, CPF, size).sum(axis=1)
    cols = lax.broadcasted_iota(jnp.int32, (1, size), 1)
    weight = jnp.where((cols == 0) | (cols == half), 1.0 / size, 2.0 / size)
    both = jnp.concatenate([conv, gm], axis=0)
    out = jnp.einsum("tf,rf->tr", own_table * weight, both, precision=precise)
    lag = jnp.einsum("rf,tf->rt", fgs, own_table * weight, precision=precise)
    for s in range(1, blocks):
        table = block_table(packed, (place + s) % blocks) * weight
        share = jnp.einsum("rf,tf->rt", fgs, table, precision=precise)
        pairs = [(i, (i + s) % blocks) for i in range(blocks)]
        lag = lag + lax.ppermute(share, "ctx", pairs)
    return out[:, :c], out[:, c:], lag


def chunk_work(local3, common, hsum, tables):
    cw, sw, fwd, inv, inverse, place = tables
    block = local3.shape[-1]
    outer = cw.shape[1]
    own = outer_step(local3, cw, sw, place)
    y = jnp.stack([own[:, 0] + common, own[:, 1] + common, own[:, 2]], axis=1)
    spec = inner_step(y, fwd)
    hspec = jnp.repeat(inner_step(hsum, fwd), CPF, axis=1)
    hr, hi = hspec[..., :block], hspec[..., block:]
    mr, mi = spec[:, 0, :, :block], spec[:, 0, :, block:]
    wr, wi = spec[:, 1, :, :block], spec[:, 1, :, block:]
    br, bi = spec[:, 2, :, :block], spec[:, 2, :, block:]
    conv = jnp.concatenate([hr * mr - hi * mi, hr * mi + hi * mr], axis=-1)
    gm = jnp.concatenate([hr * wr + hi * wi, hr * wi - hi * wr], axis=-1)
    fgs = jnp.concatenate([br * wr + bi * wi, br * wi - bi * wr], axis=-1)
    fgs = fgs.reshape(outer, -1, CPF, 2 * block).sum(axis=2)
    pair = jnp.stack([conv, gm]).transpose(0, 2, 1, 3)
    rows = pair.shape[0] * pair.shape[1]
    both = jnp.dot(pair.reshape(rows, -1), inverse, precision=precise)
    both = both.reshape(2, -1, block)
    z = inner_step(fgs, inv)
    zr, zi = z[..., :block], z[..., block:]
    fg = jnp.stack(
        [jnp.sum(cw[p][:, None] * zr + sw[p][:, None] * zi, axis=0) for p in range(cw.shape[0])]
    )
    return both[0], both[1], fg / (outer * block)


def finish(conv, grad_mixed, lag, filter_scale, query_in, grad_query, key_back, value_back):
    conv = conv * filter_scale
    grad_mixed = grad_mixed * filter_scale
    result = (query_in * conv).astype(jnp.bfloat16)
    next_input = from_behind(result[None], "pipe", 1)
    grad_key = grad_mixed * value_back
    grad_value = grad_mixed * key_back
    grad_stack = jnp.stack([grad_query, grad_key, grad_value], axis=1).astype(jnp.bfloat16)
    prev_grad = from_behind(grad_stack[None], "pipe", -1)
    filter_grad = (lag * filter_scale)[None]
    return (next_input, prev_grad, filter_grad)


def on_device(qkv_in, qkv_saved, conv_saved, out_grad, filters):
    blocks = lax.axis_size("ctx")
    place = lax.axis_index("ctx")
    block = qkv_in.shape[1]
    channels = qkv_in.shape[3]
    groups = filters.shape[1]
    length = blocks * block
    outer = 2 * blocks
    size = outer * block
    filter_scale = (CPF * length) ** (-0.5)

    query_in = qkv_in[0, :, 0].astype(jnp.float32)
    mixed_in = qkv_in[0, :, 1].astype(jnp.float32) * qkv_in[0, :, 2].astype(jnp.float32)
    query_back = qkv_saved[0, :, 0].astype(jnp.float32)
    key_back = qkv_saved[0, :, 1].astype(jnp.float32)
    value_back = qkv_saved[0, :, 2].astype(jnp.float32)
    mixed_back = key_back * value_back
    upstream = out_grad[0].astype(jnp.float32)
    weighted = upstream * query_back
    grad_query = upstream * conv_saved[0]
    taps = filters[0]

    if blocks <= DENSE:
        conv, grad_mixed, lag = dense_path(
            place, blocks, mixed_in, weighted, mixed_back, taps.T
        )
        return finish(
            conv, grad_mixed, lag, filter_scale, query_in, grad_query, key_back, value_back
        )

    cw, sw = outer_tables(blocks, block, outer)
    fwd, inv = inner_tables(block)

    mixed_rows = mixed_in.T
    weighted_rows = weighted.T
    received = []
    for s in range(1, blocks):
        dest = place + s
        first = jnp.where(dest < blocks, mixed_rows, weighted_rows)
        payload = jnp.concatenate([first, taps], axis=0)
        pairs = [(i, (i + s) % blocks) for i in range(blocks)]
        received.append(lax.ppermute(payload, "ctx", pairs))
    hsum = outer_step(taps, cw, sw, place)
    if blocks <= STEPWISE:
        common = 0.0
        for s, got in enumerate(received, start=1):
            part = outer_step(got, cw, sw, (place - s) % blocks)
            common = common + part[:, :channels]
            hsum = hsum + part[:, channels:]
    else:
        got = jnp.stack(received)
        sources = (place - jnp.arange(1, blocks, dtype=jnp.int32)) % blocks
        weights = jnp.concatenate([cw[sources], sw[sources]], axis=-1)
        both = jnp.concatenate([got, got], axis=-1)
        part = jnp.einsum("sfp,scp->fcp", weights, both, precision=highest)
        common = part[:, :channels]
        hsum = hsum + part[:, channels:]
    local3 = jnp.stack([mixed_rows, weighted_rows, mixed_back.T])

    pos = place * block + jnp.arange(block, dtype=jnp.int32)
    freq = (
        jnp.arange(outer, dtype=jnp.int32)[:, None, None]
        + outer * jnp.arange(block, dtype=jnp.int32)[None, None, :]
    )
    prod = (freq * pos[None, :, None]) % size
    theta = prod.astype(jnp.float32) * (2.0 * math.pi / size)
    inverse = jnp.concatenate([jnp.cos(theta), -jnp.sin(theta)], axis=-1) / size
    inverse = inverse.transpose(0, 2, 1).reshape(outer * 2 * block, block)
    tables = (cw, sw, fwd, inv, inverse, place)

    per_group = 2 * block * outer * 4 * 4 * CPF * blocks
    gchunk = groups
    while gchunk > 1 and gchunk * per_group > CHUNK_BYTES and groups % (gchunk // 2) == 0:
        gchunk //= 2
    nchunk = groups // gchunk
    if nchunk == 1:
        conv, grad_mixed, fg = chunk_work(local3, common, hsum, tables)
    else:
        cc = gchunk * CPF
        ls = local3.reshape(3, nchunk, cc, block).transpose(1, 0, 2, 3)
        cs = common.reshape(outer, nchunk, cc, 2 * block).transpose(1, 0, 2, 3)
        hs = hsum.reshape(outer, nchunk, gchunk, 2 * block).transpose(1, 0, 2, 3)
        conv, grad_mixed, fg = lax.map(lambda a: chunk_work(a[0], a[1], a[2], tables), (ls, cs, hs))
        conv = conv.reshape(channels, block)
        grad_mixed = grad_mixed.reshape(channels, block)
        fg = fg.transpose(1, 0, 2, 3).reshape(blocks, groups, block)

    lag_sum = fg[place]
    for s in range(1, blocks):
        dest = (place + s) % blocks
        pairs = [(i, (i + s) % blocks) for i in range(blocks)]
        lag_sum = lag_sum + lax.ppermute(fg[dest], "ctx", pairs)

    return finish(
        conv.T, grad_mixed.T, lag_sum, filter_scale, query_in, grad_query, key_back, value_back
    )


def solution(mesh):
    return jax.shard_map(
        on_device,
        mesh=mesh,
        in_specs=(
            P("pipe", "ctx", None, None),
            P("pipe", "ctx", None, None),
            P("pipe", "ctx", None),
            P("pipe", "ctx", None),
            P("pipe", None, "ctx"),
        ),
        out_specs=(P("pipe", "ctx", None), P("pipe", "ctx", None, None), P("pipe", None, "ctx")),
        check_vma=False,
    )
```

```python
import math

import numpy as np

import jax
import jax.numpy as jnp
from jax import lax
from jax.sharding import PartitionSpec as P

CPF = 16
CHUNK_BYTES = 36 * 2**20
STEPWISE = 4
DENSE = 4

highest = lax.Precision.HIGHEST
precise = lax.Precision.HIGH


def from_behind(x, axis, by):
    devices = lax.axis_size(axis)
    pairs = [(i, i + by) for i in range(devices) if 0 <= i + by < devices]
    return lax.ppermute(x, axis, pairs)


def inner_tables(block):
    ids = np.arange(block)
    theta = 2.0 * np.pi * ((ids[:, None] * ids[None, :]) % block) / block
    cos, sin = np.cos(theta), np.sin(theta)
    fwd = np.block([[cos, -sin], [sin, cos]])
    inv = np.block([[cos, sin], [-sin, cos]])
    return jnp.asarray(fwd, jnp.float32), jnp.asarray(inv, jnp.float32)


def outer_tables(blocks, block, outer):
    size = outer * block
    pos = np.arange(blocks)[:, None, None] * block + np.arange(block)[None, None, :]
    prod = (pos * np.arange(outer)[None, :, None]) % size
    theta = 2.0 * np.pi * prod / size
    return jnp.asarray(np.cos(theta), jnp.float32), jnp.asarray(-np.sin(theta), jnp.float32)


def outer_step(parts, cw, sw, index):
    c = lax.dynamic_index_in_dim(cw, index, keepdims=False)
    s = lax.dynamic_index_in_dim(sw, index, keepdims=False)
    tail = (1,) * (parts.ndim - 1)
    c = c.reshape(c.shape[:1] + tail + c.shape[1:])
    s = s.reshape(s.shape[:1] + tail + s.shape[1:])
    return jnp.concatenate([c * parts[None], s * parts[None]], axis=-1)


def inner_step(y, mat):
    shape = y.shape
    return jnp.dot(y.reshape(-1, shape[-1]), mat, precision=precise).reshape(shape)


def packed_tables(blocks, block):
    size = 2 * blocks * block
    half = size // 2
    ids = np.arange(block)
    freqs = np.arange(half)
    theta = 2.0 * np.pi * ((ids[:, None] * freqs[None, :]) % size) / size
    phase = 2.0 * np.pi * ((np.arange(blocks)[:, None] * block * freqs[None, :]) % size) / size
    as32 = lambda a: jnp.asarray(a, jnp.float32)
    return as32(np.cos(theta)), as32(np.sin(theta)), as32(np.cos(phase)), as32(np.sin(phase))


def block_table(packed, index):
    base_c, base_s, turn_c, turn_s = packed
    c = lax.dynamic_index_in_dim(turn_c, index, keepdims=True)
    s = lax.dynamic_index_in_dim(turn_s, index, keepdims=True)
    cos = base_c * c - base_s * s
    sin = base_s * c + base_c * s
    block, half = cos.shape
    first = lax.broadcasted_iota(jnp.int32, (block, half), 1) == 0
    sign = 1.0 - 2.0 * (lax.broadcasted_iota(jnp.int32, (block, half), 0) % 2).astype(jnp.float32)
    return jnp.concatenate([cos, jnp.where(first, sign, -sin)], axis=1)


def packed_products(h, a, conj):
    half = h.shape[1] // 2
    hr, hi = h[:, :half], h[:, half:]
    ar, ai = a[:, :half], a[:, half:]
    first = lax.broadcasted_iota(jnp.int32, hr.shape, 1) == 0
    sign = -1.0 if conj else 1.0
    re = hr * ar - sign * jnp.where(first, 0.0, hi * ai)
    im = jnp.where(first, hi * ai, hr * ai + sign * (hi * ar))
    return jnp.concatenate([re, im], axis=1)


def dense_path(place, blocks, mixed, weighted, back, taps):
    block, channels = mixed.shape
    size = 2 * blocks * block
    half = size // 2
    packed = packed_tables(blocks, block)
    acc = 0.0
    for s in range(1, blocks):
        first = jnp.where(place + s < blocks, mixed, weighted)
        payload = jnp.concatenate([first, taps.reshape(-1, channels)], axis=0)
        pairs = [(i, (i + s) % blocks) for i in range(blocks)]
        got = lax.ppermute(payload, "ctx", pairs)
        table = block_table(packed, (place - s) % blocks)
        got_taps = got[block:].reshape(taps.shape)
        acc = acc + jnp.concatenate(
            [
                jnp.einsum("pr,pf->rf", got[:block], table, precision=precise),
                jnp.dot(got_taps, table, precision=precise),
            ],
            axis=0,
        )
    own_table = block_table(packed, place)
    own = jnp.concatenate([mixed, weighted, back], axis=1)
    loc = jnp.concatenate(
        [
            jnp.einsum("pr,pf->rf", own, own_table, precision=precise),
            jnp.dot(taps, own_table, precision=precise),
        ],
        axis=0,
    )
    c = channels
    mixed_spec = loc[:c] + acc[:c]
    weighted_spec = loc[c : 2 * c] + acc[:c]
    back_spec = loc[2 * c : 3 * c]
    taps_spec = jnp.repeat(loc[3 * c :] + acc[c:], CPF, axis=0)
    conv = packed_products(taps_spec, mixed_spec, False)
    gm = packed_products(taps_spec, weighted_spec, True)
    fgs = packed_products(back_spec, weighted_spec, True)
    fgs = fgs.reshape(-1, CPF, size).sum(axis=1)
    cols = lax.broadcasted_iota(jnp.int32, (1, size), 1)
    weight = jnp.where((cols == 0) | (cols == half), 1.0 / size, 2.0 / size)
    both = jnp.concatenate([conv, gm], axis=0)
    out = jnp.einsum("tf,rf->tr", own_table * weight, both, precision=precise)
    lag = jnp.einsum("rf,tf->rt", fgs, own_table * weight, precision=precise)
    for s in range(1, blocks):
        table = block_table(packed, (place + s) % blocks) * weight
        share = jnp.einsum("rf,tf->rt", fgs, table, precision=precise)
        pairs = [(i, (i + s) % blocks) for i in range(blocks)]
        lag = lag + lax.ppermute(share, "ctx", pairs)
    return out[:, :c], out[:, c:], lag


def chunk_work(local3, common, hsum, tables):
    cw, sw, fwd, inv, inverse, place = tables
    block = local3.shape[-1]
    outer = cw.shape[1]
    own = outer_step(local3, cw, sw, place)
    y = jnp.stack([own[:, 0] + common, own[:, 1] + common, own[:, 2]], axis=1)
    spec = inner_step(y, fwd)
    hspec = jnp.repeat(inner_step(hsum, fwd), CPF, axis=1)
    hr, hi = hspec[..., :block], hspec[..., block:]
    mr, mi = spec[:, 0, :, :block], spec[:, 0, :, block:]
    wr, wi = spec[:, 1, :, :block], spec[:, 1, :, block:]
    br, bi = spec[:, 2, :, :block], spec[:, 2, :, block:]
    conv = jnp.concatenate([hr * mr - hi * mi, hr * mi + hi * mr], axis=-1)
    gm = jnp.concatenate([hr * wr + hi * wi, hr * wi - hi * wr], axis=-1)
    fgs = jnp.concatenate([br * wr + bi * wi, br * wi - bi * wr], axis=-1)
    fgs = fgs.reshape(outer, -1, CPF, 2 * block).sum(axis=2)
    pair = jnp.stack([conv, gm]).transpose(0, 2, 1, 3)
    rows = pair.shape[0] * pair.shape[1]
    both = jnp.dot(pair.reshape(rows, -1), inverse, precision=precise)
    both = both.reshape(2, -1, block)
    z = inner_step(fgs, inv)
    zr, zi = z[..., :block], z[..., block:]
    fg = jnp.stack(
        [jnp.sum(cw[p][:, None] * zr + sw[p][:, None] * zi, axis=0) for p in range(cw.shape[0])]
    )
    return both[0], both[1], fg / (outer * block)


def finish(conv, grad_mixed, lag, filter_scale, query_in, grad_query, key_back, value_back):
    conv = conv * filter_scale
    grad_mixed = grad_mixed * filter_scale
    result = (query_in * conv).astype(jnp.bfloat16)
    next_input = from_behind(result[None], "pipe", 1)
    grad_key = grad_mixed * value_back
    grad_value = grad_mixed * key_back
    grad_stack = jnp.stack([grad_query, grad_key, grad_value], axis=1).astype(jnp.bfloat16)
    prev_grad = from_behind(grad_stack[None], "pipe", -1)
    filter_grad = (lag * filter_scale)[None]
    return (next_input, prev_grad, filter_grad)


def on_device(qkv_in, qkv_saved, conv_saved, out_grad, filters):
    blocks = lax.axis_size("ctx")
    place = lax.axis_index("ctx")
    block = qkv_in.shape[1]
    channels = qkv_in.shape[3]
    groups = filters.shape[1]
    length = blocks * block
    outer = 2 * blocks
    size = outer * block
    filter_scale = (CPF * length) ** (-0.5)

    query_in = qkv_in[0, :, 0].astype(jnp.float32)
    mixed_in = qkv_in[0, :, 1].astype(jnp.float32) * qkv_in[0, :, 2].astype(jnp.float32)
    query_back = qkv_saved[0, :, 0].astype(jnp.float32)
    key_back = qkv_saved[0, :, 1].astype(jnp.float32)
    value_back = qkv_saved[0, :, 2].astype(jnp.float32)
    mixed_back = key_back * value_back
    upstream = out_grad[0].astype(jnp.float32)
    weighted = upstream * query_back
    grad_query = upstream * conv_saved[0]
    taps = filters[0]

    if blocks <= DENSE:
        conv, grad_mixed, lag = dense_path(
            place, blocks, mixed_in, weighted, mixed_back, taps
        )
        return finish(
            conv, grad_mixed, lag, filter_scale, query_in, grad_query, key_back, value_back
        )

    cw, sw = outer_tables(blocks, block, outer)
    fwd, inv = inner_tables(block)

    mixed_rows = mixed_in.T
    weighted_rows = weighted.T
    received = []
    for s in range(1, blocks):
        dest = place + s
        first = jnp.where(dest < blocks, mixed_rows, weighted_rows)
        payload = jnp.concatenate([first, taps], axis=0)
        pairs = [(i, (i + s) % blocks) for i in range(blocks)]
        received.append(lax.ppermute(payload, "ctx", pairs))
    hsum = outer_step(taps, cw, sw, place)
    if blocks <= STEPWISE:
        common = 0.0
        for s, got in enumerate(received, start=1):
            part = outer_step(got, cw, sw, (place - s) % blocks)
            common = common + part[:, :channels]
            hsum = hsum + part[:, channels:]
    else:
        got = jnp.stack(received)
        sources = (place - jnp.arange(1, blocks, dtype=jnp.int32)) % blocks
        weights = jnp.concatenate([cw[sources], sw[sources]], axis=-1)
        both = jnp.concatenate([got, got], axis=-1)
        part = jnp.einsum("sfp,scp->fcp", weights, both, precision=highest)
        common = part[:, :channels]
        hsum = hsum + part[:, channels:]
    local3 = jnp.stack([mixed_rows, weighted_rows, mixed_back.T])

    pos = place * block + jnp.arange(block, dtype=jnp.int32)
    freq = (
        jnp.arange(outer, dtype=jnp.int32)[:, None, None]
        + outer * jnp.arange(block, dtype=jnp.int32)[None, None, :]
    )
    prod = (freq * pos[None, :, None]) % size
    theta = prod.astype(jnp.float32) * (2.0 * math.pi / size)
    inverse = jnp.concatenate([jnp.cos(theta), -jnp.sin(theta)], axis=-1) / size
    inverse = inverse.transpose(0, 2, 1).reshape(outer * 2 * block, block)
    tables = (cw, sw, fwd, inv, inverse, place)

    per_group = 2 * block * outer * 4 * 4 * CPF * blocks
    gchunk = groups
    while gchunk > 1 and gchunk * per_group > CHUNK_BYTES and groups % (gchunk // 2) == 0:
        gchunk //= 2
    nchunk = groups // gchunk
    if nchunk == 1:
        conv, grad_mixed, fg = chunk_work(local3, common, hsum, tables)
    else:
        cc = gchunk * CPF
        ls = local3.reshape(3, nchunk, cc, block).transpose(1, 0, 2, 3)
        cs = common.reshape(outer, nchunk, cc, 2 * block).transpose(1, 0, 2, 3)
        hs = hsum.reshape(outer, nchunk, gchunk, 2 * block).transpose(1, 0, 2, 3)
        conv, grad_mixed, fg = lax.map(lambda a: chunk_work(a[0], a[1], a[2], tables), (ls, cs, hs))
        conv = conv.reshape(channels, block)
        grad_mixed = grad_mixed.reshape(channels, block)
        fg = fg.transpose(1, 0, 2, 3).reshape(blocks, groups, block)

    lag_sum = fg[place]
    for s in range(1, blocks):
        dest = (place + s) % blocks
        pairs = [(i, (i + s) % blocks) for i in range(blocks)]
        lag_sum = lag_sum + lax.ppermute(fg[dest], "ctx", pairs)

    return finish(
        conv.T, grad_mixed.T, lag_sum, filter_scale, query_in, grad_query, key_back, value_back
    )


def solution(mesh):
    return jax.shard_map(
        on_device,
        mesh=mesh,
        in_specs=(
            P("pipe", "ctx", None, None),
            P("pipe", "ctx", None, None),
            P("pipe", "ctx", None),
            P("pipe", "ctx", None),
            P("pipe", None, "ctx"),
        ),
        out_specs=(P("pipe", "ctx", None), P("pipe", "ctx", None, None), P("pipe", None, "ctx")),
        check_vma=False,
    )
```

```python
import math

import numpy as np

import jax
import jax.numpy as jnp
from jax import lax
from jax.sharding import PartitionSpec as P

CPF = 16
CHUNK_BYTES = 36 * 2**20
STEPWISE = 4
DENSE = 4

highest = lax.Precision.HIGHEST
precise = lax.Precision.HIGH


def from_behind(x, axis, by):
    devices = lax.axis_size(axis)
    pairs = [(i, i + by) for i in range(devices) if 0 <= i + by < devices]
    return lax.ppermute(x, axis, pairs)


def inner_tables(block):
    ids = np.arange(block)
    theta = 2.0 * np.pi * ((ids[:, None] * ids[None, :]) % block) / block
    cos, sin = np.cos(theta), np.sin(theta)
    fwd = np.block([[cos, -sin], [sin, cos]])
    inv = np.block([[cos, sin], [-sin, cos]])
    return jnp.asarray(fwd, jnp.float32), jnp.asarray(inv, jnp.float32)


def outer_tables(blocks, block, outer):
    size = outer * block
    pos = np.arange(blocks)[:, None, None] * block + np.arange(block)[None, None, :]
    prod = (pos * np.arange(outer)[None, :, None]) % size
    theta = 2.0 * np.pi * prod / size
    return jnp.asarray(np.cos(theta), jnp.float32), jnp.asarray(-np.sin(theta), jnp.float32)


def outer_step(parts, cw, sw, index):
    c = lax.dynamic_index_in_dim(cw, index, keepdims=False)
    s = lax.dynamic_index_in_dim(sw, index, keepdims=False)
    tail = (1,) * (parts.ndim - 1)
    c = c.reshape(c.shape[:1] + tail + c.shape[1:])
    s = s.reshape(s.shape[:1] + tail + s.shape[1:])
    return jnp.concatenate([c * parts[None], s * parts[None]], axis=-1)


def inner_step(y, mat):
    shape = y.shape
    return jnp.dot(y.reshape(-1, shape[-1]), mat, precision=precise).reshape(shape)


def packed_tables(blocks, block):
    size = 2 * blocks * block
    half = size // 2
    ids = np.arange(block)
    freqs = np.arange(half)
    theta = 2.0 * np.pi * ((ids[:, None] * freqs[None, :]) % size) / size
    phase = 2.0 * np.pi * ((np.arange(blocks)[:, None] * block * freqs[None, :]) % size) / size
    as32 = lambda a: jnp.asarray(a, jnp.float32)
    return as32(np.cos(theta)), as32(np.sin(theta)), as32(np.cos(phase)), as32(np.sin(phase))


def block_table(packed, index):
    base_c, base_s, turn_c, turn_s = packed
    c = lax.dynamic_index_in_dim(turn_c, index, keepdims=True)
    s = lax.dynamic_index_in_dim(turn_s, index, keepdims=True)
    cos = base_c * c - base_s * s
    sin = base_s * c + base_c * s
    block, half = cos.shape
    first = lax.broadcasted_iota(jnp.int32, (block, half), 1) == 0
    sign = 1.0 - 2.0 * (lax.broadcasted_iota(jnp.int32, (block, half), 0) % 2).astype(jnp.float32)
    return jnp.concatenate([cos, jnp.where(first, sign, -sin)], axis=1)


def packed_products(h, a, conj):
    half = h.shape[1] // 2
    hr, hi = h[:, :half], h[:, half:]
    ar, ai = a[:, :half], a[:, half:]
    first = lax.broadcasted_iota(jnp.int32, hr.shape, 1) == 0
    sign = -1.0 if conj else 1.0
    re = hr * ar - sign * jnp.where(first, 0.0, hi * ai)
    im = jnp.where(first, hi * ai, hr * ai + sign * (hi * ar))
    return jnp.concatenate([re, im], axis=1)


def dense_path(place, blocks, mixed_rows, weighted_rows, back_rows, taps):
    channels, block = mixed_rows.shape
    size = 2 * blocks * block
    half = size // 2
    packed = packed_tables(blocks, block)
    cols = lax.broadcasted_iota(jnp.int32, (1, size), 1)
    weight = jnp.where((cols == 0) | (cols == half), 1.0 / size, 2.0 / size)
    acc = 0.0
    share_tables = [None]
    for s in range(1, blocks):
        first = jnp.where(place + s < blocks, mixed_rows, weighted_rows)
        payload = jnp.concatenate([first, taps], axis=0)
        pairs = [(i, (i + s) % blocks) for i in range(blocks)]
        got = lax.ppermute(payload, "ctx", pairs)
        got, share = lax.optimization_barrier(
            (got, block_table(packed, (place + s) % blocks) * weight)
        )
        share_tables.append(share)
        table = block_table(packed, (place - s) % blocks)
        acc = acc + jnp.dot(got, table, precision=precise)
    own_table = block_table(packed, place)
    own = jnp.concatenate([mixed_rows, weighted_rows, back_rows, taps], axis=0)
    loc = jnp.dot(own, own_table, precision=precise)
    c = channels
    mixed_spec = loc[:c] + acc[:c]
    weighted_spec = loc[c : 2 * c] + acc[:c]
    back_spec = loc[2 * c : 3 * c]
    taps_spec = jnp.repeat(loc[3 * c :] + acc[c:], CPF, axis=0)
    conv = packed_products(taps_spec, mixed_spec, False)
    gm = packed_products(taps_spec, weighted_spec, True)
    fgs = packed_products(back_spec, weighted_spec, True)
    fgs = fgs.reshape(-1, CPF, size).sum(axis=1)
    both = jnp.concatenate([conv, gm], axis=0)
    out = jnp.einsum("tf,rf->tr", own_table * weight, both, precision=precise)
    lag = jnp.einsum("rf,tf->rt", fgs, own_table * weight, precision=precise)
    for s in range(1, blocks):
        share = jnp.einsum("rf,tf->rt", fgs, share_tables[s], precision=precise)
        pairs = [(i, (i + s) % blocks) for i in range(blocks)]
        lag = lag + lax.ppermute(share, "ctx", pairs)
    return out[:, :c], out[:, c:], lag


def chunk_work(local3, common, hsum, tables):
    cw, sw, fwd, inv, inverse, place = tables
    block = local3.shape[-1]
    outer = cw.shape[1]
    own = outer_step(local3, cw, sw, place)
    y = jnp.stack([own[:, 0] + common, own[:, 1] + common, own[:, 2]], axis=1)
    spec = inner_step(y, fwd)
    hspec = jnp.repeat(inner_step(hsum, fwd), CPF, axis=1)
    hr, hi = hspec[..., :block], hspec[..., block:]
    mr, mi = spec[:, 0, :, :block], spec[:, 0, :, block:]
    wr, wi = spec[:, 1, :, :block], spec[:, 1, :, block:]
    br, bi = spec[:, 2, :, :block], spec[:, 2, :, block:]
    conv = jnp.concatenate([hr * mr - hi * mi, hr * mi + hi * mr], axis=-1)
    gm = jnp.concatenate([hr * wr + hi * wi, hr * wi - hi * wr], axis=-1)
    fgs = jnp.concatenate([br * wr + bi * wi, br * wi - bi * wr], axis=-1)
    fgs = fgs.reshape(outer, -1, CPF, 2 * block).sum(axis=2)
    pair = jnp.stack([conv, gm]).transpose(0, 2, 1, 3)
    rows = pair.shape[0] * pair.shape[1]
    both = jnp.dot(pair.reshape(rows, -1), inverse, precision=precise)
    both = both.reshape(2, -1, block)
    z = inner_step(fgs, inv)
    zr, zi = z[..., :block], z[..., block:]
    fg = jnp.stack(
        [jnp.sum(cw[p][:, None] * zr + sw[p][:, None] * zi, axis=0) for p in range(cw.shape[0])]
    )
    return both[0], both[1], fg / (outer * block)


def finish(conv, grad_mixed, lag, filter_scale, query_in, grad_query, key_back, value_back):
    conv = conv * filter_scale
    grad_mixed = grad_mixed * filter_scale
    result = (query_in * conv).astype(jnp.bfloat16)
    next_input = from_behind(result[None], "pipe", 1)
    grad_key = grad_mixed * value_back
    grad_value = grad_mixed * key_back
    grad_stack = jnp.stack([grad_query, grad_key, grad_value], axis=1).astype(jnp.bfloat16)
    prev_grad = from_behind(grad_stack[None], "pipe", -1)
    filter_grad = (lag * filter_scale)[None]
    return (next_input, prev_grad, filter_grad)


def on_device(qkv_in, qkv_saved, conv_saved, out_grad, filters):
    blocks = lax.axis_size("ctx")
    place = lax.axis_index("ctx")
    block = qkv_in.shape[1]
    channels = qkv_in.shape[3]
    groups = filters.shape[1]
    length = blocks * block
    outer = 2 * blocks
    size = outer * block
    filter_scale = (CPF * length) ** (-0.5)

    query_in = qkv_in[0, :, 0].astype(jnp.float32)
    mixed_in = qkv_in[0, :, 1].astype(jnp.float32) * qkv_in[0, :, 2].astype(jnp.float32)
    query_back = qkv_saved[0, :, 0].astype(jnp.float32)
    key_back = qkv_saved[0, :, 1].astype(jnp.float32)
    value_back = qkv_saved[0, :, 2].astype(jnp.float32)
    mixed_back = key_back * value_back
    upstream = out_grad[0].astype(jnp.float32)
    weighted = upstream * query_back
    grad_query = upstream * conv_saved[0]
    taps = filters[0]

    if blocks <= DENSE:
        conv, grad_mixed, lag = dense_path(
            place, blocks, mixed_in.T, weighted.T, mixed_back.T, taps
        )
        return finish(
            conv, grad_mixed, lag, filter_scale, query_in, grad_query, key_back, value_back
        )

    cw, sw = outer_tables(blocks, block, outer)
    fwd, inv = inner_tables(block)

    mixed_rows = mixed_in.T
    weighted_rows = weighted.T
    received = []
    for s in range(1, blocks):
        dest = place + s
        first = jnp.where(dest < blocks, mixed_rows, weighted_rows)
        payload = jnp.concatenate([first, taps], axis=0)
        pairs = [(i, (i + s) % blocks) for i in range(blocks)]
        received.append(lax.ppermute(payload, "ctx", pairs))
    hsum = outer_step(taps, cw, sw, place)
    if blocks <= STEPWISE:
        common = 0.0
        for s, got in enumerate(received, start=1):
            part = outer_step(got, cw, sw, (place - s) % blocks)
            common = common + part[:, :channels]
            hsum = hsum + part[:, channels:]
    else:
        got = jnp.stack(received)
        sources = (place - jnp.arange(1, blocks, dtype=jnp.int32)) % blocks
        weights = jnp.concatenate([cw[sources], sw[sources]], axis=-1)
        both = jnp.concatenate([got, got], axis=-1)
        part = jnp.einsum("sfp,scp->fcp", weights, both, precision=highest)
        common = part[:, :channels]
        hsum = hsum + part[:, channels:]
    local3 = jnp.stack([mixed_rows, weighted_rows, mixed_back.T])

    pos = place * block + jnp.arange(block, dtype=jnp.int32)
    freq = (
        jnp.arange(outer, dtype=jnp.int32)[:, None, None]
        + outer * jnp.arange(block, dtype=jnp.int32)[None, None, :]
    )
    prod = (freq * pos[None, :, None]) % size
    theta = prod.astype(jnp.float32) * (2.0 * math.pi / size)
    inverse = jnp.concatenate([jnp.cos(theta), -jnp.sin(theta)], axis=-1) / size
    inverse = inverse.transpose(0, 2, 1).reshape(outer * 2 * block, block)
    tables = (cw, sw, fwd, inv, inverse, place)

    per_group = 2 * block * outer * 4 * 4 * CPF * blocks
    gchunk = groups
    while gchunk > 1 and gchunk * per_group > CHUNK_BYTES and groups % (gchunk // 2) == 0:
        gchunk //= 2
    nchunk = groups // gchunk
    if nchunk == 1:
        conv, grad_mixed, fg = chunk_work(local3, common, hsum, tables)
    else:
        cc = gchunk * CPF
        ls = local3.reshape(3, nchunk, cc, block).transpose(1, 0, 2, 3)
        cs = common.reshape(outer, nchunk, cc, 2 * block).transpose(1, 0, 2, 3)
        hs = hsum.reshape(outer, nchunk, gchunk, 2 * block).transpose(1, 0, 2, 3)
        conv, grad_mixed, fg = lax.map(lambda a: chunk_work(a[0], a[1], a[2], tables), (ls, cs, hs))
        conv = conv.reshape(channels, block)
        grad_mixed = grad_mixed.reshape(channels, block)
        fg = fg.transpose(1, 0, 2, 3).reshape(blocks, groups, block)

    lag_sum = fg[place]
    for s in range(1, blocks):
        dest = (place + s) % blocks
        pairs = [(i, (i + s) % blocks) for i in range(blocks)]
        lag_sum = lag_sum + lax.ppermute(fg[dest], "ctx", pairs)

    return finish(
        conv.T, grad_mixed.T, lag_sum, filter_scale, query_in, grad_query, key_back, value_back
    )


def solution(mesh):
    return jax.shard_map(
        on_device,
        mesh=mesh,
        in_specs=(
            P("pipe", "ctx", None, None),
            P("pipe", "ctx", None, None),
            P("pipe", "ctx", None),
            P("pipe", "ctx", None),
            P("pipe", None, "ctx"),
        ),
        out_specs=(P("pipe", "ctx", None), P("pipe", "ctx", None, None), P("pipe", None, "ctx")),
        check_vma=False,
    )
```

```python
import math

import numpy as np

import jax
import jax.numpy as jnp
from jax import lax
from jax.sharding import PartitionSpec as P

CPF = 16
CHUNK_BYTES = 36 * 2**20
STEPWISE = 4
DENSE = 4

highest = lax.Precision.HIGHEST
precise = lax.Precision.HIGH


def from_behind(x, axis, by):
    devices = lax.axis_size(axis)
    pairs = [(i, i + by) for i in range(devices) if 0 <= i + by < devices]
    return lax.ppermute(x, axis, pairs)


def inner_tables(block):
    ids = np.arange(block)
    theta = 2.0 * np.pi * ((ids[:, None] * ids[None, :]) % block) / block
    cos, sin = np.cos(theta), np.sin(theta)
    fwd = np.block([[cos, -sin], [sin, cos]])
    inv = np.block([[cos, sin], [-sin, cos]])
    return jnp.asarray(fwd, jnp.float32), jnp.asarray(inv, jnp.float32)


def outer_tables(blocks, block, outer):
    size = outer * block
    pos = np.arange(blocks)[:, None, None] * block + np.arange(block)[None, None, :]
    prod = (pos * np.arange(outer)[None, :, None]) % size
    theta = 2.0 * np.pi * prod / size
    return jnp.asarray(np.cos(theta), jnp.float32), jnp.asarray(-np.sin(theta), jnp.float32)


def outer_step(parts, cw, sw, index):
    c = lax.dynamic_index_in_dim(cw, index, keepdims=False)
    s = lax.dynamic_index_in_dim(sw, index, keepdims=False)
    tail = (1,) * (parts.ndim - 1)
    c = c.reshape(c.shape[:1] + tail + c.shape[1:])
    s = s.reshape(s.shape[:1] + tail + s.shape[1:])
    return jnp.concatenate([c * parts[None], s * parts[None]], axis=-1)


def inner_step(y, mat):
    shape = y.shape
    return jnp.dot(y.reshape(-1, shape[-1]), mat, precision=precise).reshape(shape)


def packed_tables(blocks, block):
    size = 2 * blocks * block
    half = size // 2
    ids = np.arange(block)
    freqs = np.arange(half)
    theta = 2.0 * np.pi * ((ids[:, None] * freqs[None, :]) % size) / size
    phase = 2.0 * np.pi * ((np.arange(blocks)[:, None] * block * freqs[None, :]) % size) / size
    as32 = lambda a: jnp.asarray(a, jnp.float32)
    return as32(np.cos(theta)), as32(np.sin(theta)), as32(np.cos(phase)), as32(np.sin(phase))


def block_table(packed, index):
    base_c, base_s, turn_c, turn_s = packed
    c = lax.dynamic_index_in_dim(turn_c, index, keepdims=True)
    s = lax.dynamic_index_in_dim(turn_s, index, keepdims=True)
    cos = base_c * c - base_s * s
    sin = base_s * c + base_c * s
    block, half = cos.shape
    first = lax.broadcasted_iota(jnp.int32, (block, half), 1) == 0
    sign = 1.0 - 2.0 * (lax.broadcasted_iota(jnp.int32, (block, half), 0) % 2).astype(jnp.float32)
    return jnp.concatenate([cos, jnp.where(first, sign, -sin)], axis=1)


def packed_products(h, a, conj):
    half = h.shape[1] // 2
    hr, hi = h[:, :half], h[:, half:]
    ar, ai = a[:, :half], a[:, half:]
    first = lax.broadcasted_iota(jnp.int32, hr.shape, 1) == 0
    sign = -1.0 if conj else 1.0
    re = hr * ar - sign * jnp.where(first, 0.0, hi * ai)
    im = jnp.where(first, hi * ai, hr * ai + sign * (hi * ar))
    return jnp.concatenate([re, im], axis=1)


def dense_path(place, blocks, mixed_rows, weighted_rows, back_rows, taps, ahead, behind):
    channels, block = mixed_rows.shape
    size = 2 * blocks * block
    half = size // 2
    packed = packed_tables(blocks, block)
    all_taps = lax.all_gather(taps, "ctx")
    acc = 0.0
    for s in range(1, blocks):
        payload = jnp.where(place + s < blocks, ahead, behind)
        pairs = [(i, (i + s) % blocks) for i in range(blocks)]
        got = lax.ppermute(payload, "ctx", pairs)
        product = got[:, 0].astype(jnp.float32) * got[:, 1].astype(jnp.float32)
        table = block_table(packed, (place - s) % blocks)
        acc = acc + jnp.einsum("pr,pf->rf", product, table, precision=precise)
    own_table = block_table(packed, place)
    own = jnp.concatenate([mixed_rows, weighted_rows, back_rows], axis=0)
    loc = jnp.dot(own, own_table, precision=precise)
    taps_spec = 0.0
    for b in range(blocks):
        taps_spec = taps_spec + jnp.dot(all_taps[b], block_table(packed, b), precision=precise)
    c = channels
    mixed_spec = loc[:c] + acc
    weighted_spec = loc[c : 2 * c] + acc
    back_spec = loc[2 * c : 3 * c]
    taps_spec = jnp.repeat(taps_spec, CPF, axis=0)
    conv = packed_products(taps_spec, mixed_spec, False)
    gm = packed_products(taps_spec, weighted_spec, True)
    fgs = packed_products(back_spec, weighted_spec, True)
    fgs = fgs.reshape(-1, CPF, size).sum(axis=1)
    cols = lax.broadcasted_iota(jnp.int32, (1, size), 1)
    weight = jnp.where((cols == 0) | (cols == half), 1.0 / size, 2.0 / size)
    both = jnp.concatenate([conv, gm], axis=0)
    out = jnp.einsum("tf,rf->tr", own_table * weight, both, precision=precise)
    lag = jnp.einsum("rf,tf->rt", fgs, own_table * weight, precision=precise)
    for s in range(1, blocks):
        table = block_table(packed, (place + s) % blocks) * weight
        share = jnp.einsum("rf,tf->rt", fgs, table, precision=precise)
        pairs = [(i, (i + s) % blocks) for i in range(blocks)]
        lag = lag + lax.ppermute(share, "ctx", pairs)
    return out[:, :c], out[:, c:], lag


def chunk_work(local3, common, hsum, tables):
    cw, sw, fwd, inv, inverse, place = tables
    block = local3.shape[-1]
    outer = cw.shape[1]
    own = outer_step(local3, cw, sw, place)
    y = jnp.stack([own[:, 0] + common, own[:, 1] + common, own[:, 2]], axis=1)
    spec = inner_step(y, fwd)
    hspec = jnp.repeat(inner_step(hsum, fwd), CPF, axis=1)
    hr, hi = hspec[..., :block], hspec[..., block:]
    mr, mi = spec[:, 0, :, :block], spec[:, 0, :, block:]
    wr, wi = spec[:, 1, :, :block], spec[:, 1, :, block:]
    br, bi = spec[:, 2, :, :block], spec[:, 2, :, block:]
    conv = jnp.concatenate([hr * mr - hi * mi, hr * mi + hi * mr], axis=-1)
    gm = jnp.concatenate([hr * wr + hi * wi, hr * wi - hi * wr], axis=-1)
    fgs = jnp.concatenate([br * wr + bi * wi, br * wi - bi * wr], axis=-1)
    fgs = fgs.reshape(outer, -1, CPF, 2 * block).sum(axis=2)
    pair = jnp.stack([conv, gm]).transpose(0, 2, 1, 3)
    rows = pair.shape[0] * pair.shape[1]
    both = jnp.dot(pair.reshape(rows, -1), inverse, precision=precise)
    both = both.reshape(2, -1, block)
    z = inner_step(fgs, inv)
    zr, zi = z[..., :block], z[..., block:]
    fg = jnp.stack(
        [jnp.sum(cw[p][:, None] * zr + sw[p][:, None] * zi, axis=0) for p in range(cw.shape[0])]
    )
    return both[0], both[1], fg / (outer * block)


def finish(conv, grad_mixed, lag, filter_scale, query_in, grad_query, key_back, value_back):
    conv = conv * filter_scale
    grad_mixed = grad_mixed * filter_scale
    result = (query_in * conv).astype(jnp.bfloat16)
    next_input = from_behind(result[None], "pipe", 1)
    grad_key = grad_mixed * value_back
    grad_value = grad_mixed * key_back
    grad_stack = jnp.stack([grad_query, grad_key, grad_value], axis=1).astype(jnp.bfloat16)
    prev_grad = from_behind(grad_stack[None], "pipe", -1)
    filter_grad = (lag * filter_scale)[None]
    return (next_input, prev_grad, filter_grad)


def on_device(qkv_in, qkv_saved, conv_saved, out_grad, filters):
    blocks = lax.axis_size("ctx")
    place = lax.axis_index("ctx")
    block = qkv_in.shape[1]
    channels = qkv_in.shape[3]
    groups = filters.shape[1]
    length = blocks * block
    outer = 2 * blocks
    size = outer * block
    filter_scale = (CPF * length) ** (-0.5)

    query_in = qkv_in[0, :, 0].astype(jnp.float32)
    mixed_in = qkv_in[0, :, 1].astype(jnp.float32) * qkv_in[0, :, 2].astype(jnp.float32)
    query_back = qkv_saved[0, :, 0].astype(jnp.float32)
    key_back = qkv_saved[0, :, 1].astype(jnp.float32)
    value_back = qkv_saved[0, :, 2].astype(jnp.float32)
    mixed_back = key_back * value_back
    upstream = out_grad[0].astype(jnp.float32)
    weighted = upstream * query_back
    grad_query = upstream * conv_saved[0]
    taps = filters[0]

    if blocks <= DENSE:
        conv, grad_mixed, lag = dense_path(
            place,
            blocks,
            mixed_in.T,
            weighted.T,
            mixed_back.T,
            taps,
            qkv_in[0, :, 1:3],
            jnp.stack([out_grad[0], qkv_saved[0, :, 0]], axis=1),
        )
        return finish(
            conv, grad_mixed, lag, filter_scale, query_in, grad_query, key_back, value_back
        )

    cw, sw = outer_tables(blocks, block, outer)
    fwd, inv = inner_tables(block)

    mixed_rows = mixed_in.T
    weighted_rows = weighted.T
    received = []
    for s in range(1, blocks):
        dest = place + s
        first = jnp.where(dest < blocks, mixed_rows, weighted_rows)
        payload = jnp.concatenate([first, taps], axis=0)
        pairs = [(i, (i + s) % blocks) for i in range(blocks)]
        received.append(lax.ppermute(payload, "ctx", pairs))
    hsum = outer_step(taps, cw, sw, place)
    if blocks <= STEPWISE:
        common = 0.0
        for s, got in enumerate(received, start=1):
            part = outer_step(got, cw, sw, (place - s) % blocks)
            common = common + part[:, :channels]
            hsum = hsum + part[:, channels:]
    else:
        got = jnp.stack(received)
        sources = (place - jnp.arange(1, blocks, dtype=jnp.int32)) % blocks
        weights = jnp.concatenate([cw[sources], sw[sources]], axis=-1)
        both = jnp.concatenate([got, got], axis=-1)
        part = jnp.einsum("sfp,scp->fcp", weights, both, precision=highest)
        common = part[:, :channels]
        hsum = hsum + part[:, channels:]
    local3 = jnp.stack([mixed_rows, weighted_rows, mixed_back.T])

    pos = place * block + jnp.arange(block, dtype=jnp.int32)
    freq = (
        jnp.arange(outer, dtype=jnp.int32)[:, None, None]
        + outer * jnp.arange(block, dtype=jnp.int32)[None, None, :]
    )
    prod = (freq * pos[None, :, None]) % size
    theta = prod.astype(jnp.float32) * (2.0 * math.pi / size)
    inverse = jnp.concatenate([jnp.cos(theta), -jnp.sin(theta)], axis=-1) / size
    inverse = inverse.transpose(0, 2, 1).reshape(outer * 2 * block, block)
    tables = (cw, sw, fwd, inv, inverse, place)

    per_group = 2 * block * outer * 4 * 4 * CPF * blocks
    gchunk = groups
    while gchunk > 1 and gchunk * per_group > CHUNK_BYTES and groups % (gchunk // 2) == 0:
        gchunk //= 2
    nchunk = groups // gchunk
    if nchunk == 1:
        conv, grad_mixed, fg = chunk_work(local3, common, hsum, tables)
    else:
        cc = gchunk * CPF
        ls = local3.reshape(3, nchunk, cc, block).transpose(1, 0, 2, 3)
        cs = common.reshape(outer, nchunk, cc, 2 * block).transpose(1, 0, 2, 3)
        hs = hsum.reshape(outer, nchunk, gchunk, 2 * block).transpose(1, 0, 2, 3)
        conv, grad_mixed, fg = lax.map(lambda a: chunk_work(a[0], a[1], a[2], tables), (ls, cs, hs))
        conv = conv.reshape(channels, block)
        grad_mixed = grad_mixed.reshape(channels, block)
        fg = fg.transpose(1, 0, 2, 3).reshape(blocks, groups, block)

    lag_sum = fg[place]
    for s in range(1, blocks):
        dest = (place + s) % blocks
        pairs = [(i, (i + s) % blocks) for i in range(blocks)]
        lag_sum = lag_sum + lax.ppermute(fg[dest], "ctx", pairs)

    return finish(
        conv.T, grad_mixed.T, lag_sum, filter_scale, query_in, grad_query, key_back, value_back
    )


def solution(mesh):
    return jax.shard_map(
        on_device,
        mesh=mesh,
        in_specs=(
            P("pipe", "ctx", None, None),
            P("pipe", "ctx", None, None),
            P("pipe", "ctx", None),
            P("pipe", "ctx", None),
            P("pipe", None, "ctx"),
        ),
        out_specs=(P("pipe", "ctx", None), P("pipe", "ctx", None, None), P("pipe", None, "ctx")),
        check_vma=False,
    )
```

```python
import math

import numpy as np

import jax
import jax.numpy as jnp
from jax import lax
from jax.sharding import PartitionSpec as P

CPF = 16
CHUNK_BYTES = 36 * 2**20
STEPWISE = 4
DENSE = 4

highest = lax.Precision.HIGHEST
precise = lax.Precision.HIGH


def from_behind(x, axis, by):
    devices = lax.axis_size(axis)
    pairs = [(i, i + by) for i in range(devices) if 0 <= i + by < devices]
    return lax.ppermute(x, axis, pairs)


def inner_tables(block):
    ids = np.arange(block)
    theta = 2.0 * np.pi * ((ids[:, None] * ids[None, :]) % block) / block
    cos, sin = np.cos(theta), np.sin(theta)
    fwd = np.block([[cos, -sin], [sin, cos]])
    inv = np.block([[cos, sin], [-sin, cos]])
    return jnp.asarray(fwd, jnp.float32), jnp.asarray(inv, jnp.float32)


def outer_tables(blocks, block, outer):
    size = outer * block
    pos = np.arange(blocks)[:, None, None] * block + np.arange(block)[None, None, :]
    prod = (pos * np.arange(outer)[None, :, None]) % size
    theta = 2.0 * np.pi * prod / size
    return jnp.asarray(np.cos(theta), jnp.float32), jnp.asarray(-np.sin(theta), jnp.float32)


def outer_step(parts, cw, sw, index):
    c = lax.dynamic_index_in_dim(cw, index, keepdims=False)
    s = lax.dynamic_index_in_dim(sw, index, keepdims=False)
    tail = (1,) * (parts.ndim - 1)
    c = c.reshape(c.shape[:1] + tail + c.shape[1:])
    s = s.reshape(s.shape[:1] + tail + s.shape[1:])
    return jnp.concatenate([c * parts[None], s * parts[None]], axis=-1)


def inner_step(y, mat):
    shape = y.shape
    return jnp.dot(y.reshape(-1, shape[-1]), mat, precision=precise).reshape(shape)


def packed_tables(blocks, block):
    size = 2 * blocks * block
    half = size // 2
    ids = np.arange(block)
    freqs = np.arange(half)
    theta = 2.0 * np.pi * ((ids[:, None] * freqs[None, :]) % size) / size
    phase = 2.0 * np.pi * ((np.arange(blocks)[:, None] * block * freqs[None, :]) % size) / size
    as32 = lambda a: jnp.asarray(a, jnp.float32)
    return as32(np.cos(theta)), as32(np.sin(theta)), as32(np.cos(phase)), as32(np.sin(phase))


def block_table(packed, index):
    base_c, base_s, turn_c, turn_s = packed
    c = lax.dynamic_index_in_dim(turn_c, index, keepdims=True)
    s = lax.dynamic_index_in_dim(turn_s, index, keepdims=True)
    cos = base_c * c - base_s * s
    sin = base_s * c + base_c * s
    block, half = cos.shape
    first = lax.broadcasted_iota(jnp.int32, (block, half), 1) == 0
    sign = 1.0 - 2.0 * (lax.broadcasted_iota(jnp.int32, (block, half), 0) % 2).astype(jnp.float32)
    return jnp.concatenate([cos, jnp.where(first, sign, -sin)], axis=1)


def packed_products(h, a, conj):
    half = h.shape[1] // 2
    hr, hi = h[:, :half], h[:, half:]
    ar, ai = a[:, :half], a[:, half:]
    first = lax.broadcasted_iota(jnp.int32, hr.shape, 1) == 0
    sign = -1.0 if conj else 1.0
    re = hr * ar - sign * jnp.where(first, 0.0, hi * ai)
    im = jnp.where(first, hi * ai, hr * ai + sign * (hi * ar))
    return jnp.concatenate([re, im], axis=1)


def dense_path(place, blocks, mixed_rows, weighted_rows, back_rows, taps):
    channels, block = mixed_rows.shape
    size = 2 * blocks * block
    half = size // 2
    packed = packed_tables(blocks, block)
    acc = 0.0
    for s in range(1, blocks):
        first = jnp.where(place + s < blocks, mixed_rows, weighted_rows)
        payload = jnp.concatenate([first, taps], axis=0)
        pairs = [(i, (i + s) % blocks) for i in range(blocks)]
        got = lax.ppermute(payload, "ctx", pairs)
        table = block_table(packed, (place - s) % blocks)
        acc = acc + jnp.dot(got, table, precision=precise)
    own_table = block_table(packed, place)
    own = jnp.concatenate([mixed_rows, weighted_rows, back_rows, taps], axis=0)
    loc = jnp.dot(own, own_table, precision=precise)
    c = channels
    mixed_spec = loc[:c] + acc[:c]
    weighted_spec = loc[c : 2 * c] + acc[:c]
    back_spec = loc[2 * c : 3 * c]
    taps_spec = jnp.repeat(loc[3 * c :] + acc[c:], CPF, axis=0)
    conv = packed_products(taps_spec, mixed_spec, False)
    gm = packed_products(taps_spec, weighted_spec, True)
    fgs = packed_products(back_spec, weighted_spec, True)
    fgs = fgs.reshape(-1, CPF, size).sum(axis=1)
    cols = lax.broadcasted_iota(jnp.int32, (1, size), 1)
    weight = jnp.where((cols == 0) | (cols == half), 1.0 / size, 2.0 / size)
    both = jnp.concatenate([conv, gm], axis=0)
    out = jnp.einsum("tf,rf->tr", own_table * weight, both, precision=precise)
    lag = jnp.einsum("rf,tf->rt", fgs, own_table * weight, precision=precise)
    for s in range(1, blocks):
        table = block_table(packed, (place + s) % blocks) * weight
        share = jnp.einsum("rf,tf->rt", fgs, table, precision=precise)
        pairs = [(i, (i + s) % blocks) for i in range(blocks) if i + (i + s) % blocks < blocks]
        lag = lag + lax.ppermute(share, "ctx", pairs)
    return out[:, :c], out[:, c:], lag


def chunk_work(local3, common, hsum, tables):
    cw, sw, fwd, inv, inverse, place = tables
    block = local3.shape[-1]
    outer = cw.shape[1]
    own = outer_step(local3, cw, sw, place)
    y = jnp.stack([own[:, 0] + common, own[:, 1] + common, own[:, 2]], axis=1)
    spec = inner_step(y, fwd)
    hspec = jnp.repeat(inner_step(hsum, fwd), CPF, axis=1)
    hr, hi = hspec[..., :block], hspec[..., block:]
    mr, mi = spec[:, 0, :, :block], spec[:, 0, :, block:]
    wr, wi = spec[:, 1, :, :block], spec[:, 1, :, block:]
    br, bi = spec[:, 2, :, :block], spec[:, 2, :, block:]
    conv = jnp.concatenate([hr * mr - hi * mi, hr * mi + hi * mr], axis=-1)
    gm = jnp.concatenate([hr * wr + hi * wi, hr * wi - hi * wr], axis=-1)
    fgs = jnp.concatenate([br * wr + bi * wi, br * wi - bi * wr], axis=-1)
    fgs = fgs.reshape(outer, -1, CPF, 2 * block).sum(axis=2)
    pair = jnp.stack([conv, gm]).transpose(0, 2, 1, 3)
    rows = pair.shape[0] * pair.shape[1]
    both = jnp.dot(pair.reshape(rows, -1), inverse, precision=precise)
    both = both.reshape(2, -1, block)
    z = inner_step(fgs, inv)
    zr, zi = z[..., :block], z[..., block:]
    fg = jnp.stack(
        [jnp.sum(cw[p][:, None] * zr + sw[p][:, None] * zi, axis=0) for p in range(cw.shape[0])]
    )
    return both[0], both[1], fg / (outer * block)


def finish(conv, grad_mixed, lag, filter_scale, query_in, grad_query, key_back, value_back):
    conv = conv * filter_scale
    grad_mixed = grad_mixed * filter_scale
    result = (query_in * conv).astype(jnp.bfloat16)
    next_input = from_behind(result[None], "pipe", 1)
    grad_key = grad_mixed * value_back
    grad_value = grad_mixed * key_back
    grad_stack = jnp.stack([grad_query, grad_key, grad_value], axis=1).astype(jnp.bfloat16)
    prev_grad = from_behind(grad_stack[None], "pipe", -1)
    filter_grad = (lag * filter_scale)[None]
    return (next_input, prev_grad, filter_grad)


def on_device(qkv_in, qkv_saved, conv_saved, out_grad, filters):
    blocks = lax.axis_size("ctx")
    place = lax.axis_index("ctx")
    block = qkv_in.shape[1]
    channels = qkv_in.shape[3]
    groups = filters.shape[1]
    length = blocks * block
    outer = 2 * blocks
    size = outer * block
    filter_scale = (CPF * length) ** (-0.5)

    query_in = qkv_in[0, :, 0].astype(jnp.float32)
    mixed_in = qkv_in[0, :, 1].astype(jnp.float32) * qkv_in[0, :, 2].astype(jnp.float32)
    query_back = qkv_saved[0, :, 0].astype(jnp.float32)
    key_back = qkv_saved[0, :, 1].astype(jnp.float32)
    value_back = qkv_saved[0, :, 2].astype(jnp.float32)
    mixed_back = key_back * value_back
    upstream = out_grad[0].astype(jnp.float32)
    weighted = upstream * query_back
    grad_query = upstream * conv_saved[0]
    taps = filters[0]

    if blocks <= DENSE:
        conv, grad_mixed, lag = dense_path(
            place, blocks, mixed_in.T, weighted.T, mixed_back.T, taps
        )
        return finish(
            conv, grad_mixed, lag, filter_scale, query_in, grad_query, key_back, value_back
        )

    cw, sw = outer_tables(blocks, block, outer)
    fwd, inv = inner_tables(block)

    mixed_rows = mixed_in.T
    weighted_rows = weighted.T
    received = []
    for s in range(1, blocks):
        dest = place + s
        first = jnp.where(dest < blocks, mixed_rows, weighted_rows)
        payload = jnp.concatenate([first, taps], axis=0)
        pairs = [(i, (i + s) % blocks) for i in range(blocks)]
        received.append(lax.ppermute(payload, "ctx", pairs))
    hsum = outer_step(taps, cw, sw, place)
    if blocks <= STEPWISE:
        common = 0.0
        for s, got in enumerate(received, start=1):
            part = outer_step(got, cw, sw, (place - s) % blocks)
            common = common + part[:, :channels]
            hsum = hsum + part[:, channels:]
    else:
        got = jnp.stack(received)
        sources = (place - jnp.arange(1, blocks, dtype=jnp.int32)) % blocks
        weights = jnp.concatenate([cw[sources], sw[sources]], axis=-1)
        both = jnp.concatenate([got, got], axis=-1)
        part = jnp.einsum("sfp,scp->fcp", weights, both, precision=highest)
        common = part[:, :channels]
        hsum = hsum + part[:, channels:]
    local3 = jnp.stack([mixed_rows, weighted_rows, mixed_back.T])

    pos = place * block + jnp.arange(block, dtype=jnp.int32)
    freq = (
        jnp.arange(outer, dtype=jnp.int32)[:, None, None]
        + outer * jnp.arange(block, dtype=jnp.int32)[None, None, :]
    )
    prod = (freq * pos[None, :, None]) % size
    theta = prod.astype(jnp.float32) * (2.0 * math.pi / size)
    inverse = jnp.concatenate([jnp.cos(theta), -jnp.sin(theta)], axis=-1) / size
    inverse = inverse.transpose(0, 2, 1).reshape(outer * 2 * block, block)
    tables = (cw, sw, fwd, inv, inverse, place)

    per_group = 2 * block * outer * 4 * 4 * CPF * blocks
    gchunk = groups
    while gchunk > 1 and gchunk * per_group > CHUNK_BYTES and groups % (gchunk // 2) == 0:
        gchunk //= 2
    nchunk = groups // gchunk
    if nchunk == 1:
        conv, grad_mixed, fg = chunk_work(local3, common, hsum, tables)
    else:
        cc = gchunk * CPF
        ls = local3.reshape(3, nchunk, cc, block).transpose(1, 0, 2, 3)
        cs = common.reshape(outer, nchunk, cc, 2 * block).transpose(1, 0, 2, 3)
        hs = hsum.reshape(outer, nchunk, gchunk, 2 * block).transpose(1, 0, 2, 3)
        conv, grad_mixed, fg = lax.map(lambda a: chunk_work(a[0], a[1], a[2], tables), (ls, cs, hs))
        conv = conv.reshape(channels, block)
        grad_mixed = grad_mixed.reshape(channels, block)
        fg = fg.transpose(1, 0, 2, 3).reshape(blocks, groups, block)

    lag_sum = fg[place]
    for s in range(1, blocks):
        dest = (place + s) % blocks
        pairs = [(i, (i + s) % blocks) for i in range(blocks)]
        lag_sum = lag_sum + lax.ppermute(fg[dest], "ctx", pairs)

    return finish(
        conv.T, grad_mixed.T, lag_sum, filter_scale, query_in, grad_query, key_back, value_back
    )


def solution(mesh):
    return jax.shard_map(
        on_device,
        mesh=mesh,
        in_specs=(
            P("pipe", "ctx", None, None),
            P("pipe", "ctx", None, None),
            P("pipe", "ctx", None),
            P("pipe", "ctx", None),
            P("pipe", None, "ctx"),
        ),
        out_specs=(P("pipe", "ctx", None), P("pipe", "ctx", None, None), P("pipe", None, "ctx")),
        check_vma=False,
    )
```

```python
import math

import numpy as np

import jax
import jax.numpy as jnp
from jax import lax
from jax.sharding import PartitionSpec as P

CPF = 16
CHUNK_BYTES = 36 * 2**20
STEPWISE = 4
DENSE = 4

highest = lax.Precision.HIGHEST
precise = lax.Precision.HIGH


def from_behind(x, axis, by):
    devices = lax.axis_size(axis)
    pairs = [(i, (i + by) % devices) for i in range(devices)]
    got = lax.ppermute(x, axis, pairs)
    source = lax.axis_index(axis) - by
    return jnp.where((source >= 0) & (source < devices), got, jnp.zeros_like(got))


def inner_tables(block):
    ids = np.arange(block)
    theta = 2.0 * np.pi * ((ids[:, None] * ids[None, :]) % block) / block
    cos, sin = np.cos(theta), np.sin(theta)
    fwd = np.block([[cos, -sin], [sin, cos]])
    inv = np.block([[cos, sin], [-sin, cos]])
    return jnp.asarray(fwd, jnp.float32), jnp.asarray(inv, jnp.float32)


def outer_tables(blocks, block, outer):
    size = outer * block
    pos = np.arange(blocks)[:, None, None] * block + np.arange(block)[None, None, :]
    prod = (pos * np.arange(outer)[None, :, None]) % size
    theta = 2.0 * np.pi * prod / size
    return jnp.asarray(np.cos(theta), jnp.float32), jnp.asarray(-np.sin(theta), jnp.float32)


def outer_step(parts, cw, sw, index):
    c = lax.dynamic_index_in_dim(cw, index, keepdims=False)
    s = lax.dynamic_index_in_dim(sw, index, keepdims=False)
    tail = (1,) * (parts.ndim - 1)
    c = c.reshape(c.shape[:1] + tail + c.shape[1:])
    s = s.reshape(s.shape[:1] + tail + s.shape[1:])
    return jnp.concatenate([c * parts[None], s * parts[None]], axis=-1)


def inner_step(y, mat):
    shape = y.shape
    return jnp.dot(y.reshape(-1, shape[-1]), mat, precision=precise).reshape(shape)


def packed_tables(blocks, block):
    size = 2 * blocks * block
    half = size // 2
    ids = np.arange(block)
    freqs = np.arange(half)
    theta = 2.0 * np.pi * ((ids[:, None] * freqs[None, :]) % size) / size
    phase = 2.0 * np.pi * ((np.arange(blocks)[:, None] * block * freqs[None, :]) % size) / size
    as32 = lambda a: jnp.asarray(a, jnp.float32)
    return as32(np.cos(theta)), as32(np.sin(theta)), as32(np.cos(phase)), as32(np.sin(phase))


def block_table(packed, index):
    base_c, base_s, turn_c, turn_s = packed
    c = lax.dynamic_index_in_dim(turn_c, index, keepdims=True)
    s = lax.dynamic_index_in_dim(turn_s, index, keepdims=True)
    cos = base_c * c - base_s * s
    sin = base_s * c + base_c * s
    block, half = cos.shape
    first = lax.broadcasted_iota(jnp.int32, (block, half), 1) == 0
    sign = 1.0 - 2.0 * (lax.broadcasted_iota(jnp.int32, (block, half), 0) % 2).astype(jnp.float32)
    return jnp.concatenate([cos, jnp.where(first, sign, -sin)], axis=1)


def packed_products(h, a, conj):
    half = h.shape[1] // 2
    hr, hi = h[:, :half], h[:, half:]
    ar, ai = a[:, :half], a[:, half:]
    first = lax.broadcasted_iota(jnp.int32, hr.shape, 1) == 0
    sign = -1.0 if conj else 1.0
    re = hr * ar - sign * jnp.where(first, 0.0, hi * ai)
    im = jnp.where(first, hi * ai, hr * ai + sign * (hi * ar))
    return jnp.concatenate([re, im], axis=1)


def dense_path(place, blocks, mixed_rows, weighted_rows, back_rows, taps):
    channels, block = mixed_rows.shape
    size = 2 * blocks * block
    half = size // 2
    packed = packed_tables(blocks, block)
    acc = 0.0
    for s in range(1, blocks):
        first = jnp.where(place + s < blocks, mixed_rows, weighted_rows)
        payload = jnp.concatenate([first, taps], axis=0)
        pairs = [(i, (i + s) % blocks) for i in range(blocks)]
        got = lax.ppermute(payload, "ctx", pairs)
        table = block_table(packed, (place - s) % blocks)
        acc = acc + jnp.dot(got, table, precision=precise)
    own_table = block_table(packed, place)
    own = jnp.concatenate([mixed_rows, weighted_rows, back_rows, taps], axis=0)
    loc = jnp.dot(own, own_table, precision=precise)
    c = channels
    mixed_spec = loc[:c] + acc[:c]
    weighted_spec = loc[c : 2 * c] + acc[:c]
    back_spec = loc[2 * c : 3 * c]
    taps_spec = jnp.repeat(loc[3 * c :] + acc[c:], CPF, axis=0)
    conv = packed_products(taps_spec, mixed_spec, False)
    gm = packed_products(taps_spec, weighted_spec, True)
    fgs = packed_products(back_spec, weighted_spec, True)
    fgs = fgs.reshape(-1, CPF, size).sum(axis=1)
    cols = lax.broadcasted_iota(jnp.int32, (1, size), 1)
    weight = jnp.where((cols == 0) | (cols == half), 1.0 / size, 2.0 / size)
    both = jnp.concatenate([conv, gm], axis=0)
    out = jnp.einsum("tf,rf->tr", own_table * weight, both, precision=precise)
    lag = jnp.einsum("rf,tf->rt", fgs, own_table * weight, precision=precise)
    for s in range(1, blocks):
        table = block_table(packed, (place + s) % blocks) * weight
        share = jnp.einsum("rf,tf->rt", fgs, table, precision=precise)
        pairs = [(i, (i + s) % blocks) for i in range(blocks)]
        lag = lag + lax.ppermute(share, "ctx", pairs)
    return out[:, :c], out[:, c:], lag


def chunk_work(local3, common, hsum, tables):
    cw, sw, fwd, inv, inverse, place = tables
    block = local3.shape[-1]
    outer = cw.shape[1]
    own = outer_step(local3, cw, sw, place)
    y = jnp.stack([own[:, 0] + common, own[:, 1] + common, own[:, 2]], axis=1)
    spec = inner_step(y, fwd)
    hspec = jnp.repeat(inner_step(hsum, fwd), CPF, axis=1)
    hr, hi = hspec[..., :block], hspec[..., block:]
    mr, mi = spec[:, 0, :, :block], spec[:, 0, :, block:]
    wr, wi = spec[:, 1, :, :block], spec[:, 1, :, block:]
    br, bi = spec[:, 2, :, :block], spec[:, 2, :, block:]
    conv = jnp.concatenate([hr * mr - hi * mi, hr * mi + hi * mr], axis=-1)
    gm = jnp.concatenate([hr * wr + hi * wi, hr * wi - hi * wr], axis=-1)
    fgs = jnp.concatenate([br * wr + bi * wi, br * wi - bi * wr], axis=-1)
    fgs = fgs.reshape(outer, -1, CPF, 2 * block).sum(axis=2)
    pair = jnp.stack([conv, gm]).transpose(0, 2, 1, 3)
    rows = pair.shape[0] * pair.shape[1]
    both = jnp.dot(pair.reshape(rows, -1), inverse, precision=precise)
    both = both.reshape(2, -1, block)
    z = inner_step(fgs, inv)
    zr, zi = z[..., :block], z[..., block:]
    fg = jnp.stack(
        [jnp.sum(cw[p][:, None] * zr + sw[p][:, None] * zi, axis=0) for p in range(cw.shape[0])]
    )
    return both[0], both[1], fg / (outer * block)


def finish(conv, grad_mixed, lag, filter_scale, query_in, grad_query, key_back, value_back):
    conv = conv * filter_scale
    grad_mixed = grad_mixed * filter_scale
    result = (query_in * conv).astype(jnp.bfloat16)
    next_input = from_behind(result[None], "pipe", 1)
    grad_key = grad_mixed * value_back
    grad_value = grad_mixed * key_back
    grad_stack = jnp.stack([grad_query, grad_key, grad_value], axis=1).astype(jnp.bfloat16)
    prev_grad = from_behind(grad_stack[None], "pipe", -1)
    filter_grad = (lag * filter_scale)[None]
    return (next_input, prev_grad, filter_grad)


def on_device(qkv_in, qkv_saved, conv_saved, out_grad, filters):
    blocks = lax.axis_size("ctx")
    place = lax.axis_index("ctx")
    block = qkv_in.shape[1]
    channels = qkv_in.shape[3]
    groups = filters.shape[1]
    length = blocks * block
    outer = 2 * blocks
    size = outer * block
    filter_scale = (CPF * length) ** (-0.5)

    query_in = qkv_in[0, :, 0].astype(jnp.float32)
    mixed_in = qkv_in[0, :, 1].astype(jnp.float32) * qkv_in[0, :, 2].astype(jnp.float32)
    query_back = qkv_saved[0, :, 0].astype(jnp.float32)
    key_back = qkv_saved[0, :, 1].astype(jnp.float32)
    value_back = qkv_saved[0, :, 2].astype(jnp.float32)
    mixed_back = key_back * value_back
    upstream = out_grad[0].astype(jnp.float32)
    weighted = upstream * query_back
    grad_query = upstream * conv_saved[0]
    taps = filters[0]

    if blocks <= DENSE:
        conv, grad_mixed, lag = dense_path(
            place, blocks, mixed_in.T, weighted.T, mixed_back.T, taps
        )
        return finish(
            conv, grad_mixed, lag, filter_scale, query_in, grad_query, key_back, value_back
        )

    cw, sw = outer_tables(blocks, block, outer)
    fwd, inv = inner_tables(block)

    mixed_rows = mixed_in.T
    weighted_rows = weighted.T
    received = []
    for s in range(1, blocks):
        dest = place + s
        first = jnp.where(dest < blocks, mixed_rows, weighted_rows)
        payload = jnp.concatenate([first, taps], axis=0)
        pairs = [(i, (i + s) % blocks) for i in range(blocks)]
        received.append(lax.ppermute(payload, "ctx", pairs))
    hsum = outer_step(taps, cw, sw, place)
    if blocks <= STEPWISE:
        common = 0.0
        for s, got in enumerate(received, start=1):
            part = outer_step(got, cw, sw, (place - s) % blocks)
            common = common + part[:, :channels]
            hsum = hsum + part[:, channels:]
    else:
        got = jnp.stack(received)
        sources = (place - jnp.arange(1, blocks, dtype=jnp.int32)) % blocks
        weights = jnp.concatenate([cw[sources], sw[sources]], axis=-1)
        both = jnp.concatenate([got, got], axis=-1)
        part = jnp.einsum("sfp,scp->fcp", weights, both, precision=highest)
        common = part[:, :channels]
        hsum = hsum + part[:, channels:]
    local3 = jnp.stack([mixed_rows, weighted_rows, mixed_back.T])

    pos = place * block + jnp.arange(block, dtype=jnp.int32)
    freq = (
        jnp.arange(outer, dtype=jnp.int32)[:, None, None]
        + outer * jnp.arange(block, dtype=jnp.int32)[None, None, :]
    )
    prod = (freq * pos[None, :, None]) % size
    theta = prod.astype(jnp.float32) * (2.0 * math.pi / size)
    inverse = jnp.concatenate([jnp.cos(theta), -jnp.sin(theta)], axis=-1) / size
    inverse = inverse.transpose(0, 2, 1).reshape(outer * 2 * block, block)
    tables = (cw, sw, fwd, inv, inverse, place)

    per_group = 2 * block * outer * 4 * 4 * CPF * blocks
    gchunk = groups
    while gchunk > 1 and gchunk * per_group > CHUNK_BYTES and groups % (gchunk // 2) == 0:
        gchunk //= 2
    nchunk = groups // gchunk
    if nchunk == 1:
        conv, grad_mixed, fg = chunk_work(local3, common, hsum, tables)
    else:
        cc = gchunk * CPF
        ls = local3.reshape(3, nchunk, cc, block).transpose(1, 0, 2, 3)
        cs = common.reshape(outer, nchunk, cc, 2 * block).transpose(1, 0, 2, 3)
        hs = hsum.reshape(outer, nchunk, gchunk, 2 * block).transpose(1, 0, 2, 3)
        conv, grad_mixed, fg = lax.map(lambda a: chunk_work(a[0], a[1], a[2], tables), (ls, cs, hs))
        conv = conv.reshape(channels, block)
        grad_mixed = grad_mixed.reshape(channels, block)
        fg = fg.transpose(1, 0, 2, 3).reshape(blocks, groups, block)

    lag_sum = fg[place]
    for s in range(1, blocks):
        dest = (place + s) % blocks
        pairs = [(i, (i + s) % blocks) for i in range(blocks)]
        lag_sum = lag_sum + lax.ppermute(fg[dest], "ctx", pairs)

    return finish(
        conv.T, grad_mixed.T, lag_sum, filter_scale, query_in, grad_query, key_back, value_back
    )


def solution(mesh):
    return jax.shard_map(
        on_device,
        mesh=mesh,
        in_specs=(
            P("pipe", "ctx", None, None),
            P("pipe", "ctx", None, None),
            P("pipe", "ctx", None),
            P("pipe", "ctx", None),
            P("pipe", None, "ctx"),
        ),
        out_specs=(P("pipe", "ctx", None), P("pipe", "ctx", None, None), P("pipe", None, "ctx")),
        check_vma=False,
    )
```

```python
import math

import numpy as np

import jax
import jax.numpy as jnp
from jax import lax
from jax.sharding import PartitionSpec as P

CPF = 16
CHUNK_BYTES = 36 * 2**20
STEPWISE = 4
DENSE = 4

highest = lax.Precision.HIGHEST
precise = lax.Precision.HIGH


def from_behind(x, axis, by):
    devices = lax.axis_size(axis)
    pairs = [(i, i + by) for i in range(devices) if 0 <= i + by < devices]
    return lax.ppermute(x, axis, pairs)


def inner_tables(block):
    ids = np.arange(block)
    theta = 2.0 * np.pi * ((ids[:, None] * ids[None, :]) % block) / block
    cos, sin = np.cos(theta), np.sin(theta)
    fwd = np.block([[cos, -sin], [sin, cos]])
    inv = np.block([[cos, sin], [-sin, cos]])
    return jnp.asarray(fwd, jnp.float32), jnp.asarray(inv, jnp.float32)


def outer_tables(blocks, block, outer):
    size = outer * block
    pos = np.arange(blocks)[:, None, None] * block + np.arange(block)[None, None, :]
    prod = (pos * np.arange(outer)[None, :, None]) % size
    theta = 2.0 * np.pi * prod / size
    return jnp.asarray(np.cos(theta), jnp.float32), jnp.asarray(-np.sin(theta), jnp.float32)


def outer_step(parts, cw, sw, index):
    c = lax.dynamic_index_in_dim(cw, index, keepdims=False)
    s = lax.dynamic_index_in_dim(sw, index, keepdims=False)
    tail = (1,) * (parts.ndim - 1)
    c = c.reshape(c.shape[:1] + tail + c.shape[1:])
    s = s.reshape(s.shape[:1] + tail + s.shape[1:])
    return jnp.concatenate([c * parts[None], s * parts[None]], axis=-1)


def inner_step(y, mat):
    shape = y.shape
    return jnp.dot(y.reshape(-1, shape[-1]), mat, precision=precise).reshape(shape)


def packed_tables(blocks, block):
    size = 2 * blocks * block
    half = size // 2
    ids = np.arange(block)
    freqs = np.arange(half)
    theta = 2.0 * np.pi * ((ids[:, None] * freqs[None, :]) % size) / size
    phase = 2.0 * np.pi * ((np.arange(blocks)[:, None] * block * freqs[None, :]) % size) / size
    as32 = lambda a: jnp.asarray(a, jnp.float32)
    return as32(np.cos(theta)), as32(np.sin(theta)), as32(np.cos(phase)), as32(np.sin(phase))


def block_table(packed, index):
    base_c, base_s, turn_c, turn_s = packed
    c = lax.dynamic_index_in_dim(turn_c, index, keepdims=True)
    s = lax.dynamic_index_in_dim(turn_s, index, keepdims=True)
    cos = base_c * c - base_s * s
    sin = base_s * c + base_c * s
    block, half = cos.shape
    first = lax.broadcasted_iota(jnp.int32, (block, half), 1) == 0
    sign = 1.0 - 2.0 * (lax.broadcasted_iota(jnp.int32, (block, half), 0) % 2).astype(jnp.float32)
    return jnp.concatenate([cos, jnp.where(first, sign, -sin)], axis=1)


def packed_products(h, a, conj):
    half = h.shape[1] // 2
    hr, hi = h[:, :half], h[:, half:]
    ar, ai = a[:, :half], a[:, half:]
    first = lax.broadcasted_iota(jnp.int32, hr.shape, 1) == 0
    sign = -1.0 if conj else 1.0
    re = hr * ar - sign * jnp.where(first, 0.0, hi * ai)
    im = jnp.where(first, hi * ai, hr * ai + sign * (hi * ar))
    return jnp.concatenate([re, im], axis=1)


def turned(rows):
    eye = jnp.eye(rows.shape[1], dtype=rows.dtype)
    return jnp.einsum("gp,pq->qg", rows, eye, precision=highest)


def dense_path(place, blocks, mixed, weighted, back, taps):
    block, channels = mixed.shape
    size = 2 * blocks * block
    half = size // 2
    packed = packed_tables(blocks, block)
    acc = 0.0
    for s in range(1, blocks):
        first = jnp.where(place + s < blocks, mixed, weighted)
        payload = jnp.concatenate([first, taps], axis=1)
        pairs = [(i, (i + s) % blocks) for i in range(blocks)]
        got = lax.ppermute(payload, "ctx", pairs)
        table = block_table(packed, (place - s) % blocks)
        acc = acc + jnp.einsum("pr,pf->rf", got, table, precision=precise)
    own_table = block_table(packed, place)
    own = jnp.concatenate([mixed, weighted, back, taps], axis=1)
    loc = jnp.einsum("pr,pf->rf", own, own_table, precision=precise)
    c = channels
    mixed_spec = loc[:c] + acc[:c]
    weighted_spec = loc[c : 2 * c] + acc[:c]
    back_spec = loc[2 * c : 3 * c]
    taps_spec = jnp.repeat(loc[3 * c :] + acc[c:], CPF, axis=0)
    conv = packed_products(taps_spec, mixed_spec, False)
    gm = packed_products(taps_spec, weighted_spec, True)
    fgs = packed_products(back_spec, weighted_spec, True)
    fgs = fgs.reshape(-1, CPF, size).sum(axis=1)
    cols = lax.broadcasted_iota(jnp.int32, (1, size), 1)
    weight = jnp.where((cols == 0) | (cols == half), 1.0 / size, 2.0 / size)
    both = jnp.concatenate([conv, gm], axis=0)
    out = jnp.einsum("tf,rf->tr", own_table * weight, both, precision=precise)
    lag = jnp.einsum("rf,tf->rt", fgs, own_table * weight, precision=precise)
    for s in range(1, blocks):
        table = block_table(packed, (place + s) % blocks) * weight
        share = jnp.einsum("rf,tf->rt", fgs, table, precision=precise)
        pairs = [(i, (i + s) % blocks) for i in range(blocks)]
        lag = lag + lax.ppermute(share, "ctx", pairs)
    return out[:, :c], out[:, c:], lag


def chunk_work(local3, common, hsum, tables):
    cw, sw, fwd, inv, inverse, place = tables
    block = local3.shape[-1]
    outer = cw.shape[1]
    own = outer_step(local3, cw, sw, place)
    y = jnp.stack([own[:, 0] + common, own[:, 1] + common, own[:, 2]], axis=1)
    spec = inner_step(y, fwd)
    hspec = jnp.repeat(inner_step(hsum, fwd), CPF, axis=1)
    hr, hi = hspec[..., :block], hspec[..., block:]
    mr, mi = spec[:, 0, :, :block], spec[:, 0, :, block:]
    wr, wi = spec[:, 1, :, :block], spec[:, 1, :, block:]
    br, bi = spec[:, 2, :, :block], spec[:, 2, :, block:]
    conv = jnp.concatenate([hr * mr - hi * mi, hr * mi + hi * mr], axis=-1)
    gm = jnp.concatenate([hr * wr + hi * wi, hr * wi - hi * wr], axis=-1)
    fgs = jnp.concatenate([br * wr + bi * wi, br * wi - bi * wr], axis=-1)
    fgs = fgs.reshape(outer, -1, CPF, 2 * block).sum(axis=2)
    pair = jnp.stack([conv, gm]).transpose(0, 2, 1, 3)
    rows = pair.shape[0] * pair.shape[1]
    both = jnp.dot(pair.reshape(rows, -1), inverse, precision=precise)
    both = both.reshape(2, -1, block)
    z = inner_step(fgs, inv)
    zr, zi = z[..., :block], z[..., block:]
    fg = jnp.stack(
        [jnp.sum(cw[p][:, None] * zr + sw[p][:, None] * zi, axis=0) for p in range(cw.shape[0])]
    )
    return both[0], both[1], fg / (outer * block)


def finish(conv, grad_mixed, lag, filter_scale, query_in, grad_query, key_back, value_back):
    conv = conv * filter_scale
    grad_mixed = grad_mixed * filter_scale
    result = (query_in * conv).astype(jnp.bfloat16)
    next_input = from_behind(result[None], "pipe", 1)
    grad_key = grad_mixed * value_back
    grad_value = grad_mixed * key_back
    grad_stack = jnp.stack([grad_query, grad_key, grad_value], axis=1).astype(jnp.bfloat16)
    prev_grad = from_behind(grad_stack[None], "pipe", -1)
    filter_grad = (lag * filter_scale)[None]
    return (next_input, prev_grad, filter_grad)


def on_device(qkv_in, qkv_saved, conv_saved, out_grad, filters):
    blocks = lax.axis_size("ctx")
    place = lax.axis_index("ctx")
    block = qkv_in.shape[1]
    channels = qkv_in.shape[3]
    groups = filters.shape[1]
    length = blocks * block
    outer = 2 * blocks
    size = outer * block
    filter_scale = (CPF * length) ** (-0.5)

    query_in = qkv_in[0, :, 0].astype(jnp.float32)
    mixed_in = qkv_in[0, :, 1].astype(jnp.float32) * qkv_in[0, :, 2].astype(jnp.float32)
    query_back = qkv_saved[0, :, 0].astype(jnp.float32)
    key_back = qkv_saved[0, :, 1].astype(jnp.float32)
    value_back = qkv_saved[0, :, 2].astype(jnp.float32)
    mixed_back = key_back * value_back
    upstream = out_grad[0].astype(jnp.float32)
    weighted = upstream * query_back
    grad_query = upstream * conv_saved[0]
    taps = filters[0]

    if blocks <= DENSE:
        conv, grad_mixed, lag = dense_path(
            place, blocks, mixed_in, weighted, mixed_back, turned(taps)
        )
        return finish(
            conv, grad_mixed, lag, filter_scale, query_in, grad_query, key_back, value_back
        )

    cw, sw = outer_tables(blocks, block, outer)
    fwd, inv = inner_tables(block)

    mixed_rows = mixed_in.T
    weighted_rows = weighted.T
    received = []
    for s in range(1, blocks):
        dest = place + s
        first = jnp.where(dest < blocks, mixed_rows, weighted_rows)
        payload = jnp.concatenate([first, taps], axis=0)
        pairs = [(i, (i + s) % blocks) for i in range(blocks)]
        received.append(lax.ppermute(payload, "ctx", pairs))
    hsum = outer_step(taps, cw, sw, place)
    if blocks <= STEPWISE:
        common = 0.0
        for s, got in enumerate(received, start=1):
            part = outer_step(got, cw, sw, (place - s) % blocks)
            common = common + part[:, :channels]
            hsum = hsum + part[:, channels:]
    else:
        got = jnp.stack(received)
        sources = (place - jnp.arange(1, blocks, dtype=jnp.int32)) % blocks
        weights = jnp.concatenate([cw[sources], sw[sources]], axis=-1)
        both = jnp.concatenate([got, got], axis=-1)
        part = jnp.einsum("sfp,scp->fcp", weights, both, precision=highest)
        common = part[:, :channels]
        hsum = hsum + part[:, channels:]
    local3 = jnp.stack([mixed_rows, weighted_rows, mixed_back.T])

    pos = place * block + jnp.arange(block, dtype=jnp.int32)
    freq = (
        jnp.arange(outer, dtype=jnp.int32)[:, None, None]
        + outer * jnp.arange(block, dtype=jnp.int32)[None, None, :]
    )
    prod = (freq * pos[None, :, None]) % size
    theta = prod.astype(jnp.float32) * (2.0 * math.pi / size)
    inverse = jnp.concatenate([jnp.cos(theta), -jnp.sin(theta)], axis=-1) / size
    inverse = inverse.transpose(0, 2, 1).reshape(outer * 2 * block, block)
    tables = (cw, sw, fwd, inv, inverse, place)

    per_group = 2 * block * outer * 4 * 4 * CPF * blocks
    gchunk = groups
    while gchunk > 1 and gchunk * per_group > CHUNK_BYTES and groups % (gchunk // 2) == 0:
        gchunk //= 2
    nchunk = groups // gchunk
    if nchunk == 1:
        conv, grad_mixed, fg = chunk_work(local3, common, hsum, tables)
    else:
        cc = gchunk * CPF
        ls = local3.reshape(3, nchunk, cc, block).transpose(1, 0, 2, 3)
        cs = common.reshape(outer, nchunk, cc, 2 * block).transpose(1, 0, 2, 3)
        hs = hsum.reshape(outer, nchunk, gchunk, 2 * block).transpose(1, 0, 2, 3)
        conv, grad_mixed, fg = lax.map(lambda a: chunk_work(a[0], a[1], a[2], tables), (ls, cs, hs))
        conv = conv.reshape(channels, block)
        grad_mixed = grad_mixed.reshape(channels, block)
        fg = fg.transpose(1, 0, 2, 3).reshape(blocks, groups, block)

    lag_sum = fg[place]
    for s in range(1, blocks):
        dest = (place + s) % blocks
        pairs = [(i, (i + s) % blocks) for i in range(blocks)]
        lag_sum = lag_sum + lax.ppermute(fg[dest], "ctx", pairs)

    return finish(
        conv.T, grad_mixed.T, lag_sum, filter_scale, query_in, grad_query, key_back, value_back
    )


def solution(mesh):
    return jax.shard_map(
        on_device,
        mesh=mesh,
        in_specs=(
            P("pipe", "ctx", None, None),
            P("pipe", "ctx", None, None),
            P("pipe", "ctx", None),
            P("pipe", "ctx", None),
            P("pipe", None, "ctx"),
        ),
        out_specs=(P("pipe", "ctx", None), P("pipe", "ctx", None, None), P("pipe", None, "ctx")),
        check_vma=False,
    )
```

```python
import math

import numpy as np

import jax
import jax.numpy as jnp
from jax import lax
from jax.sharding import PartitionSpec as P

CPF = 16
CHUNK_BYTES = 36 * 2**20
STEPWISE = 4
DENSE = 4

highest = lax.Precision.HIGHEST
precise = lax.Precision.HIGH


def from_behind(x, axis, by):
    devices = lax.axis_size(axis)
    pairs = [(i, i + by) for i in range(devices) if 0 <= i + by < devices]
    return lax.ppermute(x, axis, pairs)


def inner_tables(block):
    ids = np.arange(block)
    theta = 2.0 * np.pi * ((ids[:, None] * ids[None, :]) % block) / block
    cos, sin = np.cos(theta), np.sin(theta)
    fwd = np.block([[cos, -sin], [sin, cos]])
    inv = np.block([[cos, sin], [-sin, cos]])
    return jnp.asarray(fwd, jnp.float32), jnp.asarray(inv, jnp.float32)


def outer_tables(blocks, block, outer):
    size = outer * block
    pos = np.arange(blocks)[:, None, None] * block + np.arange(block)[None, None, :]
    prod = (pos * np.arange(outer)[None, :, None]) % size
    theta = 2.0 * np.pi * prod / size
    return jnp.asarray(np.cos(theta), jnp.float32), jnp.asarray(-np.sin(theta), jnp.float32)


def outer_step(parts, cw, sw, index):
    c = lax.dynamic_index_in_dim(cw, index, keepdims=False)
    s = lax.dynamic_index_in_dim(sw, index, keepdims=False)
    tail = (1,) * (parts.ndim - 1)
    c = c.reshape(c.shape[:1] + tail + c.shape[1:])
    s = s.reshape(s.shape[:1] + tail + s.shape[1:])
    return jnp.concatenate([c * parts[None], s * parts[None]], axis=-1)


def inner_step(y, mat):
    shape = y.shape
    return jnp.dot(y.reshape(-1, shape[-1]), mat, precision=precise).reshape(shape)


def packed_tables(blocks, block):
    size = 2 * blocks * block
    half = size // 2
    ids = np.arange(block)
    freqs = np.arange(half)
    theta = 2.0 * np.pi * ((ids[:, None] * freqs[None, :]) % size) / size
    phase = 2.0 * np.pi * ((np.arange(blocks)[:, None] * block * freqs[None, :]) % size) / size
    as32 = lambda a: jnp.asarray(a, jnp.float32)
    return as32(np.cos(theta)), as32(np.sin(theta)), as32(np.cos(phase)), as32(np.sin(phase))


def block_table(packed, index):
    base_c, base_s, turn_c, turn_s = packed
    c = lax.dynamic_index_in_dim(turn_c, index, keepdims=True)
    s = lax.dynamic_index_in_dim(turn_s, index, keepdims=True)
    cos = base_c * c - base_s * s
    sin = base_s * c + base_c * s
    block, half = cos.shape
    first = lax.broadcasted_iota(jnp.int32, (block, half), 1) == 0
    sign = 1.0 - 2.0 * (lax.broadcasted_iota(jnp.int32, (block, half), 0) % 2).astype(jnp.float32)
    return jnp.concatenate([cos, jnp.where(first, sign, -sin)], axis=1)


def packed_products(h, a, conj):
    half = h.shape[1] // 2
    hr, hi = h[:, :half], h[:, half:]
    ar, ai = a[:, :half], a[:, half:]
    first = lax.broadcasted_iota(jnp.int32, hr.shape, 1) == 0
    sign = -1.0 if conj else 1.0
    re = hr * ar - sign * jnp.where(first, 0.0, hi * ai)
    im = jnp.where(first, hi * ai, hr * ai + sign * (hi * ar))
    return jnp.concatenate([re, im], axis=1)


def dense_path(place, blocks, mixed_rows, weighted_rows, back_rows, taps):
    channels, block = mixed_rows.shape
    size = 2 * blocks * block
    half = size // 2
    packed = packed_tables(blocks, block)
    acc = 0.0
    for s in range(1, blocks):
        first = jnp.where(place + s < blocks, mixed_rows, weighted_rows)
        payload = jnp.concatenate([first, taps], axis=0)
        pairs = [(i, (i + s) % blocks) for i in range(blocks)]
        got = lax.ppermute(payload, "ctx", pairs)
        table = block_table(packed, (place - s) % blocks)
        acc = acc + jnp.dot(got, table, precision=precise)
    own_table = block_table(packed, place)
    own = jnp.concatenate([mixed_rows, weighted_rows, back_rows, taps], axis=0)
    loc = jnp.dot(own, own_table, precision=precise)
    c = channels
    mixed_spec = loc[:c] + acc[:c]
    weighted_spec = loc[c : 2 * c] + acc[:c]
    back_spec = loc[2 * c : 3 * c]
    taps_spec = jnp.repeat(loc[3 * c :] + acc[c:], CPF, axis=0)
    conv = packed_products(taps_spec, mixed_spec, False)
    gm = packed_products(taps_spec, weighted_spec, True)
    fgs = packed_products(back_spec, weighted_spec, True)
    fgs = fgs.reshape(-1, CPF, size).sum(axis=1)
    cols = lax.broadcasted_iota(jnp.int32, (1, size), 1)
    weight = jnp.where((cols == 0) | (cols == half), 1.0 / size, 2.0 / size)
    both = jnp.concatenate([conv, gm], axis=0)
    out = jnp.einsum("tf,rf->tr", own_table * weight, both, precision=precise)
    lag = jnp.einsum("rf,tf->rt", fgs, own_table * weight, precision=precise)
    others = jnp.concatenate(
        [block_table(packed, (place + s) % blocks) for s in range(1, blocks)], axis=0
    )
    shares = jnp.einsum("rf,tf->rt", fgs, others * weight, precision=precise)
    for s in range(1, blocks):
        share = shares[:, (s - 1) * block : s * block]
        pairs = [(i, (i + s) % blocks) for i in range(blocks)]
        lag = lag + lax.ppermute(share, "ctx", pairs)
    return out[:, :c], out[:, c:], lag


def chunk_work(local3, common, hsum, tables):
    cw, sw, fwd, inv, inverse, place = tables
    block = local3.shape[-1]
    outer = cw.shape[1]
    own = outer_step(local3, cw, sw, place)
    y = jnp.stack([own[:, 0] + common, own[:, 1] + common, own[:, 2]], axis=1)
    spec = inner_step(y, fwd)
    hspec = jnp.repeat(inner_step(hsum, fwd), CPF, axis=1)
    hr, hi = hspec[..., :block], hspec[..., block:]
    mr, mi = spec[:, 0, :, :block], spec[:, 0, :, block:]
    wr, wi = spec[:, 1, :, :block], spec[:, 1, :, block:]
    br, bi = spec[:, 2, :, :block], spec[:, 2, :, block:]
    conv = jnp.concatenate([hr * mr - hi * mi, hr * mi + hi * mr], axis=-1)
    gm = jnp.concatenate([hr * wr + hi * wi, hr * wi - hi * wr], axis=-1)
    fgs = jnp.concatenate([br * wr + bi * wi, br * wi - bi * wr], axis=-1)
    fgs = fgs.reshape(outer, -1, CPF, 2 * block).sum(axis=2)
    pair = jnp.stack([conv, gm]).transpose(0, 2, 1, 3)
    rows = pair.shape[0] * pair.shape[1]
    both = jnp.dot(pair.reshape(rows, -1), inverse, precision=precise)
    both = both.reshape(2, -1, block)
    z = inner_step(fgs, inv)
    zr, zi = z[..., :block], z[..., block:]
    fg = jnp.stack(
        [jnp.sum(cw[p][:, None] * zr + sw[p][:, None] * zi, axis=0) for p in range(cw.shape[0])]
    )
    return both[0], both[1], fg / (outer * block)


def finish(conv, grad_mixed, lag, filter_scale, query_in, grad_query, key_back, value_back):
    conv = conv * filter_scale
    grad_mixed = grad_mixed * filter_scale
    result = (query_in * conv).astype(jnp.bfloat16)
    next_input = from_behind(result[None], "pipe", 1)
    grad_key = grad_mixed * value_back
    grad_value = grad_mixed * key_back
    grad_stack = jnp.stack([grad_query, grad_key, grad_value], axis=1).astype(jnp.bfloat16)
    prev_grad = from_behind(grad_stack[None], "pipe", -1)
    filter_grad = (lag * filter_scale)[None]
    return (next_input, prev_grad, filter_grad)


def on_device(qkv_in, qkv_saved, conv_saved, out_grad, filters):
    blocks = lax.axis_size("ctx")
    place = lax.axis_index("ctx")
    block = qkv_in.shape[1]
    channels = qkv_in.shape[3]
    groups = filters.shape[1]
    length = blocks * block
    outer = 2 * blocks
    size = outer * block
    filter_scale = (CPF * length) ** (-0.5)

    query_in = qkv_in[0, :, 0].astype(jnp.float32)
    mixed_in = qkv_in[0, :, 1].astype(jnp.float32) * qkv_in[0, :, 2].astype(jnp.float32)
    query_back = qkv_saved[0, :, 0].astype(jnp.float32)
    key_back = qkv_saved[0, :, 1].astype(jnp.float32)
    value_back = qkv_saved[0, :, 2].astype(jnp.float32)
    mixed_back = key_back * value_back
    upstream = out_grad[0].astype(jnp.float32)
    weighted = upstream * query_back
    grad_query = upstream * conv_saved[0]
    taps = filters[0]

    if blocks <= DENSE:
        conv, grad_mixed, lag = dense_path(
            place, blocks, mixed_in.T, weighted.T, mixed_back.T, taps
        )
        return finish(
            conv, grad_mixed, lag, filter_scale, query_in, grad_query, key_back, value_back
        )

    cw, sw = outer_tables(blocks, block, outer)
    fwd, inv = inner_tables(block)

    mixed_rows = mixed_in.T
    weighted_rows = weighted.T
    received = []
    for s in range(1, blocks):
        dest = place + s
        first = jnp.where(dest < blocks, mixed_rows, weighted_rows)
        payload = jnp.concatenate([first, taps], axis=0)
        pairs = [(i, (i + s) % blocks) for i in range(blocks)]
        received.append(lax.ppermute(payload, "ctx", pairs))
    hsum = outer_step(taps, cw, sw, place)
    if blocks <= STEPWISE:
        common = 0.0
        for s, got in enumerate(received, start=1):
            part = outer_step(got, cw, sw, (place - s) % blocks)
            common = common + part[:, :channels]
            hsum = hsum + part[:, channels:]
    else:
        got = jnp.stack(received)
        sources = (place - jnp.arange(1, blocks, dtype=jnp.int32)) % blocks
        weights = jnp.concatenate([cw[sources], sw[sources]], axis=-1)
        both = jnp.concatenate([got, got], axis=-1)
        part = jnp.einsum("sfp,scp->fcp", weights, both, precision=highest)
        common = part[:, :channels]
        hsum = hsum + part[:, channels:]
    local3 = jnp.stack([mixed_rows, weighted_rows, mixed_back.T])

    pos = place * block + jnp.arange(block, dtype=jnp.int32)
    freq = (
        jnp.arange(outer, dtype=jnp.int32)[:, None, None]
        + outer * jnp.arange(block, dtype=jnp.int32)[None, None, :]
    )
    prod = (freq * pos[None, :, None]) % size
    theta = prod.astype(jnp.float32) * (2.0 * math.pi / size)
    inverse = jnp.concatenate([jnp.cos(theta), -jnp.sin(theta)], axis=-1) / size
    inverse = inverse.transpose(0, 2, 1).reshape(outer * 2 * block, block)
    tables = (cw, sw, fwd, inv, inverse, place)

    per_group = 2 * block * outer * 4 * 4 * CPF * blocks
    gchunk = groups
    while gchunk > 1 and gchunk * per_group > CHUNK_BYTES and groups % (gchunk // 2) == 0:
        gchunk //= 2
    nchunk = groups // gchunk
    if nchunk == 1:
        conv, grad_mixed, fg = chunk_work(local3, common, hsum, tables)
    else:
        cc = gchunk * CPF
        ls = local3.reshape(3, nchunk, cc, block).transpose(1, 0, 2, 3)
        cs = common.reshape(outer, nchunk, cc, 2 * block).transpose(1, 0, 2, 3)
        hs = hsum.reshape(outer, nchunk, gchunk, 2 * block).transpose(1, 0, 2, 3)
        conv, grad_mixed, fg = lax.map(lambda a: chunk_work(a[0], a[1], a[2], tables), (ls, cs, hs))
        conv = conv.reshape(channels, block)
        grad_mixed = grad_mixed.reshape(channels, block)
        fg = fg.transpose(1, 0, 2, 3).reshape(blocks, groups, block)

    lag_sum = fg[place]
    for s in range(1, blocks):
        dest = (place + s) % blocks
        pairs = [(i, (i + s) % blocks) for i in range(blocks)]
        lag_sum = lag_sum + lax.ppermute(fg[dest], "ctx", pairs)

    return finish(
        conv.T, grad_mixed.T, lag_sum, filter_scale, query_in, grad_query, key_back, value_back
    )


def solution(mesh):
    return jax.shard_map(
        on_device,
        mesh=mesh,
        in_specs=(
            P("pipe", "ctx", None, None),
            P("pipe", "ctx", None, None),
            P("pipe", "ctx", None),
            P("pipe", "ctx", None),
            P("pipe", None, "ctx"),
        ),
        out_specs=(P("pipe", "ctx", None), P("pipe", "ctx", None, None), P("pipe", None, "ctx")),
        check_vma=False,
    )
```

```python
import math

import numpy as np

import jax
import jax.numpy as jnp
from jax import lax
from jax.sharding import PartitionSpec as P

CPF = 16
CHUNK_BYTES = 36 * 2**20
STEPWISE = 4
DENSE = 4

highest = lax.Precision.HIGHEST
precise = lax.Precision.HIGH


def from_behind(x, axis, by):
    devices = lax.axis_size(axis)
    pairs = [(i, i + by) for i in range(devices) if 0 <= i + by < devices]
    return lax.ppermute(x, axis, pairs)


def inner_tables(block):
    ids = np.arange(block)
    theta = 2.0 * np.pi * ((ids[:, None] * ids[None, :]) % block) / block
    cos, sin = np.cos(theta), np.sin(theta)
    fwd = np.block([[cos, -sin], [sin, cos]])
    inv = np.block([[cos, sin], [-sin, cos]])
    return jnp.asarray(fwd, jnp.float32), jnp.asarray(inv, jnp.float32)


def outer_tables(blocks, block, outer):
    size = outer * block
    pos = np.arange(blocks)[:, None, None] * block + np.arange(block)[None, None, :]
    prod = (pos * np.arange(outer)[None, :, None]) % size
    theta = 2.0 * np.pi * prod / size
    return jnp.asarray(np.cos(theta), jnp.float32), jnp.asarray(-np.sin(theta), jnp.float32)


def outer_step(parts, cw, sw, index):
    c = lax.dynamic_index_in_dim(cw, index, keepdims=False)
    s = lax.dynamic_index_in_dim(sw, index, keepdims=False)
    tail = (1,) * (parts.ndim - 1)
    c = c.reshape(c.shape[:1] + tail + c.shape[1:])
    s = s.reshape(s.shape[:1] + tail + s.shape[1:])
    return jnp.concatenate([c * parts[None], s * parts[None]], axis=-1)


def inner_step(y, mat):
    shape = y.shape
    return jnp.dot(y.reshape(-1, shape[-1]), mat, precision=precise).reshape(shape)


def packed_tables(blocks, block):
    size = 2 * blocks * block
    half = size // 2
    ids = np.arange(block)
    freqs = np.arange(half)
    theta = 2.0 * np.pi * ((ids[:, None] * freqs[None, :]) % size) / size
    phase = 2.0 * np.pi * ((np.arange(blocks)[:, None] * block * freqs[None, :]) % size) / size
    as32 = lambda a: jnp.asarray(a, jnp.float32)
    return as32(np.cos(theta)), as32(np.sin(theta)), as32(np.cos(phase)), as32(np.sin(phase))


def block_table(packed, index):
    base_c, base_s, turn_c, turn_s = packed
    c = lax.dynamic_index_in_dim(turn_c, index, keepdims=True)
    s = lax.dynamic_index_in_dim(turn_s, index, keepdims=True)
    cos = base_c * c - base_s * s
    sin = base_s * c + base_c * s
    block, half = cos.shape
    first = lax.broadcasted_iota(jnp.int32, (block, half), 1) == 0
    sign = 1.0 - 2.0 * (lax.broadcasted_iota(jnp.int32, (block, half), 0) % 2).astype(jnp.float32)
    return jnp.concatenate([cos, jnp.where(first, sign, -sin)], axis=1)


def packed_products(h, a, conj):
    half = h.shape[1] // 2
    hr, hi = h[:, :half], h[:, half:]
    ar, ai = a[:, :half], a[:, half:]
    first = lax.broadcasted_iota(jnp.int32, hr.shape, 1) == 0
    sign = -1.0 if conj else 1.0
    re = hr * ar - sign * jnp.where(first, 0.0, hi * ai)
    im = jnp.where(first, hi * ai, hr * ai + sign * (hi * ar))
    return jnp.concatenate([re, im], axis=1)


def dense_path(place, blocks, mixed_rows, weighted_rows, back_rows, taps):
    channels, block = mixed_rows.shape
    size = 2 * blocks * block
    half = size // 2
    packed = packed_tables(blocks, block)
    swap = blocks & (blocks - 1) == 0
    dest = (lambda i, s: i ^ s) if swap else (lambda i, s: (i + s) % blocks)
    source = (lambda i, s: i ^ s) if swap else (lambda i, s: (i - s) % blocks)
    acc = 0.0
    for s in range(1, blocks):
        first = jnp.where(dest(place, s) > place, mixed_rows, weighted_rows)
        payload = jnp.concatenate([first, taps], axis=0)
        pairs = [(i, dest(i, s)) for i in range(blocks)]
        got = lax.ppermute(payload, "ctx", pairs)
        table = block_table(packed, source(place, s))
        acc = acc + jnp.dot(got, table, precision=precise)
    own_table = block_table(packed, place)
    own = jnp.concatenate([mixed_rows, weighted_rows, back_rows, taps], axis=0)
    loc = jnp.dot(own, own_table, precision=precise)
    c = channels
    mixed_spec = loc[:c] + acc[:c]
    weighted_spec = loc[c : 2 * c] + acc[:c]
    back_spec = loc[2 * c : 3 * c]
    taps_spec = jnp.repeat(loc[3 * c :] + acc[c:], CPF, axis=0)
    conv = packed_products(taps_spec, mixed_spec, False)
    gm = packed_products(taps_spec, weighted_spec, True)
    fgs = packed_products(back_spec, weighted_spec, True)
    fgs = fgs.reshape(-1, CPF, size).sum(axis=1)
    cols = lax.broadcasted_iota(jnp.int32, (1, size), 1)
    weight = jnp.where((cols == 0) | (cols == half), 1.0 / size, 2.0 / size)
    both = jnp.concatenate([conv, gm], axis=0)
    out = jnp.einsum("tf,rf->tr", own_table * weight, both, precision=precise)
    lag = jnp.einsum("rf,tf->rt", fgs, own_table * weight, precision=precise)
    for s in range(1, blocks):
        table = block_table(packed, dest(place, s)) * weight
        share = jnp.einsum("rf,tf->rt", fgs, table, precision=precise)
        pairs = [(i, dest(i, s)) for i in range(blocks)]
        lag = lag + lax.ppermute(share, "ctx", pairs)
    return out[:, :c], out[:, c:], lag


def chunk_work(local3, common, hsum, tables):
    cw, sw, fwd, inv, inverse, place = tables
    block = local3.shape[-1]
    outer = cw.shape[1]
    own = outer_step(local3, cw, sw, place)
    y = jnp.stack([own[:, 0] + common, own[:, 1] + common, own[:, 2]], axis=1)
    spec = inner_step(y, fwd)
    hspec = jnp.repeat(inner_step(hsum, fwd), CPF, axis=1)
    hr, hi = hspec[..., :block], hspec[..., block:]
    mr, mi = spec[:, 0, :, :block], spec[:, 0, :, block:]
    wr, wi = spec[:, 1, :, :block], spec[:, 1, :, block:]
    br, bi = spec[:, 2, :, :block], spec[:, 2, :, block:]
    conv = jnp.concatenate([hr * mr - hi * mi, hr * mi + hi * mr], axis=-1)
    gm = jnp.concatenate([hr * wr + hi * wi, hr * wi - hi * wr], axis=-1)
    fgs = jnp.concatenate([br * wr + bi * wi, br * wi - bi * wr], axis=-1)
    fgs = fgs.reshape(outer, -1, CPF, 2 * block).sum(axis=2)
    pair = jnp.stack([conv, gm]).transpose(0, 2, 1, 3)
    rows = pair.shape[0] * pair.shape[1]
    both = jnp.dot(pair.reshape(rows, -1), inverse, precision=precise)
    both = both.reshape(2, -1, block)
    z = inner_step(fgs, inv)
    zr, zi = z[..., :block], z[..., block:]
    fg = jnp.stack(
        [jnp.sum(cw[p][:, None] * zr + sw[p][:, None] * zi, axis=0) for p in range(cw.shape[0])]
    )
    return both[0], both[1], fg / (outer * block)


def finish(conv, grad_mixed, lag, filter_scale, query_in, grad_query, key_back, value_back):
    conv = conv * filter_scale
    grad_mixed = grad_mixed * filter_scale
    result = (query_in * conv).astype(jnp.bfloat16)
    next_input = from_behind(result[None], "pipe", 1)
    grad_key = grad_mixed * value_back
    grad_value = grad_mixed * key_back
    grad_stack = jnp.stack([grad_query, grad_key, grad_value], axis=1).astype(jnp.bfloat16)
    prev_grad = from_behind(grad_stack[None], "pipe", -1)
    filter_grad = (lag * filter_scale)[None]
    return (next_input, prev_grad, filter_grad)


def on_device(qkv_in, qkv_saved, conv_saved, out_grad, filters):
    blocks = lax.axis_size("ctx")
    place = lax.axis_index("ctx")
    block = qkv_in.shape[1]
    channels = qkv_in.shape[3]
    groups = filters.shape[1]
    length = blocks * block
    outer = 2 * blocks
    size = outer * block
    filter_scale = (CPF * length) ** (-0.5)

    query_in = qkv_in[0, :, 0].astype(jnp.float32)
    mixed_in = qkv_in[0, :, 1].astype(jnp.float32) * qkv_in[0, :, 2].astype(jnp.float32)
    query_back = qkv_saved[0, :, 0].astype(jnp.float32)
    key_back = qkv_saved[0, :, 1].astype(jnp.float32)
    value_back = qkv_saved[0, :, 2].astype(jnp.float32)
    mixed_back = key_back * value_back
    upstream = out_grad[0].astype(jnp.float32)
    weighted = upstream * query_back
    grad_query = upstream * conv_saved[0]
    taps = filters[0]

    if blocks <= DENSE:
        conv, grad_mixed, lag = dense_path(
            place, blocks, mixed_in.T, weighted.T, mixed_back.T, taps
        )
        return finish(
            conv, grad_mixed, lag, filter_scale, query_in, grad_query, key_back, value_back
        )

    cw, sw = outer_tables(blocks, block, outer)
    fwd, inv = inner_tables(block)

    mixed_rows = mixed_in.T
    weighted_rows = weighted.T
    received = []
    for s in range(1, blocks):
        dest = place + s
        first = jnp.where(dest < blocks, mixed_rows, weighted_rows)
        payload = jnp.concatenate([first, taps], axis=0)
        pairs = [(i, (i + s) % blocks) for i in range(blocks)]
        received.append(lax.ppermute(payload, "ctx", pairs))
    hsum = outer_step(taps, cw, sw, place)
    if blocks <= STEPWISE:
        common = 0.0
        for s, got in enumerate(received, start=1):
            part = outer_step(got, cw, sw, (place - s) % blocks)
            common = common + part[:, :channels]
            hsum = hsum + part[:, channels:]
    else:
        got = jnp.stack(received)
        sources = (place - jnp.arange(1, blocks, dtype=jnp.int32)) % blocks
        weights = jnp.concatenate([cw[sources], sw[sources]], axis=-1)
        both = jnp.concatenate([got, got], axis=-1)
        part = jnp.einsum("sfp,scp->fcp", weights, both, precision=highest)
        common = part[:, :channels]
        hsum = hsum + part[:, channels:]
    local3 = jnp.stack([mixed_rows, weighted_rows, mixed_back.T])

    pos = place * block + jnp.arange(block, dtype=jnp.int32)
    freq = (
        jnp.arange(outer, dtype=jnp.int32)[:, None, None]
        + outer * jnp.arange(block, dtype=jnp.int32)[None, None, :]
    )
    prod = (freq * pos[None, :, None]) % size
    theta = prod.astype(jnp.float32) * (2.0 * math.pi / size)
    inverse = jnp.concatenate([jnp.cos(theta), -jnp.sin(theta)], axis=-1) / size
    inverse = inverse.transpose(0, 2, 1).reshape(outer * 2 * block, block)
    tables = (cw, sw, fwd, inv, inverse, place)

    per_group = 2 * block * outer * 4 * 4 * CPF * blocks
    gchunk = groups
    while gchunk > 1 and gchunk * per_group > CHUNK_BYTES and groups % (gchunk // 2) == 0:
        gchunk //= 2
    nchunk = groups // gchunk
    if nchunk == 1:
        conv, grad_mixed, fg = chunk_work(local3, common, hsum, tables)
    else:
        cc = gchunk * CPF
        ls = local3.reshape(3, nchunk, cc, block).transpose(1, 0, 2, 3)
        cs = common.reshape(outer, nchunk, cc, 2 * block).transpose(1, 0, 2, 3)
        hs = hsum.reshape(outer, nchunk, gchunk, 2 * block).transpose(1, 0, 2, 3)
        conv, grad_mixed, fg = lax.map(lambda a: chunk_work(a[0], a[1], a[2], tables), (ls, cs, hs))
        conv = conv.reshape(channels, block)
        grad_mixed = grad_mixed.reshape(channels, block)
        fg = fg.transpose(1, 0, 2, 3).reshape(blocks, groups, block)

    lag_sum = fg[place]
    for s in range(1, blocks):
        dest = (place + s) % blocks
        pairs = [(i, (i + s) % blocks) for i in range(blocks)]
        lag_sum = lag_sum + lax.ppermute(fg[dest], "ctx", pairs)

    return finish(
        conv.T, grad_mixed.T, lag_sum, filter_scale, query_in, grad_query, key_back, value_back
    )


def solution(mesh):
    return jax.shard_map(
        on_device,
        mesh=mesh,
        in_specs=(
            P("pipe", "ctx", None, None),
            P("pipe", "ctx", None, None),
            P("pipe", "ctx", None),
            P("pipe", "ctx", None),
            P("pipe", None, "ctx"),
        ),
        out_specs=(P("pipe", "ctx", None), P("pipe", "ctx", None, None), P("pipe", None, "ctx")),
        check_vma=False,
    )
```
